32 devices in a mesh: shard: 4 (over z), ctx: 4 (over y, x), tp: 2 (over core).
Axes of the slice: x: 2, y: 2, z: 4, core: 2. Of those that a mesh axis runs over, the one named last changes fastest.
Arguments:
- hidden_in: bfloat16 [24, 680, 1024], P('shard', 'ctx'), may hold values from -6 to 6
- cond: bfloat16 [24, 1024], P('shard'), may hold values from -6 to 6
- scale_len: int32 [24, 10], P('shard'), may hold values from 1 to 256, 680 in all within a row
- ada_weight: bfloat16 [1024, 6, 1024], P('shard'), may hold values from -0.1875 to 0.1875
- ada_bias: float32 [6, 1024], replicated, may hold values from -3 to 3
- qkv_weight: bfloat16 [1024, 3, 1024], P('shard', None, 'tp'), may hold values from -0.1875 to 0.1875
- query_bias: float32 [1024], P('tp'), may hold values from -3 to 3
- value_bias: float32 [1024], P('tp'), may hold values from -3 to 3
- head_scale: float32 [16], P('tp'), may hold values from 2 to 3
- proj_weight: bfloat16 [1024, 1024], P('tp', 'shard'), may hold values from -0.5 to 0.5
- proj_bias: float32 [1024], replicated, may hold values from -2 to 2
- up_weight: bfloat16 [1024, 4096], P('shard', 'tp'), may hold values from -0.1875 to 0.1875
- up_bias: float32 [4096], P('tp'), may hold values from -3 to 3
- down_weight: bfloat16 [4096, 1024], P('tp', 'shard'), may hold values from -0.125 to 0.125
- down_bias: float32 [1024], replicated, may hold values from -2 to 2
- out_grad: bfloat16 [24, 680, 1024], P('shard', 'ctx'), may hold values from -6 to 6
Outputs:
- hidden_out: bfloat16 [24, 680, 1024], P('shard', 'ctx')
- grad_hidden: bfloat16 [24, 680, 1024], P('shard', 'ctx')
- grad_cond: float32 [24, 1024], P('shard')
- grad_ada_weight: float32 [1024, 6, 1024], P('shard')
- grad_ada_bias: float32 [6, 1024], replicated
- grad_qkv_weight: float32 [1024, 3, 1024], P('shard', None, 'tp')
- grad_query_bias: float32 [1024], P('tp')
- grad_value_bias: float32 [1024], P('tp')
- grad_head_scale: float32 [16], P('tp')
- grad_proj_weight: float32 [1024, 1024], P('tp', 'shard')
- grad_proj_bias: float32 [1024], replicated
- grad_up_weight: float32 [1024, 4096], P('shard', 'tp')
- grad_up_bias: float32 [4096], P('tp')
- grad_down_weight: float32 [4096, 1024], P('tp', 'shard')
- grad_down_bias: float32 [1024], replicated
- norm_stats: float32 [3], replicated
The draws below stay inside these ranges and needn't reach their ends.
Inputs may be any that keep to these rules, and one draw needn't show every extreme that they name: `scale_len`: each row holds the token counts of one map's 10 scales in order; they sum to 680, and the largest in every row is 256.
All inputs are finite; a program needn't handle non-finite values.
Results may differ from the reference program's by a relative error of at most 0.03.
Values may be sent and summed in bfloat16 or wider, within the bound.
No kernel may reach another device: no remote copies, remote signals or barrier semaphores. Data moves between devices by JAX's collectives and lax.ppermute only.
A program may use at most 256 MiB of HBM per device.

```python
import math
import jax
import jax.numpy as jnp
import numpy as np
from jax import lax

D = 1024
HEADS = 16
HD = 64
FF = 4096
L = 680
SCALES = 10
MOST = 256
MAPS = 24


def block_scale(key, extent, split, least, top_value):
    def one(dim, parts):
        heights = jax.random.uniform(jax.random.fold_in(jax.random.fold_in(key, 6), dim), (parts,), jnp.float32, least / len(split), top_value / len(split))
        return jnp.repeat(jnp.exp(heights), extent[dim] // parts).reshape((-1,) + (1,) * (len(extent) - dim - 1))

    level = one(*split[0])
    for cut in split[1:]:
        level = level * one(*cut)
    return level


def length_profile(count, total, reach, lean):
    portions = [(1 << 20) // math.isqrt(standing ** lean) + 1 for standing in range(2, count + 1)]
    spare, holding = total - reach - (count - 1), [1] * (count - 1)
    while spare > 0:
        free = [i for i in range(count - 1) if holding[i] < reach]
        whole, left = sum([portions[i] for i in free]), spare
        for i in free:
            addition = min(reach - holding[i], max(1, left * portions[i] // whole), spare)
            holding[i] = holding[i] + addition
            spare = spare - addition
    return np.array([reach] + holding)


def ragged(key, count, total, reach, lean):
    if count == 2:
        one = jax.random.randint(key, (), max(1, total - reach), min(reach, total - 1) + 1)
        return jnp.stack([one, total - one])
    sizes = jnp.asarray(length_profile(count, total, reach, lean), jnp.int32)
    twos = (count - 1) // 2
    giver, taker = sizes[1:1 + 2 * twos:2], sizes[2:2 + 2 * twos:2]
    room = jnp.minimum(giver - 1, reach - taker)
    shifted = jax.random.randint(jax.random.fold_in(key, 1), (twos,), 0, 1 << 20) % (room + 1)
    sizes = sizes.at[1:1 + 2 * twos:2].set(giver - shifted).at[2:2 + 2 * twos:2].set(taker + shifted)
    return sizes[jax.random.permutation(jax.random.fold_in(key, 2), count)]


def scatter_about(stream_key, extent, scale, limit, shards=(), held_as=jnp.bfloat16):
    level = block_scale(stream_key, extent, shards, -0.22, 0.18) if shards else 1.0
    array = jax.random.normal(stream_key, extent, jnp.float32) * scale * level
    return jnp.minimum(jnp.maximum(array, -limit), limit).astype(held_as)


def setup_inputs(seed: int = 0) -> dict:
    seeds = jax.random.split(jax.random.key(seed), 17)
    return {
        "hidden_in": scatter_about(seeds[0], (MAPS, L, D), 1.0, 6.0, ((0, 4), (1, 4))),
        "cond": scatter_about(seeds[1], (MAPS, D), 1.0, 6.0, ((0, 4),)),
        "scale_len": jax.vmap(lambda own: ragged(own, SCALES, L, MOST, 2))(jax.random.split(seeds[2], MAPS)).reshape((MAPS, SCALES)).astype(jnp.int32),
        "ada_weight": scatter_about(seeds[3], (D, 6, D), D ** -0.5, 0.1875, ((0, 4),)),
        "ada_bias": scatter_about(seeds[4], (6, D), 0.5, 3.0, (), jnp.float32),
        "qkv_weight": scatter_about(seeds[5], (D, 3, D), D ** -0.5, 0.1875, ((0, 4), (2, 2))),
        "query_bias": scatter_about(seeds[6], (D,), 0.5, 3.0, ((0, 2),), jnp.float32),
        "value_bias": scatter_about(seeds[7], (D,), 0.5, 3.0, ((0, 2),), jnp.float32),
        "head_scale": jnp.clip(2.0 + 1.0 * jax.random.uniform(seeds[8], (HEADS,), jnp.float32) ** block_scale(seeds[8], (HEADS,), ((0, 2),), -0.2, 0.2), 2.0, 3.0),
        "proj_weight": scatter_about(seeds[9], (D, D), (D // 8) ** -0.5, 0.5, ((0, 2), (1, 4))),
        "proj_bias": scatter_about(seeds[10], (D,), 0.3, 2.0, (), jnp.float32),
        "up_weight": scatter_about(seeds[11], (D, FF), D ** -0.5, 0.1875, ((0, 4), (1, 2))),
        "up_bias": scatter_about(seeds[12], (FF,), 0.5, 3.0, ((0, 2),), jnp.float32),
        "down_weight": scatter_about(seeds[13], (FF, D), (FF // 2) ** -0.5, 0.125, ((0, 2), (1, 4))),
        "down_bias": scatter_about(seeds[14], (D,), 0.3, 2.0, (), jnp.float32),
        "out_grad": scatter_about(seeds[15], (MAPS, L, D), 1.0, 6.0, ((0, 4), (1, 4))),
    }


@jax.custom_vjp
def low(v):
    return lax.optimization_barrier(v.astype(jnp.bfloat16)).astype(jnp.float32)

@jax.custom_vjp
def low_back(v):
    return v

def low_keep(v):
    return (low(v), None)

def low_pass(kept, grad):
    return (grad,)

def back_keep(v):
    return (v, None)

def back_low(kept, grad):
    return (low(grad),)
low.defvjp(low_keep, low_pass)
low_back.defvjp(back_keep, back_low)
HIGHEST = lax.Precision.HIGHEST

def layer_norm(values):
    center = values - lax.optimization_barrier(jnp.mean(values, axis=-1, keepdims=True))
    spread = lax.optimization_barrier(jnp.mean(center * center, axis=-1, keepdims=True))
    return center * lax.rsqrt(spread + 1e-06)

def unit_rows(values):
    return values * lax.rsqrt(lax.optimization_barrier(jnp.sum(values * values, axis=-1, keepdims=True)) + 1e-06)

def map_layer(weights, item):
    ada_weight, ada_bias, qkv_weight, query_bias, value_bias, head_scale, proj_weight, proj_bias, up_weight, up_bias, down_weight, down_bias = weights
    stream_in, cond_vec, lengths = item
    cond_in = low(jax.nn.silu(cond_vec))
    modulation = low_back(jnp.dot(cond_in, ada_weight.reshape(D, 6 * D), precision=HIGHEST).reshape(6, D) + ada_bias)
    gamma_one = modulation[0]
    gamma_two = modulation[1]
    scale_one = modulation[2]
    scale_two = modulation[3]
    shift_one = modulation[4]
    shift_two = modulation[5]
    attn_in = low(layer_norm(stream_in) * (1.0 + scale_one) + shift_one)
    qkv = low_back(jnp.dot(attn_in, qkv_weight.reshape(D, 3 * D), precision=HIGHEST)).reshape(L, 3, D)
    query = (qkv[:, 0] + query_bias).reshape(L, HEADS, HD)
    key_raw = qkv[:, 1].reshape(L, HEADS, HD)
    value = low(qkv[:, 2] + value_bias).reshape(L, HEADS, HD)
    query_unit = low(unit_rows(query) * jnp.exp(head_scale)[None, :, None])
    key_unit = low(unit_rows(key_raw))
    scale_ends = jnp.cumsum(lengths).astype(jnp.int32)
    position = jnp.arange(L, dtype=jnp.int32)
    visible_end = lax.optimization_barrier(jnp.min(jnp.where(scale_ends[None, :] > position[:, None], scale_ends[None, :], L), axis=1))
    key_mask = position[None, :] < visible_end[:, None]
    scores = low_back(jnp.einsum('qhd,khd->hqk', query_unit, key_unit, precision=HIGHEST))
    scores = jnp.where(key_mask[None], scores, -1e+30)
    row_max = lax.optimization_barrier(jnp.max(scores, axis=-1, keepdims=True))
    exp_scores = jnp.exp(scores - row_max)
    probs = exp_scores / lax.optimization_barrier(jnp.sum(exp_scores, axis=-1, keepdims=True))
    probs_low = low(probs)
    heads_out = jnp.einsum('hqk,khd->qhd', probs_low, value, precision=HIGHEST).reshape(L, D)
    heads_out = low(low_back(heads_out))
    attn_branch = low_back(jnp.dot(heads_out, proj_weight, precision=HIGHEST)) + proj_bias
    attn_part = gamma_one * attn_branch
    mid_stream = stream_in + attn_part
    mlp_in = low(layer_norm(mid_stream) * (1.0 + scale_two) + shift_two)
    pre_act = low_back(jnp.dot(mlp_in, up_weight, precision=HIGHEST)) + up_bias
    activation = low(jax.nn.gelu(pre_act, approximate=True))
    mlp_branch = low_back(jnp.dot(activation, down_weight, precision=HIGHEST)) + down_bias
    mlp_part = gamma_two * mlp_branch
    stream = mid_stream + mlp_part
    squares = jnp.stack([jnp.sum(stream * stream), jnp.sum(attn_part * attn_part), jnp.sum(mlp_part * mlp_part)])
    return (stream, squares)

def reference(hidden_in, cond, scale_len, ada_weight, ada_bias, qkv_weight, query_bias, value_bias, head_scale, proj_weight, proj_bias, up_weight, up_bias, down_weight, down_bias, out_grad):
    weights = tuple((item.astype(jnp.float32) for item in (ada_weight, ada_bias, qkv_weight, query_bias, value_bias, head_scale, proj_weight, proj_bias, up_weight, up_bias, down_weight, down_bias)))
    stream_in = hidden_in.astype(jnp.float32)
    cond_vec = cond.astype(jnp.float32)

    def layer_forward(stream_in, cond_vec, weights):

        def one_item(item):
            return map_layer(weights, item)
        return lax.map(jax.checkpoint(one_item), (stream_in, cond_vec, scale_len))
    (streams, squares), pullback = jax.vjp(layer_forward, stream_in, cond_vec, weights)
    grad_stream, grad_cond, grad_weights = pullback((out_grad.astype(jnp.float32), jnp.zeros_like(squares)))
    norm_stats = jnp.sqrt(lax.optimization_barrier(jnp.sum(squares, axis=0)) / (MAPS * L * D))
    return (streams.astype(jnp.bfloat16), grad_stream.astype(jnp.bfloat16), grad_cond, grad_weights[0], grad_weights[1], grad_weights[2], grad_weights[3], grad_weights[4], grad_weights[5], grad_weights[6], grad_weights[7], grad_weights[8], grad_weights[9], grad_weights[10], grad_weights[11], norm_stats)
```

```python
import jax
import jax.numpy as jnp
from jax import lax
from jax.sharding import PartitionSpec as P


def layer_norm(values):
    center = values - jnp.mean(values, axis=-1, keepdims=True)
    spread = jnp.mean(center * center, axis=-1, keepdims=True)
    return center * lax.rsqrt(spread + 1e-06)


def modulate(values, scale, shift):
    return layer_norm(values) * (1.0 + scale[:, None, :]) + shift[:, None, :]


def unit_scaled(values, gains):
    normed = values * lax.rsqrt(jnp.sum(values * values, axis=-1, keepdims=True) + 1e-06)
    return normed * jnp.exp(gains)[None, None, :, None]


def unit_plain(values):
    return values * lax.rsqrt(jnp.sum(values * values, axis=-1, keepdims=True) + 1e-06)


def gelu_tanh(values):
    return jax.nn.gelu(values, approximate=True)


def tp_sum(values):
    count = lax.axis_size("tp")
    if count != 2:
        return lax.psum(values, "tp")
    return values + lax.ppermute(values, "tp", [(0, 1), (1, 0)])


def ctx_shifts(values):
    count = lax.axis_size("ctx")
    parts = [values]
    for shift in range(1, count):
        pairs = [(i, (i + shift) % count) for i in range(count)]
        parts.append(lax.ppermute(values, "ctx", pairs))
    return jnp.stack(parts)


def ctx_return(parts):
    count = lax.axis_size("ctx")
    total = parts[0].astype(jnp.float32)
    for shift in range(1, count):
        pairs = [(i, (i - shift) % count) for i in range(count)]
        total = total + lax.ppermute(parts[shift], "ctx", pairs).astype(jnp.float32)
    return total


def body(
    hidden_in,
    cond,
    scale_len,
    ada_weight,
    ada_bias,
    qkv_weight,
    query_bias,
    value_bias,
    head_scale,
    proj_weight,
    proj_bias,
    up_weight,
    up_bias,
    down_weight,
    down_bias,
    out_grad,
):
    map_count = hidden_in.shape[0]
    piece_rows = hidden_in.shape[1]
    model_width = hidden_in.shape[2]
    ctx_count = lax.axis_size("ctx")
    ctx_index = lax.axis_index("ctx")
    shard_index = lax.axis_index("shard")
    map_length = piece_rows * ctx_count
    heads_here = head_scale.shape[0]
    local_width = query_bias.shape[0]
    head_dim = local_width // heads_here
    row_count = map_count * piece_rows
    head_shape = (map_count, piece_rows, heads_here, head_dim)
    ada_rows = ada_weight.shape[0]
    full_qkv, full_up, full_proj, full_down = (
        lax.all_gather(qkv_weight, "shard", axis=0, tiled=True),
        lax.all_gather(up_weight, "shard", axis=0, tiled=True),
        lax.all_gather(proj_weight, "shard", axis=1, tiled=True),
        lax.all_gather(down_weight, "shard", axis=1, tiled=True),
    )
    qkv_matrix = full_qkv.reshape(model_width, 3 * local_width)

    cond_wide = cond.astype(jnp.float32)
    cond_all = lax.all_gather(cond, "shard", axis=0, tiled=True).astype(jnp.float32)
    cond_in_all = jax.nn.silu(cond_all).astype(jnp.bfloat16)
    cond_cols = lax.dynamic_slice_in_dim(cond_in_all, shard_index * ada_rows, ada_rows, axis=1)
    ada_local = ada_weight.reshape(ada_rows, 6 * model_width)
    mod_partial = jnp.dot(cond_cols, ada_local, preferred_element_type=jnp.float32)
    modulation = lax.psum_scatter(mod_partial, "shard", scatter_dimension=0, tiled=True)
    modulation = modulation.reshape(map_count, 6, model_width) + ada_bias[None]
    gamma_one = modulation[:, 0]
    gamma_two = modulation[:, 1]
    scale_one = modulation[:, 2]
    scale_two = modulation[:, 3]
    shift_one = modulation[:, 4]
    shift_two = modulation[:, 5]
    stream_in = hidden_in.astype(jnp.float32)
    first_mod, first_back = jax.vjp(modulate, stream_in, scale_one, shift_one)
    attn_in = first_mod.astype(jnp.bfloat16).reshape(row_count, model_width)
    qkv = jnp.dot(attn_in, qkv_matrix, preferred_element_type=jnp.float32).reshape(
        map_count, piece_rows, 3, local_width
    )
    query = (qkv[:, :, 0] + query_bias).reshape(head_shape)
    key_raw = qkv[:, :, 1].reshape(head_shape)
    value_low = (qkv[:, :, 2] + value_bias).astype(jnp.bfloat16).reshape(head_shape)
    query_unit, query_back = jax.vjp(unit_scaled, query, head_scale)
    key_unit, key_back = jax.vjp(unit_plain, key_raw)
    query_low = query_unit.astype(jnp.bfloat16)
    key_low = key_unit.astype(jnp.bfloat16)
    keys_parts = ctx_shifts(key_low)
    values_parts = ctx_shifts(value_low)
    scale_ends = jnp.cumsum(scale_len, axis=1)
    query_pos = ctx_index * piece_rows + jnp.arange(piece_rows, dtype=jnp.int32)
    visible_end = jnp.min(
        jnp.where(scale_ends[:, None, :] > query_pos[None, :, None], scale_ends[:, None, :], map_length),
        axis=2,
    )
    owners = (ctx_index - jnp.arange(ctx_count, dtype=jnp.int32)) % ctx_count
    key_pos = owners[:, None] * piece_rows + jnp.arange(piece_rows, dtype=jnp.int32)[None, :]
    key_mask = key_pos[None, None, :, :] < visible_end[:, :, None, None]

    def masked_scores():
        raw_scores = jnp.einsum(
            "mqhd,nmkhd->mhqnk", query_low, keys_parts, preferred_element_type=jnp.float32
        )
        return jnp.where(key_mask[:, None], raw_scores, -1e30)

    scores = masked_scores()
    row_max = jnp.max(scores, axis=(-2, -1), keepdims=True)
    exp_scores = jnp.exp(scores - row_max)
    exp_total = jnp.sum(exp_scores, axis=(-2, -1), keepdims=True)
    log_total = row_max + jnp.log(exp_total)
    probs_low = (exp_scores / exp_total).astype(jnp.bfloat16)
    heads_out = jnp.einsum(
        "mhqnk,nmkhd->mqhd", probs_low, values_parts, preferred_element_type=jnp.float32
    )
    heads_out = heads_out.reshape(row_count, local_width).astype(jnp.bfloat16)
    attn_partial = jnp.dot(heads_out, full_proj, preferred_element_type=jnp.float32)
    attn_branch = tp_sum(attn_partial).reshape(map_count, piece_rows, model_width) + proj_bias
    attn_part = gamma_one[:, None] * attn_branch
    mid_stream = stream_in + attn_part
    second_mod, second_back = jax.vjp(modulate, mid_stream, scale_two, shift_two)
    mlp_in = second_mod.astype(jnp.bfloat16).reshape(row_count, model_width)
    pre_act = jnp.dot(mlp_in, full_up, preferred_element_type=jnp.float32) + up_bias
    activation, gelu_back = jax.vjp(gelu_tanh, pre_act)
    act_low = activation.astype(jnp.bfloat16)
    mlp_partial = jnp.dot(act_low, full_down, preferred_element_type=jnp.float32)
    mlp_branch = tp_sum(mlp_partial).reshape(map_count, piece_rows, model_width) + down_bias
    mlp_part = gamma_two[:, None] * mlp_branch
    stream = mid_stream + mlp_part
    grad_top = out_grad.astype(jnp.float32)
    d_gamma_two = jnp.sum(grad_top * mlp_branch, axis=1)
    d_mlp = gamma_two[:, None] * grad_top
    d_down_bias = jnp.sum(d_mlp, axis=(0, 1))
    d_mlp_low = d_mlp.astype(jnp.bfloat16).reshape(row_count, model_width)
    g_down = jnp.einsum("rf,rd->fd", act_low, d_mlp_low, preferred_element_type=jnp.float32)
    d_act = jnp.einsum("rd,fd->rf", d_mlp_low, full_down, preferred_element_type=jnp.float32)
    (d_pre,) = gelu_back(d_act)
    d_up_bias = jnp.sum(d_pre, axis=0)
    d_pre_low = d_pre.astype(jnp.bfloat16)
    g_up = jnp.einsum("rd,rf->df", mlp_in, d_pre_low, preferred_element_type=jnp.float32)
    d_mlp_in_part = jnp.einsum("rf,df->rd", d_pre_low, full_up, preferred_element_type=jnp.float32)
    d_mlp_in = tp_sum(d_mlp_in_part).reshape(map_count, piece_rows, model_width)
    d_mid, d_scale_two, d_shift_two = second_back(d_mlp_in)
    d_mid = d_mid + grad_top
    d_gamma_one = jnp.sum(d_mid * attn_branch, axis=1)
    d_attn = gamma_one[:, None] * d_mid
    d_proj_bias = jnp.sum(d_attn, axis=(0, 1))
    d_attn_low = d_attn.astype(jnp.bfloat16).reshape(row_count, model_width)
    g_proj = jnp.einsum("ri,rd->id", heads_out, d_attn_low, preferred_element_type=jnp.float32)
    d_heads = jnp.einsum("rd,id->ri", d_attn_low, full_proj, preferred_element_type=jnp.float32)
    d_heads = d_heads.astype(jnp.bfloat16).reshape(head_shape)
    probs = jnp.exp(masked_scores() - log_total)
    d_probs = jnp.einsum(
        "mqhd,nmkhd->mhqnk", d_heads, values_parts, preferred_element_type=jnp.float32
    )
    row_delta = jnp.sum(probs * d_probs, axis=(-2, -1), keepdims=True)
    d_scores = (probs * (d_probs - row_delta)).astype(jnp.bfloat16)
    d_query_unit = jnp.einsum(
        "mhqnk,nmkhd->mqhd", d_scores, keys_parts, preferred_element_type=jnp.float32
    )
    probs_again = probs.astype(jnp.bfloat16)
    d_key_parts = jnp.einsum(
        "mhqnk,mqhd->nmkhd", d_scores, query_low, preferred_element_type=jnp.float32
    ).astype(jnp.bfloat16)
    d_value_parts = jnp.einsum(
        "mhqnk,mqhd->nmkhd", probs_again, d_heads, preferred_element_type=jnp.float32
    ).astype(jnp.bfloat16)
    d_key_unit = ctx_return(d_key_parts)
    d_value = ctx_return(d_value_parts)
    d_query, d_head_scale = query_back(d_query_unit)
    (d_key,) = key_back(d_key_unit)
    d_query = d_query.reshape(map_count, piece_rows, local_width)
    d_key = d_key.reshape(map_count, piece_rows, local_width)
    d_value = d_value.reshape(map_count, piece_rows, local_width)
    d_query_bias = jnp.sum(d_query, axis=(0, 1))
    d_value_bias = jnp.sum(d_value, axis=(0, 1))
    d_qkv = (
        jnp.stack([d_query, d_key, d_value], axis=2)
        .astype(jnp.bfloat16)
        .reshape(row_count, 3 * local_width)
    )
    g_qkv = jnp.einsum("rd,rc->dc", attn_in, d_qkv, preferred_element_type=jnp.float32).reshape(
        model_width, 3, local_width
    )
    d_attn_in_part = jnp.einsum("rc,dc->rd", d_qkv, qkv_matrix, preferred_element_type=jnp.float32)
    d_attn_in = tp_sum(d_attn_in_part).reshape(map_count, piece_rows, model_width)
    d_input, d_scale_one, d_shift_one = first_back(d_attn_in)
    d_input = d_input + d_mid
    d_mod_part = jnp.stack(
        [d_gamma_one, d_gamma_two, d_scale_one, d_scale_two, d_shift_one, d_shift_two], axis=1
    )
    d_mod = lax.psum(d_mod_part, "ctx").astype(jnp.bfloat16).reshape(map_count, 6 * model_width)
    d_mod_all = lax.all_gather(d_mod, "shard", axis=0, tiled=True)
    g_ada = jnp.einsum(
        "md,mc->dc", cond_cols, d_mod_all, preferred_element_type=jnp.float32
    ).reshape(ada_rows, 6, model_width)
    d_ada_bias = jnp.sum(d_mod_all.astype(jnp.float32), axis=0).reshape(6, model_width)
    d_cond_cols = jnp.einsum("mc,dc->md", d_mod_all, ada_local, preferred_element_type=jnp.float32)
    d_cond_in = lax.all_to_all(d_cond_cols, "shard", 0, 1, tiled=True)
    silu_value, silu_back = jax.vjp(jax.nn.silu, cond_wide)
    (d_cond,) = silu_back(d_cond_in)
    shard_grads = (
        lax.psum_scatter(
            g_qkv.astype(jnp.bfloat16), "shard", scatter_dimension=0, tiled=True
        ),
        lax.psum_scatter(
            g_up.astype(jnp.bfloat16), "shard", scatter_dimension=0, tiled=True
        ),
        lax.psum_scatter(
            g_proj.astype(jnp.bfloat16), "shard", scatter_dimension=1, tiled=True
        ),
        lax.psum_scatter(
            g_down.astype(jnp.bfloat16), "shard", scatter_dimension=1, tiled=True
        ),
    )
    summed = tuple(lax.psum(g, "ctx").astype(jnp.float32) for g in shard_grads)
    square_sums = jnp.stack(
        [jnp.sum(stream * stream), jnp.sum(attn_part * attn_part), jnp.sum(mlp_part * mlp_part)]
    )
    small_parts = (
        square_sums,
        d_query_bias,
        d_value_bias,
        d_head_scale,
        d_proj_bias,
        d_up_bias,
        d_down_bias,
    )
    small_flat = lax.psum(jnp.concatenate(small_parts), ("shard", "ctx"))
    small = []
    offset = 0
    for part in small_parts:
        small.append(small_flat[offset:offset + part.shape[0]])
        offset += part.shape[0]
    entry_total = map_count * map_length * model_width * lax.axis_size("shard")
    norm_stats = jnp.sqrt(small[0] / entry_total)
    return (
        stream.astype(jnp.bfloat16),
        d_input.astype(jnp.bfloat16),
        d_cond,
        g_ada,
        d_ada_bias,
        summed[0],
        small[1],
        small[2],
        small[3],
        summed[2],
        small[4],
        summed[1],
        small[5],
        summed[3],
        small[6],
        norm_stats,
    )


def solution(mesh):
    in_specs = (
        P("shard", "ctx", None),
        P("shard", None),
        P("shard", None),
        P("shard", None, None),
        P(),
        P("shard", None, "tp"),
        P("tp"),
        P("tp"),
        P("tp"),
        P("tp", "shard"),
        P(),
        P("shard", "tp"),
        P("tp"),
        P("tp", "shard"),
        P(),
        P("shard", "ctx", None),
    )
    out_specs = (
        P("shard", "ctx", None),
        P("shard", "ctx", None),
        P("shard", None),
        P("shard", None, None),
        P(),
        P("shard", None, "tp"),
        P("tp"),
        P("tp"),
        P("tp"),
        P("tp", "shard"),
        P(),
        P("shard", "tp"),
        P("tp"),
        P("tp", "shard"),
        P(),
        P(),
    )
    return jax.shard_map(body, mesh=mesh, in_specs=in_specs, out_specs=out_specs, check_vma=False)
```

```python
import jax
import jax.numpy as jnp
from jax import lax
from jax.sharding import PartitionSpec as P


def layer_norm(values):
    center = values - jnp.mean(values, axis=-1, keepdims=True)
    spread = jnp.mean(center * center, axis=-1, keepdims=True)
    return center * lax.rsqrt(spread + 1e-06)


def modulate(values, scale, shift):
    return layer_norm(values) * (1.0 + scale[:, None, :]) + shift[:, None, :]


def unit_scaled(values, gains):
    normed = values * lax.rsqrt(jnp.sum(values * values, axis=-1, keepdims=True) + 1e-06)
    return normed * jnp.exp(gains)[None, None, :, None]


def unit_plain(values):
    return values * lax.rsqrt(jnp.sum(values * values, axis=-1, keepdims=True) + 1e-06)


def gelu_tanh(values):
    return jax.nn.gelu(values, approximate=True)


def tp_sum(values):
    count = lax.axis_size("tp")
    if count != 2:
        return lax.psum(values, "tp")
    return values + lax.ppermute(values, "tp", [(0, 1), (1, 0)])


def ctx_shifts(values):
    count = lax.axis_size("ctx")
    parts = [values]
    for shift in range(1, count):
        pairs = [(i, (i + shift) % count) for i in range(count)]
        parts.append(lax.ppermute(values, "ctx", pairs))
    return jnp.stack(parts)


def ctx_return(parts):
    count = lax.axis_size("ctx")
    total = parts[0].astype(jnp.float32)
    for shift in range(1, count):
        pairs = [(i, (i - shift) % count) for i in range(count)]
        total = total + lax.ppermute(parts[shift], "ctx", pairs).astype(jnp.float32)
    return total


def gather_axis(values, axis):
    count = lax.axis_size(axis)
    me = lax.axis_index(axis)
    parts = [values]
    for shift in range(1, count):
        pairs = [(i, (i + shift) % count) for i in range(count)]
        parts.append(lax.ppermute(values, axis, pairs))
    stacked = jnp.stack(parts)
    order = (me - jnp.arange(count, dtype=jnp.int32)) % count
    return jnp.take(stacked, order, axis=0)


def small_sum(values):
    every = gather_axis(gather_axis(values, "ctx"), "shard")
    return jnp.sum(every, axis=(0, 1))


def body(
    hidden_in,
    cond,
    scale_len,
    ada_weight,
    ada_bias,
    qkv_weight,
    query_bias,
    value_bias,
    head_scale,
    proj_weight,
    proj_bias,
    up_weight,
    up_bias,
    down_weight,
    down_bias,
    out_grad,
):
    map_count = hidden_in.shape[0]
    piece_rows = hidden_in.shape[1]
    model_width = hidden_in.shape[2]
    ctx_count = lax.axis_size("ctx")
    ctx_index = lax.axis_index("ctx")
    shard_index = lax.axis_index("shard")
    map_length = piece_rows * ctx_count
    heads_here = head_scale.shape[0]
    local_width = query_bias.shape[0]
    head_dim = local_width // heads_here
    row_count = map_count * piece_rows
    head_shape = (map_count, piece_rows, heads_here, head_dim)
    ada_rows = ada_weight.shape[0]
    shard_count = lax.axis_size("shard")
    full_qkv = lax.all_gather(qkv_weight, "shard", axis=0, tiled=True)
    packed = jnp.concatenate([proj_weight.reshape(-1), up_weight.reshape(-1), down_weight.reshape(-1)])
    packed_all = lax.all_gather(packed, "shard", axis=0, tiled=False)
    proj_size, up_size = proj_weight.size, up_weight.size
    proj_parts = packed_all[:, :proj_size].reshape((shard_count,) + proj_weight.shape)
    up_parts = packed_all[:, proj_size:proj_size + up_size].reshape((shard_count,) + up_weight.shape)
    down_parts = packed_all[:, proj_size + up_size:].reshape((shard_count,) + down_weight.shape)
    full_proj = jnp.transpose(proj_parts, (1, 0, 2)).reshape(proj_weight.shape[0], -1)
    full_up = up_parts.reshape(-1, up_weight.shape[1])
    full_down = jnp.transpose(down_parts, (1, 0, 2)).reshape(down_weight.shape[0], -1)
    qkv_matrix = full_qkv.reshape(model_width, 3 * local_width)

    cond_wide = cond.astype(jnp.float32)
    cond_all = lax.all_gather(cond, "shard", axis=0, tiled=True).astype(jnp.float32)
    cond_in_all = jax.nn.silu(cond_all).astype(jnp.bfloat16)
    cond_cols = lax.dynamic_slice_in_dim(cond_in_all, shard_index * ada_rows, ada_rows, axis=1)
    ada_local = ada_weight.reshape(ada_rows, 6 * model_width)
    mod_partial = jnp.dot(cond_cols, ada_local, preferred_element_type=jnp.float32)
    modulation = lax.psum_scatter(mod_partial, "shard", scatter_dimension=0, tiled=True)
    modulation = modulation.reshape(map_count, 6, model_width) + ada_bias[None]
    gamma_one = modulation[:, 0]
    gamma_two = modulation[:, 1]
    scale_one = modulation[:, 2]
    scale_two = modulation[:, 3]
    shift_one = modulation[:, 4]
    shift_two = modulation[:, 5]
    stream_in = hidden_in.astype(jnp.float32)
    first_mod, first_back = jax.vjp(modulate, stream_in, scale_one, shift_one)
    attn_in = first_mod.astype(jnp.bfloat16).reshape(row_count, model_width)
    qkv = jnp.dot(attn_in, qkv_matrix, preferred_element_type=jnp.float32).reshape(
        map_count, piece_rows, 3, local_width
    )
    query = (qkv[:, :, 0] + query_bias).reshape(head_shape)
    key_raw = qkv[:, :, 1].reshape(head_shape)
    value_low = (qkv[:, :, 2] + value_bias).astype(jnp.bfloat16).reshape(head_shape)
    query_unit, query_back = jax.vjp(unit_scaled, query, head_scale)
    key_unit, key_back = jax.vjp(unit_plain, key_raw)
    query_low = query_unit.astype(jnp.bfloat16)
    key_low = key_unit.astype(jnp.bfloat16)
    keys_parts = ctx_shifts(key_low)
    values_parts = ctx_shifts(value_low)
    scale_ends = jnp.cumsum(scale_len, axis=1)
    query_pos = ctx_index * piece_rows + jnp.arange(piece_rows, dtype=jnp.int32)
    visible_end = jnp.min(
        jnp.where(scale_ends[:, None, :] > query_pos[None, :, None], scale_ends[:, None, :], map_length),
        axis=2,
    )
    owners = (ctx_index - jnp.arange(ctx_count, dtype=jnp.int32)) % ctx_count
    key_pos = owners[:, None] * piece_rows + jnp.arange(piece_rows, dtype=jnp.int32)[None, :]
    key_mask = key_pos[None, None, :, :] < visible_end[:, :, None, None]

    def masked_scores():
        raw_scores = jnp.einsum(
            "mqhd,nmkhd->mhqnk", query_low, keys_parts, preferred_element_type=jnp.float32
        )
        return jnp.where(key_mask[:, None], raw_scores, -1e30)

    scores = masked_scores()
    row_max = jnp.max(scores, axis=(-2, -1), keepdims=True)
    exp_scores = jnp.exp(scores - row_max)
    exp_total = jnp.sum(exp_scores, axis=(-2, -1), keepdims=True)
    log_total = row_max + jnp.log(exp_total)
    probs_low = (exp_scores / exp_total).astype(jnp.bfloat16)
    heads_out = jnp.einsum(
        "mhqnk,nmkhd->mqhd", probs_low, values_parts, preferred_element_type=jnp.float32
    )
    heads_out = heads_out.reshape(row_count, local_width).astype(jnp.bfloat16)
    attn_partial = jnp.dot(heads_out, full_proj, preferred_element_type=jnp.float32)
    attn_branch = tp_sum(attn_partial).reshape(map_count, piece_rows, model_width) + proj_bias
    attn_part = gamma_one[:, None] * attn_branch
    mid_stream = stream_in + attn_part
    second_mod, second_back = jax.vjp(modulate, mid_stream, scale_two, shift_two)
    mlp_in = second_mod.astype(jnp.bfloat16).reshape(row_count, model_width)
    pre_act = jnp.dot(mlp_in, full_up, preferred_element_type=jnp.float32) + up_bias
    activation, gelu_back = jax.vjp(gelu_tanh, pre_act)
    act_low = activation.astype(jnp.bfloat16)
    mlp_partial = jnp.dot(act_low, full_down, preferred_element_type=jnp.float32)
    mlp_branch = tp_sum(mlp_partial).reshape(map_count, piece_rows, model_width) + down_bias
    mlp_part = gamma_two[:, None] * mlp_branch
    stream = mid_stream + mlp_part
    grad_top = out_grad.astype(jnp.float32)
    d_gamma_two = jnp.sum(grad_top * mlp_branch, axis=1)
    d_mlp = gamma_two[:, None] * grad_top
    d_down_bias = jnp.sum(d_mlp, axis=(0, 1))
    d_mlp_low = d_mlp.astype(jnp.bfloat16).reshape(row_count, model_width)
    g_down = jnp.einsum("rf,rd->fd", act_low, d_mlp_low, preferred_element_type=jnp.float32)
    d_act = jnp.einsum("rd,fd->rf", d_mlp_low, full_down, preferred_element_type=jnp.float32)
    (d_pre,) = gelu_back(d_act)
    d_up_bias = jnp.sum(d_pre, axis=0)
    d_pre_low = d_pre.astype(jnp.bfloat16)
    g_up = jnp.einsum("rd,rf->df", mlp_in, d_pre_low, preferred_element_type=jnp.float32)
    d_mlp_in_part = jnp.einsum("rf,df->rd", d_pre_low, full_up, preferred_element_type=jnp.float32)
    d_mlp_in = tp_sum(d_mlp_in_part).reshape(map_count, piece_rows, model_width)
    d_mid, d_scale_two, d_shift_two = second_back(d_mlp_in)
    d_mid = d_mid + grad_top
    d_gamma_one = jnp.sum(d_mid * attn_branch, axis=1)
    d_attn = gamma_one[:, None] * d_mid
    d_proj_bias = jnp.sum(d_attn, axis=(0, 1))
    d_attn_low = d_attn.astype(jnp.bfloat16).reshape(row_count, model_width)
    g_proj = jnp.einsum("ri,rd->id", heads_out, d_attn_low, preferred_element_type=jnp.float32)
    d_heads = jnp.einsum("rd,id->ri", d_attn_low, full_proj, preferred_element_type=jnp.float32)
    d_heads = d_heads.astype(jnp.bfloat16).reshape(head_shape)
    probs = jnp.exp(masked_scores() - log_total)
    d_probs = jnp.einsum(
        "mqhd,nmkhd->mhqnk", d_heads, values_parts, preferred_element_type=jnp.float32
    )
    row_delta = jnp.sum(probs * d_probs, axis=(-2, -1), keepdims=True)
    d_scores = (probs * (d_probs - row_delta)).astype(jnp.bfloat16)
    d_query_unit = jnp.einsum(
        "mhqnk,nmkhd->mqhd", d_scores, keys_parts, preferred_element_type=jnp.float32
    )
    probs_again = probs.astype(jnp.bfloat16)
    d_key_parts = jnp.einsum(
        "mhqnk,mqhd->nmkhd", d_scores, query_low, preferred_element_type=jnp.float32
    ).astype(jnp.bfloat16)
    d_value_parts = jnp.einsum(
        "mhqnk,mqhd->nmkhd", probs_again, d_heads, preferred_element_type=jnp.float32
    ).astype(jnp.bfloat16)
    d_key_unit = ctx_return(d_key_parts)
    d_value = ctx_return(d_value_parts)
    d_query, d_head_scale = query_back(d_query_unit)
    (d_key,) = key_back(d_key_unit)
    d_query = d_query.reshape(map_count, piece_rows, local_width)
    d_key = d_key.reshape(map_count, piece_rows, local_width)
    d_value = d_value.reshape(map_count, piece_rows, local_width)
    d_query_bias = jnp.sum(d_query, axis=(0, 1))
    d_value_bias = jnp.sum(d_value, axis=(0, 1))
    d_qkv = (
        jnp.stack([d_query, d_key, d_value], axis=2)
        .astype(jnp.bfloat16)
        .reshape(row_count, 3 * local_width)
    )
    g_qkv = jnp.einsum("rd,rc->dc", attn_in, d_qkv, preferred_element_type=jnp.float32).reshape(
        model_width, 3, local_width
    )
    d_attn_in_part = jnp.einsum("rc,dc->rd", d_qkv, qkv_matrix, preferred_element_type=jnp.float32)
    d_attn_in = tp_sum(d_attn_in_part).reshape(map_count, piece_rows, model_width)
    d_input, d_scale_one, d_shift_one = first_back(d_attn_in)
    d_input = d_input + d_mid
    d_mod_part = jnp.stack(
        [d_gamma_one, d_gamma_two, d_scale_one, d_scale_two, d_shift_one, d_shift_two], axis=1
    )
    d_mod = lax.psum(d_mod_part, "ctx").astype(jnp.bfloat16).reshape(map_count, 6 * model_width)
    d_mod_all = lax.all_gather(d_mod, "shard", axis=0, tiled=True)
    g_ada = jnp.einsum(
        "md,mc->dc", cond_cols, d_mod_all, preferred_element_type=jnp.float32
    ).reshape(ada_rows, 6, model_width)
    d_ada_bias = jnp.sum(d_mod_all.astype(jnp.float32), axis=0).reshape(6, model_width)
    d_cond_cols = jnp.einsum("mc,dc->md", d_mod_all, ada_local, preferred_element_type=jnp.float32)
    d_cond_in = lax.all_to_all(d_cond_cols, "shard", 0, 1, tiled=True)
    silu_value, silu_back = jax.vjp(jax.nn.silu, cond_wide)
    (d_cond,) = silu_back(d_cond_in)
    shard_grads = (
        lax.psum_scatter(
            g_qkv.astype(jnp.bfloat16), "shard", scatter_dimension=0, tiled=True
        ),
        lax.psum_scatter(
            g_up.astype(jnp.bfloat16), "shard", scatter_dimension=0, tiled=True
        ),
        lax.psum_scatter(
            g_proj.astype(jnp.bfloat16), "shard", scatter_dimension=1, tiled=True
        ),
        lax.psum_scatter(
            g_down.astype(jnp.bfloat16), "shard", scatter_dimension=1, tiled=True
        ),
    )
    summed = tuple(lax.psum(g, "ctx").astype(jnp.float32) for g in shard_grads)
    square_sums = jnp.stack(
        [jnp.sum(stream * stream), jnp.sum(attn_part * attn_part), jnp.sum(mlp_part * mlp_part)]
    )
    small_parts = (
        square_sums,
        d_query_bias,
        d_value_bias,
        d_head_scale,
        d_proj_bias,
        d_up_bias,
        d_down_bias,
    )
    small_flat = small_sum(jnp.concatenate(small_parts))
    small = []
    offset = 0
    for part in small_parts:
        small.append(small_flat[offset:offset + part.shape[0]])
        offset += part.shape[0]
    entry_total = map_count * map_length * model_width * lax.axis_size("shard")
    norm_stats = jnp.sqrt(small[0] / entry_total)
    return (
        stream.astype(jnp.bfloat16),
        d_input.astype(jnp.bfloat16),
        d_cond,
        g_ada,
        d_ada_bias,
        summed[0],
        small[1],
        small[2],
        small[3],
        summed[2],
        small[4],
        summed[1],
        small[5],
        summed[3],
        small[6],
        norm_stats,
    )


def solution(mesh):
    in_specs = (
        P("shard", "ctx", None),
        P("shard", None),
        P("shard", None),
        P("shard", None, None),
        P(),
        P("shard", None, "tp"),
        P("tp"),
        P("tp"),
        P("tp"),
        P("tp", "shard"),
        P(),
        P("shard", "tp"),
        P("tp"),
        P("tp", "shard"),
        P(),
        P("shard", "ctx", None),
    )
    out_specs = (
        P("shard", "ctx", None),
        P("shard", "ctx", None),
        P("shard", None),
        P("shard", None, None),
        P(),
        P("shard", None, "tp"),
        P("tp"),
        P("tp"),
        P("tp"),
        P("tp", "shard"),
        P(),
        P("shard", "tp"),
        P("tp"),
        P("tp", "shard"),
        P(),
        P(),
    )
    return jax.shard_map(body, mesh=mesh, in_specs=in_specs, out_specs=out_specs, check_vma=False)
```

```python
import jax
import jax.numpy as jnp
from jax import lax
from jax.sharding import PartitionSpec as P


def layer_norm(values):
    center = values - jnp.mean(values, axis=-1, keepdims=True)
    spread = jnp.mean(center * center, axis=-1, keepdims=True)
    return center * lax.rsqrt(spread + 1e-06)


def modulate(values, scale, shift):
    return layer_norm(values) * (1.0 + scale[:, None, :]) + shift[:, None, :]


def unit_scaled(values, gains):
    normed = values * lax.rsqrt(jnp.sum(values * values, axis=-1, keepdims=True) + 1e-06)
    return normed * jnp.exp(gains)[None, None, :, None]


def unit_plain(values):
    return values * lax.rsqrt(jnp.sum(values * values, axis=-1, keepdims=True) + 1e-06)


def gelu_tanh(values):
    return jax.nn.gelu(values, approximate=True)


def tp_sum(values):
    count = lax.axis_size("tp")
    if count != 2:
        return lax.psum(values, "tp")
    return values + lax.ppermute(values, "tp", [(0, 1), (1, 0)])


def ctx_shifts(values):
    count = lax.axis_size("ctx")
    parts = [values]
    for shift in range(1, count):
        pairs = [(i, (i + shift) % count) for i in range(count)]
        parts.append(lax.ppermute(values, "ctx", pairs))
    return jnp.stack(parts)


def ctx_return(parts):
    count = lax.axis_size("ctx")
    total = parts[0].astype(jnp.float32)
    for shift in range(1, count):
        pairs = [(i, (i - shift) % count) for i in range(count)]
        total = total + lax.ppermute(parts[shift], "ctx", pairs).astype(jnp.float32)
    return total


def group_send(values):
    count = lax.axis_size("ctx")
    me = lax.axis_index("ctx")
    parts = []
    for shift in range(count):
        block = lax.dynamic_index_in_dim(values, (me + shift) % count, axis=2, keepdims=False)
        if shift:
            pairs = [(i, (i + shift) % count) for i in range(count)]
            block = lax.ppermute(block, "ctx", pairs)
        parts.append(block)
    return jnp.stack(parts)


def group_return(parts):
    count = lax.axis_size("ctx")
    me = lax.axis_index("ctx")
    back = [parts[0]]
    for shift in range(1, count):
        pairs = [(i, (i - shift) % count) for i in range(count)]
        back.append(lax.ppermute(parts[shift], "ctx", pairs))
    stacked = jnp.stack(back)
    order = (jnp.arange(count, dtype=jnp.int32) - me) % count
    return jnp.moveaxis(jnp.take(stacked, order, axis=0), 0, 2)


def gather_axis(values, axis):
    count = lax.axis_size(axis)
    me = lax.axis_index(axis)
    parts = [values]
    for shift in range(1, count):
        pairs = [(i, (i + shift) % count) for i in range(count)]
        parts.append(lax.ppermute(values, axis, pairs))
    stacked = jnp.stack(parts)
    order = (me - jnp.arange(count, dtype=jnp.int32)) % count
    return jnp.take(stacked, order, axis=0)


def small_sum(values):
    every = gather_axis(gather_axis(values, "ctx"), "shard")
    return jnp.sum(every, axis=(0, 1))


def body(
    hidden_in,
    cond,
    scale_len,
    ada_weight,
    ada_bias,
    qkv_weight,
    query_bias,
    value_bias,
    head_scale,
    proj_weight,
    proj_bias,
    up_weight,
    up_bias,
    down_weight,
    down_bias,
    out_grad,
):
    map_count = hidden_in.shape[0]
    piece_rows = hidden_in.shape[1]
    model_width = hidden_in.shape[2]
    ctx_count = lax.axis_size("ctx")
    ctx_index = lax.axis_index("ctx")
    shard_index = lax.axis_index("shard")
    map_length = piece_rows * ctx_count
    heads_here = head_scale.shape[0]
    local_width = query_bias.shape[0]
    head_dim = local_width // heads_here
    row_count = map_count * piece_rows
    head_shape = (map_count, piece_rows, heads_here, head_dim)
    ada_rows = ada_weight.shape[0]
    shard_count = lax.axis_size("shard")
    full_qkv = lax.all_gather(qkv_weight, "shard", axis=0, tiled=True)
    packed = jnp.concatenate([proj_weight.reshape(-1), up_weight.reshape(-1), down_weight.reshape(-1)])
    packed_all = lax.all_gather(packed, "shard", axis=0, tiled=False)
    proj_size, up_size = proj_weight.size, up_weight.size
    proj_parts = packed_all[:, :proj_size].reshape((shard_count,) + proj_weight.shape)
    up_parts = packed_all[:, proj_size:proj_size + up_size].reshape((shard_count,) + up_weight.shape)
    down_parts = packed_all[:, proj_size + up_size:].reshape((shard_count,) + down_weight.shape)
    full_proj = jnp.transpose(proj_parts, (1, 0, 2)).reshape(proj_weight.shape[0], -1)
    full_up = up_parts.reshape(-1, up_weight.shape[1])
    full_down = jnp.transpose(down_parts, (1, 0, 2)).reshape(down_weight.shape[0], -1)
    qkv_matrix = full_qkv.reshape(model_width, 3 * local_width)

    cond_wide = cond.astype(jnp.float32)
    cond_all = lax.all_gather(cond, "shard", axis=0, tiled=True).astype(jnp.float32)
    cond_in_all = jax.nn.silu(cond_all).astype(jnp.bfloat16)
    cond_cols = lax.dynamic_slice_in_dim(cond_in_all, shard_index * ada_rows, ada_rows, axis=1)
    ada_local = ada_weight.reshape(ada_rows, 6 * model_width)
    mod_partial = jnp.dot(cond_cols, ada_local, preferred_element_type=jnp.float32)
    modulation = lax.psum_scatter(mod_partial, "shard", scatter_dimension=0, tiled=True)
    modulation = modulation.reshape(map_count, 6, model_width) + ada_bias[None]
    gamma_one = modulation[:, 0]
    gamma_two = modulation[:, 1]
    scale_one = modulation[:, 2]
    scale_two = modulation[:, 3]
    shift_one = modulation[:, 4]
    shift_two = modulation[:, 5]
    stream_in = hidden_in.astype(jnp.float32)
    first_mod, first_back = jax.vjp(modulate, stream_in, scale_one, shift_one)
    attn_in = first_mod.astype(jnp.bfloat16).reshape(row_count, model_width)
    qkv = jnp.dot(attn_in, qkv_matrix, preferred_element_type=jnp.float32).reshape(
        map_count, piece_rows, 3, local_width
    )
    query = (qkv[:, :, 0] + query_bias).reshape(head_shape)
    key_raw = qkv[:, :, 1].reshape(head_shape)
    value_low = (qkv[:, :, 2] + value_bias).astype(jnp.bfloat16).reshape(head_shape)
    query_unit, query_back = jax.vjp(unit_scaled, query, head_scale)
    key_unit, key_back = jax.vjp(unit_plain, key_raw)
    query_low = query_unit.astype(jnp.bfloat16)
    key_low = key_unit.astype(jnp.bfloat16)
    group_heads = heads_here // ctx_count
    group_shape = (map_count, piece_rows, ctx_count, group_heads, head_dim)
    query_all = group_send(query_low.reshape(group_shape))
    keys_all = group_send(key_low.reshape(group_shape))
    values_all = group_send(value_low.reshape(group_shape))
    scale_ends = jnp.cumsum(scale_len, axis=1)
    owners = (ctx_index - jnp.arange(ctx_count, dtype=jnp.int32)) % ctx_count
    token_pos = owners[:, None] * piece_rows + jnp.arange(piece_rows, dtype=jnp.int32)[None, :]
    ends = scale_ends[:, None, None, :]
    visible_end = jnp.min(jnp.where(ends > token_pos[None, :, :, None], ends, map_length), axis=3)
    key_mask = token_pos[None, None, None, :, :] < visible_end[:, :, :, None, None]

    def masked_scores():
        raw_scores = jnp.einsum(
            "amqgd,bmkgd->mgaqbk", query_all, keys_all, preferred_element_type=jnp.float32
        )
        return jnp.where(key_mask[:, None], raw_scores, -1e30)

    scores = masked_scores()
    row_max = jnp.max(scores, axis=(-2, -1), keepdims=True)
    exp_scores = jnp.exp(scores - row_max)
    exp_total = jnp.sum(exp_scores, axis=(-2, -1), keepdims=True)
    log_total = row_max + jnp.log(exp_total)
    probs_low = (exp_scores / exp_total).astype(jnp.bfloat16)
    out_all = jnp.einsum(
        "mgaqbk,bmkgd->amqgd", probs_low, values_all, preferred_element_type=jnp.float32
    ).astype(jnp.bfloat16)
    heads_out = group_return(out_all).reshape(row_count, local_width)
    attn_partial = jnp.dot(heads_out, full_proj, preferred_element_type=jnp.float32)
    attn_branch = tp_sum(attn_partial).reshape(map_count, piece_rows, model_width) + proj_bias
    attn_part = gamma_one[:, None] * attn_branch
    mid_stream = stream_in + attn_part
    second_mod, second_back = jax.vjp(modulate, mid_stream, scale_two, shift_two)
    mlp_in = second_mod.astype(jnp.bfloat16).reshape(row_count, model_width)
    pre_act = jnp.dot(mlp_in, full_up, preferred_element_type=jnp.float32) + up_bias
    activation, gelu_back = jax.vjp(gelu_tanh, pre_act)
    act_low = activation.astype(jnp.bfloat16)
    mlp_partial = jnp.dot(act_low, full_down, preferred_element_type=jnp.float32)
    mlp_branch = tp_sum(mlp_partial).reshape(map_count, piece_rows, model_width) + down_bias
    mlp_part = gamma_two[:, None] * mlp_branch
    stream = mid_stream + mlp_part
    grad_top = out_grad.astype(jnp.float32)
    d_gamma_two = jnp.sum(grad_top * mlp_branch, axis=1)
    d_mlp = gamma_two[:, None] * grad_top
    d_down_bias = jnp.sum(d_mlp, axis=(0, 1))
    d_mlp_low = d_mlp.astype(jnp.bfloat16).reshape(row_count, model_width)
    g_down = jnp.einsum("rf,rd->fd", act_low, d_mlp_low, preferred_element_type=jnp.float32)
    d_act = jnp.einsum("rd,fd->rf", d_mlp_low, full_down, preferred_element_type=jnp.float32)
    (d_pre,) = gelu_back(d_act)
    d_up_bias = jnp.sum(d_pre, axis=0)
    d_pre_low = d_pre.astype(jnp.bfloat16)
    g_up = jnp.einsum("rd,rf->df", mlp_in, d_pre_low, preferred_element_type=jnp.float32)
    d_mlp_in_part = jnp.einsum("rf,df->rd", d_pre_low, full_up, preferred_element_type=jnp.float32)
    d_mlp_in = tp_sum(d_mlp_in_part).reshape(map_count, piece_rows, model_width)
    d_mid, d_scale_two, d_shift_two = second_back(d_mlp_in)
    d_mid = d_mid + grad_top
    d_gamma_one = jnp.sum(d_mid * attn_branch, axis=1)
    d_attn = gamma_one[:, None] * d_mid
    d_proj_bias = jnp.sum(d_attn, axis=(0, 1))
    d_attn_low = d_attn.astype(jnp.bfloat16).reshape(row_count, model_width)
    g_proj = jnp.einsum("ri,rd->id", heads_out, d_attn_low, preferred_element_type=jnp.float32)
    d_heads = jnp.einsum("rd,id->ri", d_attn_low, full_proj, preferred_element_type=jnp.float32)
    d_heads = d_heads.astype(jnp.bfloat16).reshape(head_shape)
    d_heads_all = group_send(d_heads.reshape(group_shape))
    probs = jnp.exp(masked_scores() - log_total)
    d_probs = jnp.einsum(
        "amqgd,bmkgd->mgaqbk", d_heads_all, values_all, preferred_element_type=jnp.float32
    )
    row_delta = jnp.sum(probs * d_probs, axis=(-2, -1), keepdims=True)
    d_scores = (probs * (d_probs - row_delta)).astype(jnp.bfloat16)
    probs_again = probs.astype(jnp.bfloat16)
    d_query_all = jnp.einsum(
        "mgaqbk,bmkgd->amqgd", d_scores, keys_all, preferred_element_type=jnp.float32
    ).astype(jnp.bfloat16)
    d_key_all = jnp.einsum(
        "mgaqbk,amqgd->bmkgd", d_scores, query_all, preferred_element_type=jnp.float32
    ).astype(jnp.bfloat16)
    d_value_all = jnp.einsum(
        "mgaqbk,amqgd->bmkgd", probs_again, d_heads_all, preferred_element_type=jnp.float32
    ).astype(jnp.bfloat16)
    d_query_unit = group_return(d_query_all).reshape(head_shape).astype(jnp.float32)
    d_key_unit = group_return(d_key_all).reshape(head_shape).astype(jnp.float32)
    d_value = group_return(d_value_all).reshape(head_shape).astype(jnp.float32)
    d_query, d_head_scale = query_back(d_query_unit)
    (d_key,) = key_back(d_key_unit)
    d_query = d_query.reshape(map_count, piece_rows, local_width)
    d_key = d_key.reshape(map_count, piece_rows, local_width)
    d_value = d_value.reshape(map_count, piece_rows, local_width)
    d_query_bias = jnp.sum(d_query, axis=(0, 1))
    d_value_bias = jnp.sum(d_value, axis=(0, 1))
    d_qkv = (
        jnp.stack([d_query, d_key, d_value], axis=2)
        .astype(jnp.bfloat16)
        .reshape(row_count, 3 * local_width)
    )
    g_qkv = jnp.einsum("rd,rc->dc", attn_in, d_qkv, preferred_element_type=jnp.float32).reshape(
        model_width, 3, local_width
    )
    d_attn_in_part = jnp.einsum("rc,dc->rd", d_qkv, qkv_matrix, preferred_element_type=jnp.float32)
    d_attn_in = tp_sum(d_attn_in_part).reshape(map_count, piece_rows, model_width)
    d_input, d_scale_one, d_shift_one = first_back(d_attn_in)
    d_input = d_input + d_mid
    d_mod_part = jnp.stack(
        [d_gamma_one, d_gamma_two, d_scale_one, d_scale_two, d_shift_one, d_shift_two], axis=1
    )
    d_mod = lax.psum(d_mod_part, "ctx").astype(jnp.bfloat16).reshape(map_count, 6 * model_width)
    d_mod_all = lax.all_gather(d_mod, "shard", axis=0, tiled=True)
    g_ada = jnp.einsum(
        "md,mc->dc", cond_cols, d_mod_all, preferred_element_type=jnp.float32
    ).reshape(ada_rows, 6, model_width)
    d_ada_bias = jnp.sum(d_mod_all.astype(jnp.float32), axis=0).reshape(6, model_width)
    d_cond_cols = jnp.einsum("mc,dc->md", d_mod_all, ada_local, preferred_element_type=jnp.float32)
    d_cond_in = lax.all_to_all(d_cond_cols, "shard", 0, 1, tiled=True)
    silu_value, silu_back = jax.vjp(jax.nn.silu, cond_wide)
    (d_cond,) = silu_back(d_cond_in)
    shard_grads = (
        lax.psum_scatter(
            g_qkv.astype(jnp.bfloat16), "shard", scatter_dimension=0, tiled=True
        ),
        lax.psum_scatter(
            g_up.astype(jnp.bfloat16), "shard", scatter_dimension=0, tiled=True
        ),
        lax.psum_scatter(
            g_proj.astype(jnp.bfloat16), "shard", scatter_dimension=1, tiled=True
        ),
        lax.psum_scatter(
            g_down.astype(jnp.bfloat16), "shard", scatter_dimension=1, tiled=True
        ),
    )
    summed = tuple(lax.psum(g, "ctx").astype(jnp.float32) for g in shard_grads)
    square_sums = jnp.stack(
        [jnp.sum(stream * stream), jnp.sum(attn_part * attn_part), jnp.sum(mlp_part * mlp_part)]
    )
    small_parts = (
        square_sums,
        d_query_bias,
        d_value_bias,
        d_head_scale,
        d_proj_bias,
        d_up_bias,
        d_down_bias,
    )
    small_flat = small_sum(jnp.concatenate(small_parts))
    small = []
    offset = 0
    for part in small_parts:
        small.append(small_flat[offset:offset + part.shape[0]])
        offset += part.shape[0]
    entry_total = map_count * map_length * model_width * lax.axis_size("shard")
    norm_stats = jnp.sqrt(small[0] / entry_total)
    return (
        stream.astype(jnp.bfloat16),
        d_input.astype(jnp.bfloat16),
        d_cond,
        g_ada,
        d_ada_bias,
        summed[0],
        small[1],
        small[2],
        small[3],
        summed[2],
        small[4],
        summed[1],
        small[5],
        summed[3],
        small[6],
        norm_stats,
    )


def solution(mesh):
    in_specs = (
        P("shard", "ctx", None),
        P("shard", None),
        P("shard", None),
        P("shard", None, None),
        P(),
        P("shard", None, "tp"),
        P("tp"),
        P("tp"),
        P("tp"),
        P("tp", "shard"),
        P(),
        P("shard", "tp"),
        P("tp"),
        P("tp", "shard"),
        P(),
        P("shard", "ctx", None),
    )
    out_specs = (
        P("shard", "ctx", None),
        P("shard", "ctx", None),
        P("shard", None),
        P("shard", None, None),
        P(),
        P("shard", None, "tp"),
        P("tp"),
        P("tp"),
        P("tp"),
        P("tp", "shard"),
        P(),
        P("shard", "tp"),
        P("tp"),
        P("tp", "shard"),
        P(),
        P(),
    )
    return jax.shard_map(body, mesh=mesh, in_specs=in_specs, out_specs=out_specs, check_vma=False)
```

```python
import jax
import jax.numpy as jnp
from jax import lax
from jax.sharding import PartitionSpec as P


def layer_norm(values):
    center = values - jnp.mean(values, axis=-1, keepdims=True)
    spread = jnp.mean(center * center, axis=-1, keepdims=True)
    return center * lax.rsqrt(spread + 1e-06)


def modulate(values, scale, shift):
    return layer_norm(values) * (1.0 + scale[:, None, :]) + shift[:, None, :]


def unit_scaled(values, gains):
    normed = values * lax.rsqrt(jnp.sum(values * values, axis=-1, keepdims=True) + 1e-06)
    return normed * jnp.exp(gains)[None, None, :, None]


def unit_plain(values):
    return values * lax.rsqrt(jnp.sum(values * values, axis=-1, keepdims=True) + 1e-06)


def gelu_tanh(values):
    return jax.nn.gelu(values, approximate=True)


def tp_sum(values):
    count = lax.axis_size("tp")
    if count != 2:
        return lax.psum(values, "tp")
    return values + lax.ppermute(values, "tp", [(0, 1), (1, 0)])


def ctx_shifts(values):
    count = lax.axis_size("ctx")
    parts = [values]
    for shift in range(1, count):
        pairs = [(i, (i + shift) % count) for i in range(count)]
        parts.append(lax.ppermute(values, "ctx", pairs))
    return jnp.stack(parts)


def ctx_return(parts):
    count = lax.axis_size("ctx")
    total = parts[0].astype(jnp.float32)
    for shift in range(1, count):
        pairs = [(i, (i - shift) % count) for i in range(count)]
        total = total + lax.ppermute(parts[shift], "ctx", pairs).astype(jnp.float32)
    return total


def group_send(values):
    count = lax.axis_size("ctx")
    me = lax.axis_index("ctx")
    parts = []
    for shift in range(count):
        block = lax.dynamic_index_in_dim(values, (me + shift) % count, axis=2, keepdims=False)
        if shift:
            pairs = [(i, (i + shift) % count) for i in range(count)]
            block = lax.ppermute(block, "ctx", pairs)
        parts.append(block)
    return jnp.stack(parts)


def group_return(parts):
    count = lax.axis_size("ctx")
    me = lax.axis_index("ctx")
    back = [parts[0]]
    for shift in range(1, count):
        pairs = [(i, (i - shift) % count) for i in range(count)]
        back.append(lax.ppermute(parts[shift], "ctx", pairs))
    stacked = jnp.stack(back)
    order = (jnp.arange(count, dtype=jnp.int32) - me) % count
    return jnp.moveaxis(jnp.take(stacked, order, axis=0), 0, 2)


def ctx_total(grad):
    count = lax.axis_size("ctx")
    me = lax.axis_index("ctx")
    chunks = grad.reshape(count, -1)
    own = lax.dynamic_index_in_dim(chunks, me, axis=0, keepdims=False).astype(jnp.float32)
    for shift in range(1, count):
        pairs = [(i, (i + shift) % count) for i in range(count)]
        block = lax.dynamic_index_in_dim(chunks, (me + shift) % count, axis=0, keepdims=False)
        own = own + lax.ppermute(block, "ctx", pairs).astype(jnp.float32)
    every = gather_axis(own.astype(jnp.bfloat16), "ctx")
    return every.reshape(grad.shape).astype(jnp.float32)


def gather_axis(values, axis):
    count = lax.axis_size(axis)
    me = lax.axis_index(axis)
    parts = [values]
    for shift in range(1, count):
        pairs = [(i, (i + shift) % count) for i in range(count)]
        parts.append(lax.ppermute(values, axis, pairs))
    stacked = jnp.stack(parts)
    order = (me - jnp.arange(count, dtype=jnp.int32)) % count
    return jnp.take(stacked, order, axis=0)


def small_sum(values):
    every = gather_axis(gather_axis(values, "ctx"), "shard")
    return jnp.sum(every, axis=(0, 1))


def body(
    hidden_in,
    cond,
    scale_len,
    ada_weight,
    ada_bias,
    qkv_weight,
    query_bias,
    value_bias,
    head_scale,
    proj_weight,
    proj_bias,
    up_weight,
    up_bias,
    down_weight,
    down_bias,
    out_grad,
):
    map_count = hidden_in.shape[0]
    piece_rows = hidden_in.shape[1]
    model_width = hidden_in.shape[2]
    ctx_count = lax.axis_size("ctx")
    ctx_index = lax.axis_index("ctx")
    shard_index = lax.axis_index("shard")
    map_length = piece_rows * ctx_count
    heads_here = head_scale.shape[0]
    local_width = query_bias.shape[0]
    head_dim = local_width // heads_here
    row_count = map_count * piece_rows
    head_shape = (map_count, piece_rows, heads_here, head_dim)
    ada_rows = ada_weight.shape[0]
    shard_count = lax.axis_size("shard")
    full_qkv = lax.all_gather(qkv_weight, "shard", axis=0, tiled=True)
    packed = jnp.concatenate([proj_weight.reshape(-1), up_weight.reshape(-1), down_weight.reshape(-1)])
    packed_all = lax.all_gather(packed, "shard", axis=0, tiled=False)
    proj_size, up_size = proj_weight.size, up_weight.size
    proj_parts = packed_all[:, :proj_size].reshape((shard_count,) + proj_weight.shape)
    up_parts = packed_all[:, proj_size:proj_size + up_size].reshape((shard_count,) + up_weight.shape)
    down_parts = packed_all[:, proj_size + up_size:].reshape((shard_count,) + down_weight.shape)
    full_proj = jnp.transpose(proj_parts, (1, 0, 2)).reshape(proj_weight.shape[0], -1)
    full_up = up_parts.reshape(-1, up_weight.shape[1])
    full_down = jnp.transpose(down_parts, (1, 0, 2)).reshape(down_weight.shape[0], -1)
    qkv_matrix = full_qkv.reshape(model_width, 3 * local_width)

    cond_wide = cond.astype(jnp.float32)
    cond_all = lax.all_gather(cond, "shard", axis=0, tiled=True).astype(jnp.float32)
    cond_in_all = jax.nn.silu(cond_all).astype(jnp.bfloat16)
    cond_cols = lax.dynamic_slice_in_dim(cond_in_all, shard_index * ada_rows, ada_rows, axis=1)
    ada_local = ada_weight.reshape(ada_rows, 6 * model_width)
    mod_partial = jnp.dot(cond_cols, ada_local, preferred_element_type=jnp.float32)
    modulation = lax.psum_scatter(mod_partial, "shard", scatter_dimension=0, tiled=True)
    modulation = modulation.reshape(map_count, 6, model_width) + ada_bias[None]
    gamma_one = modulation[:, 0]
    gamma_two = modulation[:, 1]
    scale_one = modulation[:, 2]
    scale_two = modulation[:, 3]
    shift_one = modulation[:, 4]
    shift_two = modulation[:, 5]
    stream_in = hidden_in.astype(jnp.float32)
    first_mod, first_back = jax.vjp(modulate, stream_in, scale_one, shift_one)
    attn_in = first_mod.astype(jnp.bfloat16).reshape(row_count, model_width)
    qkv = jnp.dot(attn_in, qkv_matrix, preferred_element_type=jnp.float32).reshape(
        map_count, piece_rows, 3, local_width
    )
    query = (qkv[:, :, 0] + query_bias).reshape(head_shape)
    key_raw = qkv[:, :, 1].reshape(head_shape)
    value_low = (qkv[:, :, 2] + value_bias).astype(jnp.bfloat16).reshape(head_shape)
    query_unit, query_back = jax.vjp(unit_scaled, query, head_scale)
    key_unit, key_back = jax.vjp(unit_plain, key_raw)
    query_low = query_unit.astype(jnp.bfloat16)
    key_low = key_unit.astype(jnp.bfloat16)
    group_heads = heads_here // ctx_count
    group_shape = (map_count, piece_rows, ctx_count, group_heads, head_dim)
    query_all = group_send(query_low.reshape(group_shape))
    keys_all = group_send(key_low.reshape(group_shape))
    values_all = group_send(value_low.reshape(group_shape))
    scale_ends = jnp.cumsum(scale_len, axis=1)
    owners = (ctx_index - jnp.arange(ctx_count, dtype=jnp.int32)) % ctx_count
    token_pos = owners[:, None] * piece_rows + jnp.arange(piece_rows, dtype=jnp.int32)[None, :]
    ends = scale_ends[:, None, None, :]
    visible_end = jnp.min(jnp.where(ends > token_pos[None, :, :, None], ends, map_length), axis=3)
    key_mask = token_pos[None, None, None, :, :] < visible_end[:, :, :, None, None]

    def masked_scores():
        raw_scores = jnp.einsum(
            "amqgd,bmkgd->mgaqbk", query_all, keys_all, preferred_element_type=jnp.float32
        )
        return jnp.where(key_mask[:, None], raw_scores, -1e30)

    scores = masked_scores()
    row_max = jnp.max(scores, axis=(-2, -1), keepdims=True)
    exp_scores = jnp.exp(scores - row_max)
    exp_total = jnp.sum(exp_scores, axis=(-2, -1), keepdims=True)
    log_total = row_max + jnp.log(exp_total)
    probs_low = (exp_scores / exp_total).astype(jnp.bfloat16)
    out_all = jnp.einsum(
        "mgaqbk,bmkgd->amqgd", probs_low, values_all, preferred_element_type=jnp.float32
    ).astype(jnp.bfloat16)
    heads_out = group_return(out_all).reshape(row_count, local_width)
    attn_partial = jnp.dot(heads_out, full_proj, preferred_element_type=jnp.float32)
    attn_branch = tp_sum(attn_partial).reshape(map_count, piece_rows, model_width) + proj_bias
    attn_part = gamma_one[:, None] * attn_branch
    mid_stream = stream_in + attn_part
    second_mod, second_back = jax.vjp(modulate, mid_stream, scale_two, shift_two)
    mlp_in = second_mod.astype(jnp.bfloat16).reshape(row_count, model_width)
    pre_act = jnp.dot(mlp_in, full_up, preferred_element_type=jnp.float32) + up_bias
    activation, gelu_back = jax.vjp(gelu_tanh, pre_act)
    act_low = activation.astype(jnp.bfloat16)
    mlp_partial = jnp.dot(act_low, full_down, preferred_element_type=jnp.float32)
    mlp_branch = tp_sum(mlp_partial).reshape(map_count, piece_rows, model_width) + down_bias
    mlp_part = gamma_two[:, None] * mlp_branch
    stream = mid_stream + mlp_part
    grad_top = out_grad.astype(jnp.float32)
    d_gamma_two = jnp.sum(grad_top * mlp_branch, axis=1)
    d_mlp = gamma_two[:, None] * grad_top
    d_down_bias = jnp.sum(d_mlp, axis=(0, 1))
    d_mlp_low = d_mlp.astype(jnp.bfloat16).reshape(row_count, model_width)
    g_down = jnp.einsum("rf,rd->fd", act_low, d_mlp_low, preferred_element_type=jnp.float32)
    d_act = jnp.einsum("rd,fd->rf", d_mlp_low, full_down, preferred_element_type=jnp.float32)
    (d_pre,) = gelu_back(d_act)
    d_up_bias = jnp.sum(d_pre, axis=0)
    d_pre_low = d_pre.astype(jnp.bfloat16)
    g_up = jnp.einsum("rd,rf->df", mlp_in, d_pre_low, preferred_element_type=jnp.float32)
    d_mlp_in_part = jnp.einsum("rf,df->rd", d_pre_low, full_up, preferred_element_type=jnp.float32)
    d_mlp_in = tp_sum(d_mlp_in_part).reshape(map_count, piece_rows, model_width)
    d_mid, d_scale_two, d_shift_two = second_back(d_mlp_in)
    d_mid = d_mid + grad_top
    d_gamma_one = jnp.sum(d_mid * attn_branch, axis=1)
    d_attn = gamma_one[:, None] * d_mid
    d_proj_bias = jnp.sum(d_attn, axis=(0, 1))
    d_attn_low = d_attn.astype(jnp.bfloat16).reshape(row_count, model_width)
    g_proj = jnp.einsum("ri,rd->id", heads_out, d_attn_low, preferred_element_type=jnp.float32)
    d_heads = jnp.einsum("rd,id->ri", d_attn_low, full_proj, preferred_element_type=jnp.float32)
    d_heads = d_heads.astype(jnp.bfloat16).reshape(head_shape)
    d_heads_all = group_send(d_heads.reshape(group_shape))
    probs = jnp.exp(masked_scores() - log_total)
    d_probs = jnp.einsum(
        "amqgd,bmkgd->mgaqbk", d_heads_all, values_all, preferred_element_type=jnp.float32
    )
    row_delta = jnp.sum(probs * d_probs, axis=(-2, -1), keepdims=True)
    d_scores = (probs * (d_probs - row_delta)).astype(jnp.bfloat16)
    probs_again = probs.astype(jnp.bfloat16)
    d_query_all = jnp.einsum(
        "mgaqbk,bmkgd->amqgd", d_scores, keys_all, preferred_element_type=jnp.float32
    ).astype(jnp.bfloat16)
    d_key_all = jnp.einsum(
        "mgaqbk,amqgd->bmkgd", d_scores, query_all, preferred_element_type=jnp.float32
    ).astype(jnp.bfloat16)
    d_value_all = jnp.einsum(
        "mgaqbk,amqgd->bmkgd", probs_again, d_heads_all, preferred_element_type=jnp.float32
    ).astype(jnp.bfloat16)
    d_query_unit = group_return(d_query_all).reshape(head_shape).astype(jnp.float32)
    d_key_unit = group_return(d_key_all).reshape(head_shape).astype(jnp.float32)
    d_value = group_return(d_value_all).reshape(head_shape).astype(jnp.float32)
    d_query, d_head_scale = query_back(d_query_unit)
    (d_key,) = key_back(d_key_unit)
    d_query = d_query.reshape(map_count, piece_rows, local_width)
    d_key = d_key.reshape(map_count, piece_rows, local_width)
    d_value = d_value.reshape(map_count, piece_rows, local_width)
    d_query_bias = jnp.sum(d_query, axis=(0, 1))
    d_value_bias = jnp.sum(d_value, axis=(0, 1))
    d_qkv = (
        jnp.stack([d_query, d_key, d_value], axis=2)
        .astype(jnp.bfloat16)
        .reshape(row_count, 3 * local_width)
    )
    g_qkv = jnp.einsum("rd,rc->dc", attn_in, d_qkv, preferred_element_type=jnp.float32).reshape(
        model_width, 3, local_width
    )
    d_attn_in_part = jnp.einsum("rc,dc->rd", d_qkv, qkv_matrix, preferred_element_type=jnp.float32)
    d_attn_in = tp_sum(d_attn_in_part).reshape(map_count, piece_rows, model_width)
    d_input, d_scale_one, d_shift_one = first_back(d_attn_in)
    d_input = d_input + d_mid
    d_mod_part = jnp.stack(
        [d_gamma_one, d_gamma_two, d_scale_one, d_scale_two, d_shift_one, d_shift_two], axis=1
    )
    d_mod = jnp.sum(gather_axis(d_mod_part, "ctx"), axis=0).astype(jnp.bfloat16)
    d_mod_all = gather_axis(d_mod.reshape(map_count, 6 * model_width), "shard").reshape(-1, 6 * model_width)
    g_ada = jnp.einsum(
        "md,mc->dc", cond_cols, d_mod_all, preferred_element_type=jnp.float32
    ).reshape(ada_rows, 6, model_width)
    d_ada_bias = jnp.sum(d_mod_all.astype(jnp.float32), axis=0).reshape(6, model_width)
    d_cond_cols = jnp.einsum("mc,dc->md", d_mod_all, ada_local, preferred_element_type=jnp.float32)
    d_cond_in = lax.all_to_all(d_cond_cols, "shard", 0, 1, tiled=True)
    silu_value, silu_back = jax.vjp(jax.nn.silu, cond_wide)
    (d_cond,) = silu_back(d_cond_in)
    shard_grads = (
        lax.psum_scatter(
            g_qkv.astype(jnp.bfloat16), "shard", scatter_dimension=0, tiled=True
        ),
        lax.psum_scatter(
            g_up.astype(jnp.bfloat16), "shard", scatter_dimension=0, tiled=True
        ),
        lax.psum_scatter(
            g_proj.astype(jnp.bfloat16), "shard", scatter_dimension=1, tiled=True
        ),
        lax.psum_scatter(
            g_down.astype(jnp.bfloat16), "shard", scatter_dimension=1, tiled=True
        ),
    )
    summed = tuple(ctx_total(g) for g in shard_grads)
    square_sums = jnp.stack(
        [jnp.sum(stream * stream), jnp.sum(attn_part * attn_part), jnp.sum(mlp_part * mlp_part)]
    )
    small_parts = (
        square_sums,
        d_query_bias,
        d_value_bias,
        d_head_scale,
        d_proj_bias,
        d_up_bias,
        d_down_bias,
    )
    small_flat = small_sum(jnp.concatenate(small_parts))
    small = []
    offset = 0
    for part in small_parts:
        small.append(small_flat[offset:offset + part.shape[0]])
        offset += part.shape[0]
    entry_total = map_count * map_length * model_width * lax.axis_size("shard")
    norm_stats = jnp.sqrt(small[0] / entry_total)
    return (
        stream.astype(jnp.bfloat16),
        d_input.astype(jnp.bfloat16),
        d_cond,
        g_ada,
        d_ada_bias,
        summed[0],
        small[1],
        small[2],
        small[3],
        summed[2],
        small[4],
        summed[1],
        small[5],
        summed[3],
        small[6],
        norm_stats,
    )


def solution(mesh):
    in_specs = (
        P("shard", "ctx", None),
        P("shard", None),
        P("shard", None),
        P("shard", None, None),
        P(),
        P("shard", None, "tp"),
        P("tp"),
        P("tp"),
        P("tp"),
        P("tp", "shard"),
        P(),
        P("shard", "tp"),
        P("tp"),
        P("tp", "shard"),
        P(),
        P("shard", "ctx", None),
    )
    out_specs = (
        P("shard", "ctx", None),
        P("shard", "ctx", None),
        P("shard", None),
        P("shard", None, None),
        P(),
        P("shard", None, "tp"),
        P("tp"),
        P("tp"),
        P("tp"),
        P("tp", "shard"),
        P(),
        P("shard", "tp"),
        P("tp"),
        P("tp", "shard"),
        P(),
        P(),
    )
    return jax.shard_map(body, mesh=mesh, in_specs=in_specs, out_specs=out_specs, check_vma=False)
```

```python
import jax
import jax.numpy as jnp
from jax import lax
from jax.sharding import PartitionSpec as P


def layer_norm(values):
    center = values - jnp.mean(values, axis=-1, keepdims=True)
    spread = jnp.mean(center * center, axis=-1, keepdims=True)
    return center * lax.rsqrt(spread + 1e-06)


def modulate(values, scale, shift):
    return layer_norm(values) * (1.0 + scale[:, None, :]) + shift[:, None, :]


def unit_scaled(values, gains):
    normed = values * lax.rsqrt(jnp.sum(values * values, axis=-1, keepdims=True) + 1e-06)
    return normed * jnp.exp(gains)[None, None, :, None]


def unit_plain(values):
    return values * lax.rsqrt(jnp.sum(values * values, axis=-1, keepdims=True) + 1e-06)


def gelu_tanh(values):
    return jax.nn.gelu(values, approximate=True)


def tp_sum(values):
    count = lax.axis_size("tp")
    if count != 2:
        return lax.psum(values, "tp")
    return values + lax.ppermute(values, "tp", [(0, 1), (1, 0)])


def ctx_shifts(values):
    count = lax.axis_size("ctx")
    parts = [values]
    for shift in range(1, count):
        pairs = [(i, (i + shift) % count) for i in range(count)]
        parts.append(lax.ppermute(values, "ctx", pairs))
    return jnp.stack(parts)


def ctx_return(parts):
    count = lax.axis_size("ctx")
    total = parts[0].astype(jnp.float32)
    for shift in range(1, count):
        pairs = [(i, (i - shift) % count) for i in range(count)]
        total = total + lax.ppermute(parts[shift], "ctx", pairs).astype(jnp.float32)
    return total


def group_send(values):
    count = lax.axis_size("ctx")
    me = lax.axis_index("ctx")
    parts = []
    for shift in range(count):
        block = lax.dynamic_index_in_dim(values, (me + shift) % count, axis=2, keepdims=False)
        if shift:
            pairs = [(i, (i + shift) % count) for i in range(count)]
            block = lax.ppermute(block, "ctx", pairs)
        parts.append(block)
    return jnp.stack(parts)


def group_return(parts):
    count = lax.axis_size("ctx")
    me = lax.axis_index("ctx")
    back = [parts[0]]
    for shift in range(1, count):
        pairs = [(i, (i - shift) % count) for i in range(count)]
        back.append(lax.ppermute(parts[shift], "ctx", pairs))
    stacked = jnp.stack(back)
    order = (jnp.arange(count, dtype=jnp.int32) - me) % count
    return jnp.moveaxis(jnp.take(stacked, order, axis=0), 0, 2)


def gather_axis(values, axis):
    count = lax.axis_size(axis)
    me = lax.axis_index(axis)
    parts = [values]
    for shift in range(1, count):
        pairs = [(i, (i + shift) % count) for i in range(count)]
        parts.append(lax.ppermute(values, axis, pairs))
    stacked = jnp.stack(parts)
    order = (me - jnp.arange(count, dtype=jnp.int32)) % count
    return jnp.take(stacked, order, axis=0)


def small_sum(values):
    every = gather_axis(gather_axis(values, "ctx"), "shard")
    return jnp.sum(every, axis=(0, 1))


def body(
    hidden_in,
    cond,
    scale_len,
    ada_weight,
    ada_bias,
    qkv_weight,
    query_bias,
    value_bias,
    head_scale,
    proj_weight,
    proj_bias,
    up_weight,
    up_bias,
    down_weight,
    down_bias,
    out_grad,
):
    map_count = hidden_in.shape[0]
    piece_rows = hidden_in.shape[1]
    model_width = hidden_in.shape[2]
    ctx_count = lax.axis_size("ctx")
    ctx_index = lax.axis_index("ctx")
    shard_index = lax.axis_index("shard")
    map_length = piece_rows * ctx_count
    heads_here = head_scale.shape[0]
    local_width = query_bias.shape[0]
    head_dim = local_width // heads_here
    row_count = map_count * piece_rows
    head_shape = (map_count, piece_rows, heads_here, head_dim)
    ada_rows = ada_weight.shape[0]
    shard_count = lax.axis_size("shard")
    full_qkv = lax.all_gather(qkv_weight, "shard", axis=0, tiled=True)
    packed = jnp.concatenate([proj_weight.reshape(-1), up_weight.reshape(-1), down_weight.reshape(-1)])
    packed_all = lax.all_gather(packed, "shard", axis=0, tiled=False)
    proj_size, up_size = proj_weight.size, up_weight.size
    proj_parts = packed_all[:, :proj_size].reshape((shard_count,) + proj_weight.shape)
    up_parts = packed_all[:, proj_size:proj_size + up_size].reshape((shard_count,) + up_weight.shape)
    down_parts = packed_all[:, proj_size + up_size:].reshape((shard_count,) + down_weight.shape)
    full_proj = jnp.transpose(proj_parts, (1, 0, 2)).reshape(proj_weight.shape[0], -1)
    full_up = up_parts.reshape(-1, up_weight.shape[1])
    full_down = jnp.transpose(down_parts, (1, 0, 2)).reshape(down_weight.shape[0], -1)
    qkv_matrix = full_qkv.reshape(model_width, 3 * local_width)

    cond_wide = cond.astype(jnp.float32)
    cond_all = lax.all_gather(cond, "shard", axis=0, tiled=True).astype(jnp.float32)
    cond_in_all = jax.nn.silu(cond_all).astype(jnp.bfloat16)
    cond_cols = lax.dynamic_slice_in_dim(cond_in_all, shard_index * ada_rows, ada_rows, axis=1)
    ada_local = ada_weight.reshape(ada_rows, 6 * model_width)
    mod_partial = jnp.dot(cond_cols, ada_local, preferred_element_type=jnp.float32)
    modulation = lax.psum_scatter(mod_partial, "shard", scatter_dimension=0, tiled=True)
    modulation = modulation.reshape(map_count, 6, model_width) + ada_bias[None]
    gamma_one = modulation[:, 0]
    gamma_two = modulation[:, 1]
    scale_one = modulation[:, 2]
    scale_two = modulation[:, 3]
    shift_one = modulation[:, 4]
    shift_two = modulation[:, 5]
    stream_in = hidden_in.astype(jnp.float32)
    first_mod, first_back = jax.vjp(modulate, stream_in, scale_one, shift_one)
    attn_in = first_mod.astype(jnp.bfloat16).reshape(row_count, model_width)
    qkv = jnp.dot(attn_in, qkv_matrix, preferred_element_type=jnp.float32).reshape(
        map_count, piece_rows, 3, local_width
    )
    query = (qkv[:, :, 0] + query_bias).reshape(head_shape)
    key_raw = qkv[:, :, 1].reshape(head_shape)
    value_low = (qkv[:, :, 2] + value_bias).astype(jnp.bfloat16).reshape(head_shape)
    query_unit, query_back = jax.vjp(unit_scaled, query, head_scale)
    key_unit, key_back = jax.vjp(unit_plain, key_raw)
    query_low = query_unit.astype(jnp.bfloat16)
    key_low = key_unit.astype(jnp.bfloat16)
    group_heads = heads_here // ctx_count
    group_shape = (map_count, piece_rows, ctx_count, group_heads, head_dim)
    query_all = group_send(query_low.reshape(group_shape))
    keys_all = group_send(key_low.reshape(group_shape))
    values_all = group_send(value_low.reshape(group_shape))
    scale_ends = jnp.cumsum(scale_len, axis=1)
    owners = (ctx_index - jnp.arange(ctx_count, dtype=jnp.int32)) % ctx_count
    token_pos = owners[:, None] * piece_rows + jnp.arange(piece_rows, dtype=jnp.int32)[None, :]
    ends = scale_ends[:, None, None, :]
    visible_end = jnp.min(jnp.where(ends > token_pos[None, :, :, None], ends, map_length), axis=3)
    key_mask = token_pos[None, None, None, :, :] < visible_end[:, :, :, None, None]

    def masked_scores():
        raw_scores = jnp.einsum(
            "amqgd,bmkgd->mgaqbk", query_all, keys_all, preferred_element_type=jnp.float32
        )
        return jnp.where(key_mask[:, None], raw_scores, -1e30)

    scores = masked_scores()
    row_max = jnp.max(scores, axis=(-2, -1), keepdims=True)
    exp_scores = jnp.exp(scores - row_max)
    exp_total = jnp.sum(exp_scores, axis=(-2, -1), keepdims=True)
    log_total = row_max + jnp.log(exp_total)
    probs_low = (exp_scores / exp_total).astype(jnp.bfloat16)
    out_all = jnp.einsum(
        "mgaqbk,bmkgd->amqgd", probs_low, values_all, preferred_element_type=jnp.float32
    ).astype(jnp.bfloat16)
    heads_out = group_return(out_all).reshape(row_count, local_width)
    attn_partial = jnp.dot(heads_out, full_proj, preferred_element_type=jnp.float32)
    attn_branch = tp_sum(attn_partial).reshape(map_count, piece_rows, model_width) + proj_bias
    attn_part = gamma_one[:, None] * attn_branch
    mid_stream = stream_in + attn_part
    second_mod, second_back = jax.vjp(modulate, mid_stream, scale_two, shift_two)
    mlp_in = second_mod.astype(jnp.bfloat16).reshape(row_count, model_width)
    pre_act = jnp.dot(mlp_in, full_up, preferred_element_type=jnp.float32) + up_bias
    activation, gelu_back = jax.vjp(gelu_tanh, pre_act)
    act_low = activation.astype(jnp.bfloat16)
    mlp_partial = jnp.dot(act_low, full_down, preferred_element_type=jnp.float32)
    mlp_branch = tp_sum(mlp_partial).reshape(map_count, piece_rows, model_width) + down_bias
    mlp_part = gamma_two[:, None] * mlp_branch
    stream = mid_stream + mlp_part
    grad_top = out_grad.astype(jnp.float32)
    d_gamma_two = jnp.sum(grad_top * mlp_branch, axis=1)
    d_mlp = gamma_two[:, None] * grad_top
    d_down_bias = jnp.sum(d_mlp, axis=(0, 1))
    d_mlp_low = d_mlp.astype(jnp.bfloat16).reshape(row_count, model_width)
    g_down = jnp.einsum("rf,rd->fd", act_low, d_mlp_low, preferred_element_type=jnp.float32)
    d_act = jnp.einsum("rd,fd->rf", d_mlp_low, full_down, preferred_element_type=jnp.float32)
    (d_pre,) = gelu_back(d_act)
    d_up_bias = jnp.sum(d_pre, axis=0)
    d_pre_low = d_pre.astype(jnp.bfloat16)
    g_up = jnp.einsum("rd,rf->df", mlp_in, d_pre_low, preferred_element_type=jnp.float32)
    d_mlp_in_part = jnp.einsum("rf,df->rd", d_pre_low, full_up, preferred_element_type=jnp.float32)
    d_mlp_in = tp_sum(d_mlp_in_part).reshape(map_count, piece_rows, model_width)
    d_mid, d_scale_two, d_shift_two = second_back(d_mlp_in)
    d_mid = d_mid + grad_top
    d_gamma_one = jnp.sum(d_mid * attn_branch, axis=1)
    d_attn = gamma_one[:, None] * d_mid
    d_proj_bias = jnp.sum(d_attn, axis=(0, 1))
    d_attn_low = d_attn.astype(jnp.bfloat16).reshape(row_count, model_width)
    g_proj = jnp.einsum("ri,rd->id", heads_out, d_attn_low, preferred_element_type=jnp.float32)
    d_heads = jnp.einsum("rd,id->ri", d_attn_low, full_proj, preferred_element_type=jnp.float32)
    d_heads = d_heads.astype(jnp.bfloat16).reshape(head_shape)
    d_heads_all = group_send(d_heads.reshape(group_shape))
    probs = probs_low.astype(jnp.float32)
    d_probs = jnp.einsum(
        "amqgd,bmkgd->mgaqbk", d_heads_all, values_all, preferred_element_type=jnp.float32
    )
    row_delta = jnp.sum(probs * d_probs, axis=(-2, -1), keepdims=True)
    d_scores = (probs * (d_probs - row_delta)).astype(jnp.bfloat16)
    probs_again = probs_low
    d_query_all = jnp.einsum(
        "mgaqbk,bmkgd->amqgd", d_scores, keys_all, preferred_element_type=jnp.float32
    ).astype(jnp.bfloat16)
    d_key_all = jnp.einsum(
        "mgaqbk,amqgd->bmkgd", d_scores, query_all, preferred_element_type=jnp.float32
    ).astype(jnp.bfloat16)
    d_value_all = jnp.einsum(
        "mgaqbk,amqgd->bmkgd", probs_again, d_heads_all, preferred_element_type=jnp.float32
    ).astype(jnp.bfloat16)
    d_query_unit = group_return(d_query_all).reshape(head_shape).astype(jnp.float32)
    d_key_unit = group_return(d_key_all).reshape(head_shape).astype(jnp.float32)
    d_value = group_return(d_value_all).reshape(head_shape).astype(jnp.float32)
    d_query, d_head_scale = query_back(d_query_unit)
    (d_key,) = key_back(d_key_unit)
    d_query = d_query.reshape(map_count, piece_rows, local_width)
    d_key = d_key.reshape(map_count, piece_rows, local_width)
    d_value = d_value.reshape(map_count, piece_rows, local_width)
    d_query_bias = jnp.sum(d_query, axis=(0, 1))
    d_value_bias = jnp.sum(d_value, axis=(0, 1))
    d_qkv = (
        jnp.stack([d_query, d_key, d_value], axis=2)
        .astype(jnp.bfloat16)
        .reshape(row_count, 3 * local_width)
    )
    g_qkv = jnp.einsum("rd,rc->dc", attn_in, d_qkv, preferred_element_type=jnp.float32).reshape(
        model_width, 3, local_width
    )
    d_attn_in_part = jnp.einsum("rc,dc->rd", d_qkv, qkv_matrix, preferred_element_type=jnp.float32)
    d_attn_in = tp_sum(d_attn_in_part).reshape(map_count, piece_rows, model_width)
    d_input, d_scale_one, d_shift_one = first_back(d_attn_in)
    d_input = d_input + d_mid
    d_mod_part = jnp.stack(
        [d_gamma_one, d_gamma_two, d_scale_one, d_scale_two, d_shift_one, d_shift_two], axis=1
    )
    d_mod = lax.psum(d_mod_part, "ctx").astype(jnp.bfloat16).reshape(map_count, 6 * model_width)
    d_mod_all = lax.all_gather(d_mod, "shard", axis=0, tiled=True)
    g_ada = jnp.einsum(
        "md,mc->dc", cond_cols, d_mod_all, preferred_element_type=jnp.float32
    ).reshape(ada_rows, 6, model_width)
    d_ada_bias = jnp.sum(d_mod_all.astype(jnp.float32), axis=0).reshape(6, model_width)
    d_cond_cols = jnp.einsum("mc,dc->md", d_mod_all, ada_local, preferred_element_type=jnp.float32)
    d_cond_in = lax.all_to_all(d_cond_cols, "shard", 0, 1, tiled=True)
    silu_value, silu_back = jax.vjp(jax.nn.silu, cond_wide)
    (d_cond,) = silu_back(d_cond_in)
    early_shards = (
        lax.psum_scatter(
            g_up.astype(jnp.bfloat16), "shard", scatter_dimension=0, tiled=True
        ),
        lax.psum_scatter(
            g_proj.astype(jnp.bfloat16), "shard", scatter_dimension=1, tiled=True
        ),
        lax.psum_scatter(
            g_down.astype(jnp.bfloat16), "shard", scatter_dimension=1, tiled=True
        ),
    )
    early_summed = lax.psum(early_shards, "ctx")
    qkv_low, early_summed = lax.optimization_barrier((g_qkv.astype(jnp.bfloat16), early_summed))
    qkv_shard = lax.psum_scatter(qkv_low, "shard", scatter_dimension=0, tiled=True)
    qkv_summed = lax.psum(qkv_shard, "ctx")
    summed = tuple(
        g.astype(jnp.float32) for g in (qkv_summed, early_summed[0], early_summed[1], early_summed[2])
    )
    square_sums = jnp.stack(
        [jnp.sum(stream * stream), jnp.sum(attn_part * attn_part), jnp.sum(mlp_part * mlp_part)]
    )
    small_parts = (
        square_sums,
        d_query_bias,
        d_value_bias,
        d_head_scale,
        d_proj_bias,
        d_up_bias,
        d_down_bias,
    )
    small_flat = small_sum(jnp.concatenate(small_parts))
    small = []
    offset = 0
    for part in small_parts:
        small.append(small_flat[offset:offset + part.shape[0]])
        offset += part.shape[0]
    entry_total = map_count * map_length * model_width * lax.axis_size("shard")
    norm_stats = jnp.sqrt(small[0] / entry_total)
    return (
        stream.astype(jnp.bfloat16),
        d_input.astype(jnp.bfloat16),
        d_cond,
        g_ada,
        d_ada_bias,
        summed[0],
        small[1],
        small[2],
        small[3],
        summed[2],
        small[4],
        summed[1],
        small[5],
        summed[3],
        small[6],
        norm_stats,
    )


def solution(mesh):
    in_specs = (
        P("shard", "ctx", None),
        P("shard", None),
        P("shard", None),
        P("shard", None, None),
        P(),
        P("shard", None, "tp"),
        P("tp"),
        P("tp"),
        P("tp"),
        P("tp", "shard"),
        P(),
        P("shard", "tp"),
        P("tp"),
        P("tp", "shard"),
        P(),
        P("shard", "ctx", None),
    )
    out_specs = (
        P("shard", "ctx", None),
        P("shard", "ctx", None),
        P("shard", None),
        P("shard", None, None),
        P(),
        P("shard", None, "tp"),
        P("tp"),
        P("tp"),
        P("tp"),
        P("tp", "shard"),
        P(),
        P("shard", "tp"),
        P("tp"),
        P("tp", "shard"),
        P(),
        P(),
    )
    return jax.shard_map(body, mesh=mesh, in_specs=in_specs, out_specs=out_specs, check_vma=False)
```

```python
import jax
import jax.numpy as jnp
from jax import lax
from jax.sharding import PartitionSpec as P


def layer_norm(values):
    center = values - jnp.mean(values, axis=-1, keepdims=True)
    spread = jnp.mean(center * center, axis=-1, keepdims=True)
    return center * lax.rsqrt(spread + 1e-06)


def modulate(values, scale, shift):
    return layer_norm(values) * (1.0 + scale[:, None, :]) + shift[:, None, :]


def unit_scaled(values, gains):
    normed = values * lax.rsqrt(jnp.sum(values * values, axis=-1, keepdims=True) + 1e-06)
    return normed * jnp.exp(gains)[None, None, :, None]


def unit_plain(values):
    return values * lax.rsqrt(jnp.sum(values * values, axis=-1, keepdims=True) + 1e-06)


def gelu_tanh(values):
    return jax.nn.gelu(values, approximate=True)


def tp_sum(values):
    count = lax.axis_size("tp")
    if count != 2:
        return lax.psum(values, "tp")
    return values + lax.ppermute(values, "tp", [(0, 1), (1, 0)])


def group_send(values):
    count = lax.axis_size("ctx")
    me = lax.axis_index("ctx")
    parts = []
    for shift in range(count):
        block = lax.dynamic_index_in_dim(values, (me + shift) % count, axis=2, keepdims=False)
        if shift:
            pairs = [(i, (i + shift) % count) for i in range(count)]
            block = lax.ppermute(block, "ctx", pairs)
        parts.append(block)
    return jnp.stack(parts)


def group_return(parts):
    count = lax.axis_size("ctx")
    me = lax.axis_index("ctx")
    back = [parts[0]]
    for shift in range(1, count):
        pairs = [(i, (i - shift) % count) for i in range(count)]
        back.append(lax.ppermute(parts[shift], "ctx", pairs))
    stacked = jnp.stack(back)
    order = (jnp.arange(count, dtype=jnp.int32) - me) % count
    return jnp.moveaxis(jnp.take(stacked, order, axis=0), 0, 2)


def gather_axis(values, axis):
    count = lax.axis_size(axis)
    me = lax.axis_index(axis)
    parts = [values]
    for shift in range(1, count):
        pairs = [(i, (i + shift) % count) for i in range(count)]
        parts.append(lax.ppermute(values, axis, pairs))
    stacked = jnp.stack(parts)
    order = (me - jnp.arange(count, dtype=jnp.int32)) % count
    return jnp.take(stacked, order, axis=0)


def small_sum(values):
    every = gather_axis(gather_axis(values, "ctx"), "shard")
    return jnp.sum(every, axis=(0, 1))


def block(
    hidden_in,
    cond,
    scale_len,
    ada_weight,
    ada_bias,
    qkv_weight,
    query_bias,
    value_bias,
    head_scale,
    proj_weight,
    proj_bias,
    up_weight,
    up_bias,
    down_weight,
    down_bias,
    out_grad,
):
    map_count = hidden_in.shape[0]
    piece_rows = hidden_in.shape[1]
    model_width = hidden_in.shape[2]
    ctx_count = lax.axis_size("ctx")
    ctx_index = lax.axis_index("ctx")
    shard_index = lax.axis_index("shard")
    map_length = piece_rows * ctx_count
    heads_here = head_scale.shape[0]
    local_width = query_bias.shape[0]
    head_dim = local_width // heads_here
    row_count = map_count * piece_rows
    head_shape = (map_count, piece_rows, heads_here, head_dim)
    ada_rows = ada_weight.shape[0]
    shard_count = lax.axis_size("shard")
    full_qkv = lax.all_gather(qkv_weight, "shard", axis=0, tiled=True)
    packed = jnp.concatenate([proj_weight.reshape(-1), up_weight.reshape(-1), down_weight.reshape(-1)])
    packed_all = lax.all_gather(packed, "shard", axis=0, tiled=False)
    proj_size, up_size = proj_weight.size, up_weight.size
    proj_parts = packed_all[:, :proj_size].reshape((shard_count,) + proj_weight.shape)
    up_parts = packed_all[:, proj_size:proj_size + up_size].reshape((shard_count,) + up_weight.shape)
    down_parts = packed_all[:, proj_size + up_size:].reshape((shard_count,) + down_weight.shape)
    full_proj = jnp.transpose(proj_parts, (1, 0, 2)).reshape(proj_weight.shape[0], -1)
    full_up = up_parts.reshape(-1, up_weight.shape[1])
    full_down = jnp.transpose(down_parts, (1, 0, 2)).reshape(down_weight.shape[0], -1)
    qkv_matrix = full_qkv.reshape(model_width, 3 * local_width)

    cond_wide = cond.astype(jnp.float32)
    cond_all = lax.all_gather(cond, "shard", axis=0, tiled=True).astype(jnp.float32)
    cond_in_all = jax.nn.silu(cond_all).astype(jnp.bfloat16)
    cond_cols = lax.dynamic_slice_in_dim(cond_in_all, shard_index * ada_rows, ada_rows, axis=1)
    ada_local = ada_weight.reshape(ada_rows, 6 * model_width)
    mod_partial = jnp.dot(cond_cols, ada_local, preferred_element_type=jnp.float32)
    modulation = lax.psum_scatter(mod_partial, "shard", scatter_dimension=0, tiled=True)
    modulation = modulation.reshape(map_count, 6, model_width) + ada_bias[None]
    gamma_one = modulation[:, 0]
    gamma_two = modulation[:, 1]
    scale_one = modulation[:, 2]
    scale_two = modulation[:, 3]
    shift_one = modulation[:, 4]
    shift_two = modulation[:, 5]
    stream_in = hidden_in.astype(jnp.float32)
    first_mod, first_back = jax.vjp(modulate, stream_in, scale_one, shift_one)
    attn_in = first_mod.astype(jnp.bfloat16).reshape(row_count, model_width)
    qkv = jnp.dot(attn_in, qkv_matrix, preferred_element_type=jnp.float32).reshape(
        map_count, piece_rows, 3, local_width
    )
    query = (qkv[:, :, 0] + query_bias).reshape(head_shape)
    key_raw = qkv[:, :, 1].reshape(head_shape)
    value_low = (qkv[:, :, 2] + value_bias).astype(jnp.bfloat16).reshape(head_shape)
    query_unit, query_back = jax.vjp(unit_scaled, query, head_scale)
    key_unit, key_back = jax.vjp(unit_plain, key_raw)
    query_low = query_unit.astype(jnp.bfloat16)
    key_low = key_unit.astype(jnp.bfloat16)
    group_heads = heads_here // ctx_count
    group_shape = (map_count, piece_rows, ctx_count, group_heads, head_dim)
    query_all = group_send(query_low.reshape(group_shape))
    keys_all = group_send(key_low.reshape(group_shape))
    values_all = group_send(value_low.reshape(group_shape))
    scale_ends = jnp.cumsum(scale_len, axis=1)
    owners = (ctx_index - jnp.arange(ctx_count, dtype=jnp.int32)) % ctx_count
    token_pos = owners[:, None] * piece_rows + jnp.arange(piece_rows, dtype=jnp.int32)[None, :]
    ends = scale_ends[:, None, None, :]
    visible_end = jnp.min(jnp.where(ends > token_pos[None, :, :, None], ends, map_length), axis=3)
    key_mask = token_pos[None, None, None, :, :] < visible_end[:, :, :, None, None]

    def masked_scores():
        raw_scores = jnp.einsum(
            "amqgd,bmkgd->mgaqbk", query_all, keys_all, preferred_element_type=jnp.float32
        )
        return jnp.where(key_mask[:, None], raw_scores, -1e30)

    scores = masked_scores()
    row_max = jnp.max(scores, axis=(-2, -1), keepdims=True)
    exp_scores = jnp.exp(scores - row_max)
    exp_total = jnp.sum(exp_scores, axis=(-2, -1), keepdims=True)
    log_total = row_max + jnp.log(exp_total)
    probs_low = (exp_scores / exp_total).astype(jnp.bfloat16)
    out_all = jnp.einsum(
        "mgaqbk,bmkgd->amqgd", probs_low, values_all, preferred_element_type=jnp.float32
    ).astype(jnp.bfloat16)
    heads_out = group_return(out_all).reshape(row_count, local_width)
    attn_partial = jnp.dot(heads_out, full_proj, preferred_element_type=jnp.float32)
    attn_branch = tp_sum(attn_partial).reshape(map_count, piece_rows, model_width) + proj_bias
    attn_part = gamma_one[:, None] * attn_branch
    mid_stream = stream_in + attn_part
    second_mod, second_back = jax.vjp(modulate, mid_stream, scale_two, shift_two)
    mlp_in = second_mod.astype(jnp.bfloat16).reshape(row_count, model_width)
    pre_act = jnp.dot(mlp_in, full_up, preferred_element_type=jnp.float32) + up_bias
    activation, gelu_back = jax.vjp(gelu_tanh, pre_act)
    act_low = activation.astype(jnp.bfloat16)
    mlp_partial = jnp.dot(act_low, full_down, preferred_element_type=jnp.float32)
    mlp_branch = tp_sum(mlp_partial).reshape(map_count, piece_rows, model_width) + down_bias
    mlp_part = gamma_two[:, None] * mlp_branch
    stream = mid_stream + mlp_part
    grad_top = out_grad.astype(jnp.float32)
    d_gamma_two = jnp.sum(grad_top * mlp_branch, axis=1)
    d_mlp = gamma_two[:, None] * grad_top
    d_down_bias = jnp.sum(d_mlp, axis=(0, 1))
    d_mlp_low = d_mlp.astype(jnp.bfloat16).reshape(row_count, model_width)
    g_down = jnp.einsum("rf,rd->fd", act_low, d_mlp_low, preferred_element_type=jnp.float32)
    down_low, d_mlp_low = lax.optimization_barrier((g_down.astype(jnp.bfloat16), d_mlp_low))
    d_act = jnp.einsum("rd,fd->rf", d_mlp_low, full_down, preferred_element_type=jnp.float32)
    (d_pre,) = gelu_back(d_act)
    d_up_bias = jnp.sum(d_pre, axis=0)
    d_pre_low = d_pre.astype(jnp.bfloat16)
    g_up = jnp.einsum("rd,rf->df", mlp_in, d_pre_low, preferred_element_type=jnp.float32)
    up_low, d_pre_low = lax.optimization_barrier((g_up.astype(jnp.bfloat16), d_pre_low))
    d_mlp_in_part = jnp.einsum("rf,df->rd", d_pre_low, full_up, preferred_element_type=jnp.float32)
    d_mlp_in = tp_sum(d_mlp_in_part).reshape(map_count, piece_rows, model_width)
    d_mid, d_scale_two, d_shift_two = second_back(d_mlp_in)
    d_mid = d_mid + grad_top
    d_gamma_one = jnp.sum(d_mid * attn_branch, axis=1)
    d_attn = gamma_one[:, None] * d_mid
    d_proj_bias = jnp.sum(d_attn, axis=(0, 1))
    d_attn_low = d_attn.astype(jnp.bfloat16).reshape(row_count, model_width)
    g_proj = jnp.einsum("ri,rd->id", heads_out, d_attn_low, preferred_element_type=jnp.float32)
    proj_low, d_attn_low = lax.optimization_barrier((g_proj.astype(jnp.bfloat16), d_attn_low))
    d_heads = jnp.einsum("rd,id->ri", d_attn_low, full_proj, preferred_element_type=jnp.float32)
    d_heads = d_heads.astype(jnp.bfloat16).reshape(head_shape)
    d_heads_all = group_send(d_heads.reshape(group_shape))
    probs = probs_low.astype(jnp.float32)
    d_probs = jnp.einsum(
        "amqgd,bmkgd->mgaqbk", d_heads_all, values_all, preferred_element_type=jnp.float32
    )
    row_delta = jnp.sum(probs * d_probs, axis=(-2, -1), keepdims=True)
    d_scores = (probs * (d_probs - row_delta)).astype(jnp.bfloat16)
    probs_again = probs_low
    d_query_all = jnp.einsum(
        "mgaqbk,bmkgd->amqgd", d_scores, keys_all, preferred_element_type=jnp.float32
    ).astype(jnp.bfloat16)
    d_key_all = jnp.einsum(
        "mgaqbk,amqgd->bmkgd", d_scores, query_all, preferred_element_type=jnp.float32
    ).astype(jnp.bfloat16)
    d_value_all = jnp.einsum(
        "mgaqbk,amqgd->bmkgd", probs_again, d_heads_all, preferred_element_type=jnp.float32
    ).astype(jnp.bfloat16)
    d_query_unit = group_return(d_query_all).reshape(head_shape).astype(jnp.float32)
    d_key_unit = group_return(d_key_all).reshape(head_shape).astype(jnp.float32)
    d_value = group_return(d_value_all).reshape(head_shape).astype(jnp.float32)
    d_query, d_head_scale = query_back(d_query_unit)
    (d_key,) = key_back(d_key_unit)
    d_query = d_query.reshape(map_count, piece_rows, local_width)
    d_key = d_key.reshape(map_count, piece_rows, local_width)
    d_value = d_value.reshape(map_count, piece_rows, local_width)
    d_query_bias = jnp.sum(d_query, axis=(0, 1))
    d_value_bias = jnp.sum(d_value, axis=(0, 1))
    d_qkv = (
        jnp.stack([d_query, d_key, d_value], axis=2)
        .astype(jnp.bfloat16)
        .reshape(row_count, 3 * local_width)
    )
    g_qkv = jnp.einsum("rd,rc->dc", attn_in, d_qkv, preferred_element_type=jnp.float32).reshape(
        model_width, 3, local_width
    )
    d_attn_in_part = jnp.einsum("rc,dc->rd", d_qkv, qkv_matrix, preferred_element_type=jnp.float32)
    d_attn_in = tp_sum(d_attn_in_part).reshape(map_count, piece_rows, model_width)
    d_input, d_scale_one, d_shift_one = first_back(d_attn_in)
    d_input = d_input + d_mid
    d_mod_part = jnp.stack(
        [d_gamma_one, d_gamma_two, d_scale_one, d_scale_two, d_shift_one, d_shift_two], axis=1
    )
    d_mod = lax.psum(d_mod_part, "ctx").astype(jnp.bfloat16).reshape(map_count, 6 * model_width)
    d_mod_all = lax.all_gather(d_mod, "shard", axis=0, tiled=True)
    g_ada = jnp.einsum(
        "md,mc->dc", cond_cols, d_mod_all, preferred_element_type=jnp.float32
    ).reshape(ada_rows, 6, model_width)
    d_ada_bias = jnp.sum(d_mod_all.astype(jnp.float32), axis=0).reshape(6, model_width)
    d_cond_cols = jnp.einsum("mc,dc->md", d_mod_all, ada_local, preferred_element_type=jnp.float32)
    d_cond_in = lax.all_to_all(d_cond_cols, "shard", 0, 1, tiled=True)
    _, silu_back = jax.vjp(jax.nn.silu, cond_wide)
    (d_cond,) = silu_back(d_cond_in)
    up_shard = lax.psum_scatter(up_low, "shard", scatter_dimension=0, tiled=True)
    proj_shard = lax.psum_scatter(proj_low, "shard", scatter_dimension=1, tiled=True)
    down_shard = lax.psum_scatter(down_low, "shard", scatter_dimension=1, tiled=True)
    early_shards = (up_shard, proj_shard, down_shard)
    early_summed = lax.psum(early_shards, "ctx")
    qkv_low, early_summed = lax.optimization_barrier((g_qkv.astype(jnp.bfloat16), early_summed))
    qkv_shard = lax.psum_scatter(qkv_low, "shard", scatter_dimension=0, tiled=True)
    qkv_summed = lax.psum(qkv_shard, "ctx")
    summed = tuple(
        g.astype(jnp.float32) for g in (qkv_summed, early_summed[0], early_summed[1], early_summed[2])
    )
    square_sums = jnp.stack(
        [jnp.sum(stream * stream), jnp.sum(attn_part * attn_part), jnp.sum(mlp_part * mlp_part)]
    )
    small_parts = (
        square_sums,
        d_query_bias,
        d_value_bias,
        d_head_scale,
        d_proj_bias,
        d_up_bias,
        d_down_bias,
    )
    small_flat = small_sum(jnp.concatenate(small_parts))
    small = []
    offset = 0
    for part in small_parts:
        small.append(small_flat[offset:offset + part.shape[0]])
        offset += part.shape[0]
    entry_total = map_count * map_length * model_width * lax.axis_size("shard")
    norm_stats = jnp.sqrt(small[0] / entry_total)
    return (
        stream.astype(jnp.bfloat16),
        d_input.astype(jnp.bfloat16),
        d_cond,
        g_ada,
        d_ada_bias,
        summed[0],
        small[1],
        small[2],
        small[3],
        summed[2],
        small[4],
        summed[1],
        small[5],
        summed[3],
        small[6],
        norm_stats,
    )


def solution(mesh):
    in_specs = (
        P("shard", "ctx", None),
        P("shard", None),
        P("shard", None),
        P("shard", None, None),
        P(),
        P("shard", None, "tp"),
        P("tp"),
        P("tp"),
        P("tp"),
        P("tp", "shard"),
        P(),
        P("shard", "tp"),
        P("tp"),
        P("tp", "shard"),
        P(),
        P("shard", "ctx", None),
    )
    out_specs = (
        P("shard", "ctx", None),
        P("shard", "ctx", None),
        P("shard", None),
        P("shard", None, None),
        P(),
        P("shard", None, "tp"),
        P("tp"),
        P("tp"),
        P("tp"),
        P("tp", "shard"),
        P(),
        P("shard", "tp"),
        P("tp"),
        P("tp", "shard"),
        P(),
        P(),
    )
    return jax.shard_map(block, mesh=mesh, in_specs=in_specs, out_specs=out_specs, check_vma=False)
```

```python
import jax
import jax.numpy as jnp
from jax import lax
from jax.sharding import PartitionSpec as P


def layer_norm(values):
    center = values - jnp.mean(values, axis=-1, keepdims=True)
    spread = jnp.mean(center * center, axis=-1, keepdims=True)
    return center * lax.rsqrt(spread + 1e-06)


def modulate(values, scale, shift):
    return layer_norm(values) * (1.0 + scale[:, None, :]) + shift[:, None, :]


def unit_scaled(values, gains):
    normed = values * lax.rsqrt(jnp.sum(values * values, axis=-1, keepdims=True) + 1e-06)
    return normed * jnp.exp(gains)[None, None, :, None]


def unit_plain(values):
    return values * lax.rsqrt(jnp.sum(values * values, axis=-1, keepdims=True) + 1e-06)


def gelu_tanh(values):
    return jax.nn.gelu(values, approximate=True)


def tp_sum(values):
    count = lax.axis_size("tp")
    if count != 2:
        return lax.psum(values, "tp")
    return values + lax.ppermute(values, "tp", [(0, 1), (1, 0)])


def ctx_shifts(values):
    count = lax.axis_size("ctx")
    parts = [values]
    for shift in range(1, count):
        pairs = [(i, (i + shift) % count) for i in range(count)]
        parts.append(lax.ppermute(values, "ctx", pairs))
    return jnp.stack(parts)


def ctx_return(parts):
    count = lax.axis_size("ctx")
    total = parts[0].astype(jnp.float32)
    for shift in range(1, count):
        pairs = [(i, (i - shift) % count) for i in range(count)]
        total = total + lax.ppermute(parts[shift], "ctx", pairs).astype(jnp.float32)
    return total


def group_send(values):
    count = lax.axis_size("ctx")
    me = lax.axis_index("ctx")
    parts = []
    for shift in range(count):
        block = lax.dynamic_index_in_dim(values, (me + shift) % count, axis=2, keepdims=False)
        if shift:
            pairs = [(i, (i + shift) % count) for i in range(count)]
            block = lax.ppermute(block, "ctx", pairs)
        parts.append(block)
    return jnp.stack(parts)


def group_return(parts):
    count = lax.axis_size("ctx")
    me = lax.axis_index("ctx")
    back = [parts[0]]
    for shift in range(1, count):
        pairs = [(i, (i - shift) % count) for i in range(count)]
        back.append(lax.ppermute(parts[shift], "ctx", pairs))
    stacked = jnp.stack(back)
    order = (jnp.arange(count, dtype=jnp.int32) - me) % count
    return jnp.moveaxis(jnp.take(stacked, order, axis=0), 0, 2)


def gather_axis(values, axis):
    count = lax.axis_size(axis)
    me = lax.axis_index(axis)
    parts = [values]
    for shift in range(1, count):
        pairs = [(i, (i + shift) % count) for i in range(count)]
        parts.append(lax.ppermute(values, axis, pairs))
    stacked = jnp.stack(parts)
    order = (me - jnp.arange(count, dtype=jnp.int32)) % count
    return jnp.take(stacked, order, axis=0)


def small_sum(values):
    every = gather_axis(gather_axis(values, "ctx"), "shard")
    return jnp.sum(every, axis=(0, 1))


def body(
    hidden_in,
    cond,
    scale_len,
    ada_weight,
    ada_bias,
    qkv_weight,
    query_bias,
    value_bias,
    head_scale,
    proj_weight,
    proj_bias,
    up_weight,
    up_bias,
    down_weight,
    down_bias,
    out_grad,
):
    map_count = hidden_in.shape[0]
    piece_rows = hidden_in.shape[1]
    model_width = hidden_in.shape[2]
    ctx_count = lax.axis_size("ctx")
    ctx_index = lax.axis_index("ctx")
    shard_index = lax.axis_index("shard")
    map_length = piece_rows * ctx_count
    heads_here = head_scale.shape[0]
    local_width = query_bias.shape[0]
    head_dim = local_width // heads_here
    row_count = map_count * piece_rows
    head_shape = (map_count, piece_rows, heads_here, head_dim)
    ada_rows = ada_weight.shape[0]
    shard_count = lax.axis_size("shard")
    full_qkv = lax.all_gather(qkv_weight, "shard", axis=0, tiled=True)
    full_proj = lax.all_gather(proj_weight, "shard", axis=1, tiled=True)
    full_up = lax.all_gather(up_weight, "shard", axis=0, tiled=True)
    full_down = lax.all_gather(down_weight, "shard", axis=1, tiled=True)
    qkv_matrix = full_qkv.reshape(model_width, 3 * local_width)

    cond_wide = cond.astype(jnp.float32)
    cond_all = lax.all_gather(cond, "shard", axis=0, tiled=True).astype(jnp.float32)
    cond_in_all = jax.nn.silu(cond_all).astype(jnp.bfloat16)
    cond_cols = lax.dynamic_slice_in_dim(cond_in_all, shard_index * ada_rows, ada_rows, axis=1)
    ada_local = ada_weight.reshape(ada_rows, 6 * model_width)
    mod_partial = jnp.dot(cond_cols, ada_local, preferred_element_type=jnp.float32)
    modulation = lax.psum_scatter(mod_partial, "shard", scatter_dimension=0, tiled=True)
    modulation = modulation.reshape(map_count, 6, model_width) + ada_bias[None]
    gamma_one = modulation[:, 0]
    gamma_two = modulation[:, 1]
    scale_one = modulation[:, 2]
    scale_two = modulation[:, 3]
    shift_one = modulation[:, 4]
    shift_two = modulation[:, 5]
    stream_in = hidden_in.astype(jnp.float32)
    first_mod, first_back = jax.vjp(modulate, stream_in, scale_one, shift_one)
    attn_in = first_mod.astype(jnp.bfloat16).reshape(row_count, model_width)
    qkv = jnp.dot(attn_in, qkv_matrix, preferred_element_type=jnp.float32).reshape(
        map_count, piece_rows, 3, local_width
    )
    query = (qkv[:, :, 0] + query_bias).reshape(head_shape)
    key_raw = qkv[:, :, 1].reshape(head_shape)
    value_low = (qkv[:, :, 2] + value_bias).astype(jnp.bfloat16).reshape(head_shape)
    query_unit, query_back = jax.vjp(unit_scaled, query, head_scale)
    key_unit, key_back = jax.vjp(unit_plain, key_raw)
    query_low = query_unit.astype(jnp.bfloat16)
    key_low = key_unit.astype(jnp.bfloat16)
    group_heads = heads_here // ctx_count
    group_shape = (map_count, piece_rows, ctx_count, group_heads, head_dim)
    query_all = group_send(query_low.reshape(group_shape))
    keys_all = group_send(key_low.reshape(group_shape))
    values_all = group_send(value_low.reshape(group_shape))
    scale_ends = jnp.cumsum(scale_len, axis=1)
    owners = (ctx_index - jnp.arange(ctx_count, dtype=jnp.int32)) % ctx_count
    token_pos = owners[:, None] * piece_rows + jnp.arange(piece_rows, dtype=jnp.int32)[None, :]
    ends = scale_ends[:, None, None, :]
    visible_end = jnp.min(jnp.where(ends > token_pos[None, :, :, None], ends, map_length), axis=3)
    key_mask = token_pos[None, None, None, :, :] < visible_end[:, :, :, None, None]

    def masked_scores():
        raw_scores = jnp.einsum(
            "amqgd,bmkgd->mgaqbk", query_all, keys_all, preferred_element_type=jnp.float32
        )
        return jnp.where(key_mask[:, None], raw_scores, -1e30)

    scores = masked_scores()
    row_max = jnp.max(scores, axis=(-2, -1), keepdims=True)
    exp_scores = jnp.exp(scores - row_max)
    exp_total = jnp.sum(exp_scores, axis=(-2, -1), keepdims=True)
    log_total = row_max + jnp.log(exp_total)
    probs_low = (exp_scores / exp_total).astype(jnp.bfloat16)
    out_all = jnp.einsum(
        "mgaqbk,bmkgd->amqgd", probs_low, values_all, preferred_element_type=jnp.float32
    ).astype(jnp.bfloat16)
    heads_out = group_return(out_all).reshape(row_count, local_width)
    attn_partial = jnp.dot(heads_out, full_proj, preferred_element_type=jnp.float32)
    attn_branch = tp_sum(attn_partial).reshape(map_count, piece_rows, model_width) + proj_bias
    attn_part = gamma_one[:, None] * attn_branch
    mid_stream = stream_in + attn_part
    second_mod, second_back = jax.vjp(modulate, mid_stream, scale_two, shift_two)
    mlp_in = second_mod.astype(jnp.bfloat16).reshape(row_count, model_width)
    pre_act = jnp.dot(mlp_in, full_up, preferred_element_type=jnp.float32) + up_bias
    activation, gelu_back = jax.vjp(gelu_tanh, pre_act)
    act_low = activation.astype(jnp.bfloat16)
    mlp_partial = jnp.dot(act_low, full_down, preferred_element_type=jnp.float32)
    mlp_branch = tp_sum(mlp_partial).reshape(map_count, piece_rows, model_width) + down_bias
    mlp_part = gamma_two[:, None] * mlp_branch
    stream = mid_stream + mlp_part
    grad_top = out_grad.astype(jnp.float32)
    d_gamma_two = jnp.sum(grad_top * mlp_branch, axis=1)
    d_mlp = gamma_two[:, None] * grad_top
    d_down_bias = jnp.sum(d_mlp, axis=(0, 1))
    d_mlp_low = d_mlp.astype(jnp.bfloat16).reshape(row_count, model_width)
    g_down = jnp.einsum("rf,rd->fd", act_low, d_mlp_low, preferred_element_type=jnp.float32)
    d_act = jnp.einsum("rd,fd->rf", d_mlp_low, full_down, preferred_element_type=jnp.float32)
    (d_pre,) = gelu_back(d_act)
    d_up_bias = jnp.sum(d_pre, axis=0)
    d_pre_low = d_pre.astype(jnp.bfloat16)
    g_up = jnp.einsum("rd,rf->df", mlp_in, d_pre_low, preferred_element_type=jnp.float32)
    d_mlp_in_part = jnp.einsum("rf,df->rd", d_pre_low, full_up, preferred_element_type=jnp.float32)
    d_mlp_in = tp_sum(d_mlp_in_part).reshape(map_count, piece_rows, model_width)
    d_mid, d_scale_two, d_shift_two = second_back(d_mlp_in)
    d_mid = d_mid + grad_top
    d_gamma_one = jnp.sum(d_mid * attn_branch, axis=1)
    d_attn = gamma_one[:, None] * d_mid
    d_proj_bias = jnp.sum(d_attn, axis=(0, 1))
    d_attn_low = d_attn.astype(jnp.bfloat16).reshape(row_count, model_width)
    g_proj = jnp.einsum("ri,rd->id", heads_out, d_attn_low, preferred_element_type=jnp.float32)
    d_heads = jnp.einsum("rd,id->ri", d_attn_low, full_proj, preferred_element_type=jnp.float32)
    d_heads = d_heads.astype(jnp.bfloat16).reshape(head_shape)
    d_heads_all = group_send(d_heads.reshape(group_shape))
    probs = probs_low.astype(jnp.float32)
    d_probs = jnp.einsum(
        "amqgd,bmkgd->mgaqbk", d_heads_all, values_all, preferred_element_type=jnp.float32
    )
    row_delta = jnp.sum(probs * d_probs, axis=(-2, -1), keepdims=True)
    d_scores = (probs * (d_probs - row_delta)).astype(jnp.bfloat16)
    probs_again = probs_low
    d_query_all = jnp.einsum(
        "mgaqbk,bmkgd->amqgd", d_scores, keys_all, preferred_element_type=jnp.float32
    ).astype(jnp.bfloat16)
    d_key_all = jnp.einsum(
        "mgaqbk,amqgd->bmkgd", d_scores, query_all, preferred_element_type=jnp.float32
    ).astype(jnp.bfloat16)
    d_value_all = jnp.einsum(
        "mgaqbk,amqgd->bmkgd", probs_again, d_heads_all, preferred_element_type=jnp.float32
    ).astype(jnp.bfloat16)
    d_query_unit = group_return(d_query_all).reshape(head_shape).astype(jnp.float32)
    d_key_unit = group_return(d_key_all).reshape(head_shape).astype(jnp.float32)
    d_value = group_return(d_value_all).reshape(head_shape).astype(jnp.float32)
    d_query, d_head_scale = query_back(d_query_unit)
    (d_key,) = key_back(d_key_unit)
    d_query = d_query.reshape(map_count, piece_rows, local_width)
    d_key = d_key.reshape(map_count, piece_rows, local_width)
    d_value = d_value.reshape(map_count, piece_rows, local_width)
    d_query_bias = jnp.sum(d_query, axis=(0, 1))
    d_value_bias = jnp.sum(d_value, axis=(0, 1))
    d_qkv = (
        jnp.stack([d_query, d_key, d_value], axis=2)
        .astype(jnp.bfloat16)
        .reshape(row_count, 3 * local_width)
    )
    g_qkv = jnp.einsum("rd,rc->dc", attn_in, d_qkv, preferred_element_type=jnp.float32).reshape(
        model_width, 3, local_width
    )
    d_attn_in_part = jnp.einsum("rc,dc->rd", d_qkv, qkv_matrix, preferred_element_type=jnp.float32)
    d_attn_in = tp_sum(d_attn_in_part).reshape(map_count, piece_rows, model_width)
    d_input, d_scale_one, d_shift_one = first_back(d_attn_in)
    d_input = d_input + d_mid
    d_mod_part = jnp.stack(
        [d_gamma_one, d_gamma_two, d_scale_one, d_scale_two, d_shift_one, d_shift_two], axis=1
    )
    d_mod = lax.psum(d_mod_part, "ctx").astype(jnp.bfloat16).reshape(map_count, 6 * model_width)
    d_mod_all = lax.all_gather(d_mod, "shard", axis=0, tiled=True)
    g_ada = jnp.einsum(
        "md,mc->dc", cond_cols, d_mod_all, preferred_element_type=jnp.float32
    ).reshape(ada_rows, 6, model_width)
    d_ada_bias = jnp.sum(d_mod_all.astype(jnp.float32), axis=0).reshape(6, model_width)
    d_cond_cols = jnp.einsum("mc,dc->md", d_mod_all, ada_local, preferred_element_type=jnp.float32)
    d_cond_in = lax.all_to_all(d_cond_cols, "shard", 0, 1, tiled=True)
    silu_value, silu_back = jax.vjp(jax.nn.silu, cond_wide)
    (d_cond,) = silu_back(d_cond_in)
    early_shards = (
        lax.psum_scatter(
            g_up.astype(jnp.bfloat16), "shard", scatter_dimension=0, tiled=True
        ),
        lax.psum_scatter(
            g_proj.astype(jnp.bfloat16), "shard", scatter_dimension=1, tiled=True
        ),
        lax.psum_scatter(
            g_down.astype(jnp.bfloat16), "shard", scatter_dimension=1, tiled=True
        ),
    )
    early_summed = lax.psum(early_shards, "ctx")
    qkv_low, early_summed = lax.optimization_barrier((g_qkv.astype(jnp.bfloat16), early_summed))
    qkv_shard = lax.psum_scatter(qkv_low, "shard", scatter_dimension=0, tiled=True)
    qkv_summed = lax.psum(qkv_shard, "ctx")
    summed = tuple(
        g.astype(jnp.float32) for g in (qkv_summed, early_summed[0], early_summed[1], early_summed[2])
    )
    square_sums = jnp.stack(
        [jnp.sum(stream * stream), jnp.sum(attn_part * attn_part), jnp.sum(mlp_part * mlp_part)]
    )
    small_parts = (
        square_sums,
        d_query_bias,
        d_value_bias,
        d_head_scale,
        d_proj_bias,
        d_up_bias,
        d_down_bias,
    )
    small_flat = small_sum(jnp.concatenate(small_parts))
    small = []
    offset = 0
    for part in small_parts:
        small.append(small_flat[offset:offset + part.shape[0]])
        offset += part.shape[0]
    entry_total = map_count * map_length * model_width * lax.axis_size("shard")
    norm_stats = jnp.sqrt(small[0] / entry_total)
    return (
        stream.astype(jnp.bfloat16),
        d_input.astype(jnp.bfloat16),
        d_cond,
        g_ada,
        d_ada_bias,
        summed[0],
        small[1],
        small[2],
        small[3],
        summed[2],
        small[4],
        summed[1],
        small[5],
        summed[3],
        small[6],
        norm_stats,
    )


def solution(mesh):
    in_specs = (
        P("shard", "ctx", None),
        P("shard", None),
        P("shard", None),
        P("shard", None, None),
        P(),
        P("shard", None, "tp"),
        P("tp"),
        P("tp"),
        P("tp"),
        P("tp", "shard"),
        P(),
        P("shard", "tp"),
        P("tp"),
        P("tp", "shard"),
        P(),
        P("shard", "ctx", None),
    )
    out_specs = (
        P("shard", "ctx", None),
        P("shard", "ctx", None),
        P("shard", None),
        P("shard", None, None),
        P(),
        P("shard", None, "tp"),
        P("tp"),
        P("tp"),
        P("tp"),
        P("tp", "shard"),
        P(),
        P("shard", "tp"),
        P("tp"),
        P("tp", "shard"),
        P(),
        P(),
    )
    return jax.shard_map(body, mesh=mesh, in_specs=in_specs, out_specs=out_specs, check_vma=False)
```

```python
import jax
import jax.numpy as jnp
from jax import lax
from jax.sharding import PartitionSpec as P


def layer_norm(values):
    center = values - jnp.mean(values, axis=-1, keepdims=True)
    spread = jnp.mean(center * center, axis=-1, keepdims=True)
    return center * lax.rsqrt(spread + 1e-06)


def modulate(values, scale, shift):
    return layer_norm(values) * (1.0 + scale[:, None, :]) + shift[:, None, :]


def unit_scaled(values, gains):
    normed = values * lax.rsqrt(jnp.sum(values * values, axis=-1, keepdims=True) + 1e-06)
    return normed * jnp.exp(gains)[None, None, :, None]


def unit_plain(values):
    return values * lax.rsqrt(jnp.sum(values * values, axis=-1, keepdims=True) + 1e-06)


def gelu_tanh(values):
    return jax.nn.gelu(values, approximate=True)


def tp_sum(values):
    count = lax.axis_size("tp")
    if count != 2:
        return lax.psum(values, "tp")
    return values + lax.ppermute(values, "tp", [(0, 1), (1, 0)])


def ctx_shifts(values):
    count = lax.axis_size("ctx")
    parts = [values]
    for shift in range(1, count):
        pairs = [(i, (i + shift) % count) for i in range(count)]
        parts.append(lax.ppermute(values, "ctx", pairs))
    return jnp.stack(parts)


def ctx_return(parts):
    count = lax.axis_size("ctx")
    total = parts[0].astype(jnp.float32)
    for shift in range(1, count):
        pairs = [(i, (i - shift) % count) for i in range(count)]
        total = total + lax.ppermute(parts[shift], "ctx", pairs).astype(jnp.float32)
    return total


def group_send(values):
    count = lax.axis_size("ctx")
    me = lax.axis_index("ctx")
    parts = []
    for shift in range(count):
        block = lax.dynamic_index_in_dim(values, (me + shift) % count, axis=2, keepdims=False)
        if shift:
            pairs = [(i, (i + shift) % count) for i in range(count)]
            block = lax.ppermute(block, "ctx", pairs)
        parts.append(block)
    return jnp.stack(parts)


def group_return(parts):
    count = lax.axis_size("ctx")
    me = lax.axis_index("ctx")
    back = [parts[0]]
    for shift in range(1, count):
        pairs = [(i, (i - shift) % count) for i in range(count)]
        back.append(lax.ppermute(parts[shift], "ctx", pairs))
    stacked = jnp.stack(back)
    order = (jnp.arange(count, dtype=jnp.int32) - me) % count
    return jnp.moveaxis(jnp.take(stacked, order, axis=0), 0, 2)


def ctx_total(grad):
    count = lax.axis_size("ctx")
    me = lax.axis_index("ctx")
    chunks = grad.reshape(count, -1)
    own = lax.dynamic_index_in_dim(chunks, me, axis=0, keepdims=False).astype(jnp.float32)
    for shift in range(1, count):
        pairs = [(i, (i + shift) % count) for i in range(count)]
        block = lax.dynamic_index_in_dim(chunks, (me + shift) % count, axis=0, keepdims=False)
        own = own + lax.ppermute(block, "ctx", pairs).astype(jnp.float32)
    return gather_axis(own.astype(jnp.bfloat16), "ctx").reshape(grad.shape)


def gather_axis(values, axis):
    count = lax.axis_size(axis)
    me = lax.axis_index(axis)
    parts = [values]
    for shift in range(1, count):
        pairs = [(i, (i + shift) % count) for i in range(count)]
        parts.append(lax.ppermute(values, axis, pairs))
    stacked = jnp.stack(parts)
    order = (me - jnp.arange(count, dtype=jnp.int32)) % count
    return jnp.take(stacked, order, axis=0)


def small_sum(values):
    every = gather_axis(gather_axis(values, "ctx"), "shard")
    return jnp.sum(every, axis=(0, 1))


def body(
    hidden_in,
    cond,
    scale_len,
    ada_weight,
    ada_bias,
    qkv_weight,
    query_bias,
    value_bias,
    head_scale,
    proj_weight,
    proj_bias,
    up_weight,
    up_bias,
    down_weight,
    down_bias,
    out_grad,
):
    map_count = hidden_in.shape[0]
    piece_rows = hidden_in.shape[1]
    model_width = hidden_in.shape[2]
    ctx_count = lax.axis_size("ctx")
    ctx_index = lax.axis_index("ctx")
    shard_index = lax.axis_index("shard")
    map_length = piece_rows * ctx_count
    heads_here = head_scale.shape[0]
    local_width = query_bias.shape[0]
    head_dim = local_width // heads_here
    row_count = map_count * piece_rows
    head_shape = (map_count, piece_rows, heads_here, head_dim)
    ada_rows = ada_weight.shape[0]
    shard_count = lax.axis_size("shard")
    full_qkv = lax.all_gather(qkv_weight, "shard", axis=0, tiled=True)
    full_proj = lax.all_gather(proj_weight, "shard", axis=1, tiled=True)
    full_up = lax.all_gather(up_weight, "shard", axis=0, tiled=True)
    full_down = lax.all_gather(down_weight, "shard", axis=1, tiled=True)
    qkv_matrix = full_qkv.reshape(model_width, 3 * local_width)

    cond_wide = cond.astype(jnp.float32)
    cond_all = lax.all_gather(cond, "shard", axis=0, tiled=True).astype(jnp.float32)
    cond_in_all = jax.nn.silu(cond_all).astype(jnp.bfloat16)
    cond_cols = lax.dynamic_slice_in_dim(cond_in_all, shard_index * ada_rows, ada_rows, axis=1)
    ada_local = ada_weight.reshape(ada_rows, 6 * model_width)
    mod_partial = jnp.dot(cond_cols, ada_local, preferred_element_type=jnp.float32)
    modulation = lax.psum_scatter(mod_partial, "shard", scatter_dimension=0, tiled=True)
    modulation = modulation.reshape(map_count, 6, model_width) + ada_bias[None]
    gamma_one = modulation[:, 0]
    gamma_two = modulation[:, 1]
    scale_one = modulation[:, 2]
    scale_two = modulation[:, 3]
    shift_one = modulation[:, 4]
    shift_two = modulation[:, 5]
    stream_in = hidden_in.astype(jnp.float32)
    first_mod, first_back = jax.vjp(modulate, stream_in, scale_one, shift_one)
    attn_in = first_mod.astype(jnp.bfloat16).reshape(row_count, model_width)
    qkv = jnp.dot(attn_in, qkv_matrix, preferred_element_type=jnp.float32).reshape(
        map_count, piece_rows, 3, local_width
    )
    query = (qkv[:, :, 0] + query_bias).reshape(head_shape)
    key_raw = qkv[:, :, 1].reshape(head_shape)
    value_low = (qkv[:, :, 2] + value_bias).astype(jnp.bfloat16).reshape(head_shape)
    query_unit, query_back = jax.vjp(unit_scaled, query, head_scale)
    key_unit, key_back = jax.vjp(unit_plain, key_raw)
    query_low = query_unit.astype(jnp.bfloat16)
    key_low = key_unit.astype(jnp.bfloat16)
    group_heads = heads_here // ctx_count
    group_shape = (map_count, piece_rows, ctx_count, group_heads, head_dim)
    query_all = group_send(query_low.reshape(group_shape))
    keys_all = group_send(key_low.reshape(group_shape))
    values_all = group_send(value_low.reshape(group_shape))
    scale_ends = jnp.cumsum(scale_len, axis=1)
    owners = (ctx_index - jnp.arange(ctx_count, dtype=jnp.int32)) % ctx_count
    token_pos = owners[:, None] * piece_rows + jnp.arange(piece_rows, dtype=jnp.int32)[None, :]
    ends = scale_ends[:, None, None, :]
    visible_end = jnp.min(jnp.where(ends > token_pos[None, :, :, None], ends, map_length), axis=3)
    key_mask = token_pos[None, None, None, :, :] < visible_end[:, :, :, None, None]

    def masked_scores():
        raw_scores = jnp.einsum(
            "amqgd,bmkgd->mgaqbk", query_all, keys_all, preferred_element_type=jnp.float32
        )
        return jnp.where(key_mask[:, None], raw_scores, -1e30)

    scores = masked_scores()
    row_max = jnp.max(scores, axis=(-2, -1), keepdims=True)
    exp_scores = jnp.exp(scores - row_max)
    exp_total = jnp.sum(exp_scores, axis=(-2, -1), keepdims=True)
    log_total = row_max + jnp.log(exp_total)
    probs_low = (exp_scores / exp_total).astype(jnp.bfloat16)
    out_all = jnp.einsum(
        "mgaqbk,bmkgd->amqgd", probs_low, values_all, preferred_element_type=jnp.float32
    ).astype(jnp.bfloat16)
    heads_out = group_return(out_all).reshape(row_count, local_width)
    attn_partial = jnp.dot(heads_out, full_proj, preferred_element_type=jnp.float32)
    attn_branch = tp_sum(attn_partial).reshape(map_count, piece_rows, model_width) + proj_bias
    attn_part = gamma_one[:, None] * attn_branch
    mid_stream = stream_in + attn_part
    second_mod, second_back = jax.vjp(modulate, mid_stream, scale_two, shift_two)
    mlp_in = second_mod.astype(jnp.bfloat16).reshape(row_count, model_width)
    pre_act = jnp.dot(mlp_in, full_up, preferred_element_type=jnp.float32) + up_bias
    activation, gelu_back = jax.vjp(gelu_tanh, pre_act)
    act_low = activation.astype(jnp.bfloat16)
    mlp_partial = jnp.dot(act_low, full_down, preferred_element_type=jnp.float32)
    mlp_branch = tp_sum(mlp_partial).reshape(map_count, piece_rows, model_width) + down_bias
    mlp_part = gamma_two[:, None] * mlp_branch
    stream = mid_stream + mlp_part
    grad_top = out_grad.astype(jnp.float32)
    d_gamma_two = jnp.sum(grad_top * mlp_branch, axis=1)
    d_mlp = gamma_two[:, None] * grad_top
    d_down_bias = jnp.sum(d_mlp, axis=(0, 1))
    d_mlp_low = d_mlp.astype(jnp.bfloat16).reshape(row_count, model_width)
    g_down = jnp.einsum("rf,rd->fd", act_low, d_mlp_low, preferred_element_type=jnp.float32)
    d_act = jnp.einsum("rd,fd->rf", d_mlp_low, full_down, preferred_element_type=jnp.float32)
    (d_pre,) = gelu_back(d_act)
    d_up_bias = jnp.sum(d_pre, axis=0)
    d_pre_low = d_pre.astype(jnp.bfloat16)
    g_up = jnp.einsum("rd,rf->df", mlp_in, d_pre_low, preferred_element_type=jnp.float32)
    d_mlp_in_part = jnp.einsum("rf,df->rd", d_pre_low, full_up, preferred_element_type=jnp.float32)
    d_mlp_in = tp_sum(d_mlp_in_part).reshape(map_count, piece_rows, model_width)
    d_mid, d_scale_two, d_shift_two = second_back(d_mlp_in)
    d_mid = d_mid + grad_top
    d_gamma_one = jnp.sum(d_mid * attn_branch, axis=1)
    d_attn = gamma_one[:, None] * d_mid
    d_proj_bias = jnp.sum(d_attn, axis=(0, 1))
    d_attn_low = d_attn.astype(jnp.bfloat16).reshape(row_count, model_width)
    g_proj = jnp.einsum("ri,rd->id", heads_out, d_attn_low, preferred_element_type=jnp.float32)
    d_heads = jnp.einsum("rd,id->ri", d_attn_low, full_proj, preferred_element_type=jnp.float32)
    d_heads = d_heads.astype(jnp.bfloat16).reshape(head_shape)
    d_heads_all = group_send(d_heads.reshape(group_shape))
    probs = probs_low.astype(jnp.float32)
    d_probs = jnp.einsum(
        "amqgd,bmkgd->mgaqbk", d_heads_all, values_all, preferred_element_type=jnp.float32
    )
    row_delta = jnp.sum(probs * d_probs, axis=(-2, -1), keepdims=True)
    d_scores = (probs * (d_probs - row_delta)).astype(jnp.bfloat16)
    probs_again = probs_low
    d_query_all = jnp.einsum(
        "mgaqbk,bmkgd->amqgd", d_scores, keys_all, preferred_element_type=jnp.float32
    ).astype(jnp.bfloat16)
    d_key_all = jnp.einsum(
        "mgaqbk,amqgd->bmkgd", d_scores, query_all, preferred_element_type=jnp.float32
    ).astype(jnp.bfloat16)
    d_value_all = jnp.einsum(
        "mgaqbk,amqgd->bmkgd", probs_again, d_heads_all, preferred_element_type=jnp.float32
    ).astype(jnp.bfloat16)
    d_query_unit = group_return(d_query_all).reshape(head_shape).astype(jnp.float32)
    d_key_unit = group_return(d_key_all).reshape(head_shape).astype(jnp.float32)
    d_value = group_return(d_value_all).reshape(head_shape).astype(jnp.float32)
    d_query, d_head_scale = query_back(d_query_unit)
    (d_key,) = key_back(d_key_unit)
    d_query = d_query.reshape(map_count, piece_rows, local_width)
    d_key = d_key.reshape(map_count, piece_rows, local_width)
    d_value = d_value.reshape(map_count, piece_rows, local_width)
    d_query_bias = jnp.sum(d_query, axis=(0, 1))
    d_value_bias = jnp.sum(d_value, axis=(0, 1))
    d_qkv = (
        jnp.stack([d_query, d_key, d_value], axis=2)
        .astype(jnp.bfloat16)
        .reshape(row_count, 3 * local_width)
    )
    g_qkv = jnp.einsum("rd,rc->dc", attn_in, d_qkv, preferred_element_type=jnp.float32).reshape(
        model_width, 3, local_width
    )
    d_attn_in_part = jnp.einsum("rc,dc->rd", d_qkv, qkv_matrix, preferred_element_type=jnp.float32)
    d_attn_in = tp_sum(d_attn_in_part).reshape(map_count, piece_rows, model_width)
    d_input, d_scale_one, d_shift_one = first_back(d_attn_in)
    d_input = d_input + d_mid
    d_mod_part = jnp.stack(
        [d_gamma_one, d_gamma_two, d_scale_one, d_scale_two, d_shift_one, d_shift_two], axis=1
    )
    d_mod = lax.psum(d_mod_part, "ctx").astype(jnp.bfloat16).reshape(map_count, 6 * model_width)
    d_mod_all = lax.all_gather(d_mod, "shard", axis=0, tiled=True)
    g_ada = jnp.einsum(
        "md,mc->dc", cond_cols, d_mod_all, preferred_element_type=jnp.float32
    ).reshape(ada_rows, 6, model_width)
    d_ada_bias = jnp.sum(d_mod_all.astype(jnp.float32), axis=0).reshape(6, model_width)
    d_cond_cols = jnp.einsum("mc,dc->md", d_mod_all, ada_local, preferred_element_type=jnp.float32)
    d_cond_in = lax.all_to_all(d_cond_cols, "shard", 0, 1, tiled=True)
    silu_value, silu_back = jax.vjp(jax.nn.silu, cond_wide)
    (d_cond,) = silu_back(d_cond_in)
    early_shards = (
        lax.psum_scatter(
            g_up.astype(jnp.bfloat16), "shard", scatter_dimension=0, tiled=True
        ),
        lax.psum_scatter(
            g_proj.astype(jnp.bfloat16), "shard", scatter_dimension=1, tiled=True
        ),
        lax.psum_scatter(
            g_down.astype(jnp.bfloat16), "shard", scatter_dimension=1, tiled=True
        ),
    )
    early_flat = ctx_total(jnp.concatenate([g.reshape(-1) for g in early_shards]))
    early_summed = []
    offset = 0
    for g in early_shards:
        early_summed.append(early_flat[offset:offset + g.size].reshape(g.shape))
        offset += g.size
    qkv_shard = lax.psum_scatter(g_qkv.astype(jnp.bfloat16), "shard", scatter_dimension=0, tiled=True)
    qkv_summed = lax.psum(qkv_shard, "ctx")
    summed = tuple(
        g.astype(jnp.float32) for g in (qkv_summed, early_summed[0], early_summed[1], early_summed[2])
    )
    square_sums = jnp.stack(
        [jnp.sum(stream * stream), jnp.sum(attn_part * attn_part), jnp.sum(mlp_part * mlp_part)]
    )
    small_parts = (
        square_sums,
        d_query_bias,
        d_value_bias,
        d_head_scale,
        d_proj_bias,
        d_up_bias,
        d_down_bias,
    )
    small_flat = small_sum(jnp.concatenate(small_parts))
    small = []
    offset = 0
    for part in small_parts:
        small.append(small_flat[offset:offset + part.shape[0]])
        offset += part.shape[0]
    entry_total = map_count * map_length * model_width * lax.axis_size("shard")
    norm_stats = jnp.sqrt(small[0] / entry_total)
    return (
        stream.astype(jnp.bfloat16),
        d_input.astype(jnp.bfloat16),
        d_cond,
        g_ada,
        d_ada_bias,
        summed[0],
        small[1],
        small[2],
        small[3],
        summed[2],
        small[4],
        summed[1],
        small[5],
        summed[3],
        small[6],
        norm_stats,
    )


def solution(mesh):
    in_specs = (
        P("shard", "ctx", None),
        P("shard", None),
        P("shard", None),
        P("shard", None, None),
        P(),
        P("shard", None, "tp"),
        P("tp"),
        P("tp"),
        P("tp"),
        P("tp", "shard"),
        P(),
        P("shard", "tp"),
        P("tp"),
        P("tp", "shard"),
        P(),
        P("shard", "ctx", None),
    )
    out_specs = (
        P("shard", "ctx", None),
        P("shard", "ctx", None),
        P("shard", None),
        P("shard", None, None),
        P(),
        P("shard", None, "tp"),
        P("tp"),
        P("tp"),
        P("tp"),
        P("tp", "shard"),
        P(),
        P("shard", "tp"),
        P("tp"),
        P("tp", "shard"),
        P(),
        P(),
    )
    return jax.shard_map(body, mesh=mesh, in_specs=in_specs, out_specs=out_specs, check_vma=False)
```

```python
import jax
import jax.numpy as jnp
from jax import lax
from jax.sharding import PartitionSpec as P


def layer_norm(values):
    center = values - jnp.mean(values, axis=-1, keepdims=True)
    spread = jnp.mean(center * center, axis=-1, keepdims=True)
    return center * lax.rsqrt(spread + 1e-06)


def modulate(values, scale, shift):
    return layer_norm(values) * (1.0 + scale[:, None, :]) + shift[:, None, :]


def unit_scaled(values, gains):
    normed = values * lax.rsqrt(jnp.sum(values * values, axis=-1, keepdims=True) + 1e-06)
    return normed * jnp.exp(gains)[None, None, :, None]


def unit_plain(values):
    return values * lax.rsqrt(jnp.sum(values * values, axis=-1, keepdims=True) + 1e-06)


def gelu_tanh(values):
    return jax.nn.gelu(values, approximate=True)


def tp_sum(values):
    count = lax.axis_size("tp")
    if count != 2:
        return lax.psum(values, "tp")
    return values + lax.ppermute(values, "tp", [(0, 1), (1, 0)])


def ctx_shifts(values):
    count = lax.axis_size("ctx")
    parts = [values]
    for shift in range(1, count):
        pairs = [(i, (i + shift) % count) for i in range(count)]
        parts.append(lax.ppermute(values, "ctx", pairs))
    return jnp.stack(parts)


def ctx_return(parts):
    count = lax.axis_size("ctx")
    total = parts[0].astype(jnp.float32)
    for shift in range(1, count):
        pairs = [(i, (i - shift) % count) for i in range(count)]
        total = total + lax.ppermute(parts[shift], "ctx", pairs).astype(jnp.float32)
    return total


def group_send(values):
    count = lax.axis_size("ctx")
    me = lax.axis_index("ctx")
    parts = []
    for shift in range(count):
        block = lax.dynamic_index_in_dim(values, (me + shift) % count, axis=2, keepdims=False)
        if shift:
            pairs = [(i, (i + shift) % count) for i in range(count)]
            block = lax.ppermute(block, "ctx", pairs)
        parts.append(block)
    return jnp.stack(parts)


def group_return(parts):
    count = lax.axis_size("ctx")
    me = lax.axis_index("ctx")
    back = [parts[0]]
    for shift in range(1, count):
        pairs = [(i, (i - shift) % count) for i in range(count)]
        back.append(lax.ppermute(parts[shift], "ctx", pairs))
    stacked = jnp.stack(back)
    order = (jnp.arange(count, dtype=jnp.int32) - me) % count
    return jnp.moveaxis(jnp.take(stacked, order, axis=0), 0, 2)


def gather_axis(values, axis):
    count = lax.axis_size(axis)
    me = lax.axis_index(axis)
    parts = [values]
    for shift in range(1, count):
        pairs = [(i, (i + shift) % count) for i in range(count)]
        parts.append(lax.ppermute(values, axis, pairs))
    stacked = jnp.stack(parts)
    order = (me - jnp.arange(count, dtype=jnp.int32)) % count
    return jnp.take(stacked, order, axis=0)


def small_sum(values):
    every = gather_axis(gather_axis(values, "ctx"), "shard")
    return jnp.sum(every, axis=(0, 1))


def body(
    hidden_in,
    cond,
    scale_len,
    ada_weight,
    ada_bias,
    qkv_weight,
    query_bias,
    value_bias,
    head_scale,
    proj_weight,
    proj_bias,
    up_weight,
    up_bias,
    down_weight,
    down_bias,
    out_grad,
):
    map_count = hidden_in.shape[0]
    piece_rows = hidden_in.shape[1]
    model_width = hidden_in.shape[2]
    ctx_count = lax.axis_size("ctx")
    ctx_index = lax.axis_index("ctx")
    shard_index = lax.axis_index("shard")
    map_length = piece_rows * ctx_count
    heads_here = head_scale.shape[0]
    local_width = query_bias.shape[0]
    head_dim = local_width // heads_here
    row_count = map_count * piece_rows
    head_shape = (map_count, piece_rows, heads_here, head_dim)
    ada_rows = ada_weight.shape[0]
    shard_count = lax.axis_size("shard")
    full_qkv = lax.all_gather(qkv_weight, "shard", axis=0, tiled=True)
    full_proj = lax.all_gather(proj_weight, "shard", axis=1, tiled=True)
    full_up = lax.all_gather(up_weight, "shard", axis=0, tiled=True)
    full_down = lax.all_gather(down_weight, "shard", axis=1, tiled=True)
    qkv_matrix = full_qkv.reshape(model_width, 3 * local_width)

    cond_wide = cond.astype(jnp.float32)
    cond_all = lax.all_gather(cond, "shard", axis=0, tiled=True).astype(jnp.float32)
    cond_in_all = jax.nn.silu(cond_all).astype(jnp.bfloat16)
    cond_cols = lax.dynamic_slice_in_dim(cond_in_all, shard_index * ada_rows, ada_rows, axis=1)
    ada_local = ada_weight.reshape(ada_rows, 6 * model_width)
    mod_partial = jnp.dot(cond_cols, ada_local, preferred_element_type=jnp.float32)
    modulation = lax.psum_scatter(mod_partial, "shard", scatter_dimension=0, tiled=True)
    modulation = modulation.reshape(map_count, 6, model_width) + ada_bias[None]
    gamma_one = modulation[:, 0]
    gamma_two = modulation[:, 1]
    scale_one = modulation[:, 2]
    scale_two = modulation[:, 3]
    shift_one = modulation[:, 4]
    shift_two = modulation[:, 5]
    stream_in = hidden_in.astype(jnp.float32)
    first_mod, first_back = jax.vjp(modulate, stream_in, scale_one, shift_one)
    attn_in = first_mod.astype(jnp.bfloat16).reshape(row_count, model_width)
    qkv = jnp.dot(attn_in, qkv_matrix, preferred_element_type=jnp.float32).reshape(
        map_count, piece_rows, 3, local_width
    )
    query = (qkv[:, :, 0] + query_bias).reshape(head_shape)
    key_raw = qkv[:, :, 1].reshape(head_shape)
    value_low = (qkv[:, :, 2] + value_bias).astype(jnp.bfloat16).reshape(head_shape)
    query_unit, query_back = jax.vjp(unit_scaled, query, head_scale)
    key_unit, key_back = jax.vjp(unit_plain, key_raw)
    query_low = query_unit.astype(jnp.bfloat16)
    key_low = key_unit.astype(jnp.bfloat16)
    group_heads = heads_here // ctx_count
    group_shape = (map_count, piece_rows, ctx_count, group_heads, head_dim)
    query_all = group_send(query_low.reshape(group_shape))
    keys_all = group_send(key_low.reshape(group_shape))
    values_all = group_send(value_low.reshape(group_shape))
    scale_ends = jnp.cumsum(scale_len, axis=1)
    owners = (ctx_index - jnp.arange(ctx_count, dtype=jnp.int32)) % ctx_count
    token_pos = owners[:, None] * piece_rows + jnp.arange(piece_rows, dtype=jnp.int32)[None, :]
    ends = scale_ends[:, None, None, :]
    visible_end = jnp.min(jnp.where(ends > token_pos[None, :, :, None], ends, map_length), axis=3)
    key_mask = token_pos[None, None, None, :, :] < visible_end[:, :, :, None, None]

    def masked_scores():
        raw_scores = jnp.einsum(
            "amqgd,bmkgd->mgaqbk", query_all, keys_all, preferred_element_type=jnp.float32
        )
        return jnp.where(key_mask[:, None], raw_scores, -1e30)

    scores = masked_scores()
    row_max = jnp.max(scores, axis=(-2, -1), keepdims=True)
    exp_scores = jnp.exp(scores - row_max)
    exp_total = jnp.sum(exp_scores, axis=(-2, -1), keepdims=True)
    log_total = row_max + jnp.log(exp_total)
    probs_low = (exp_scores / exp_total).astype(jnp.bfloat16)
    out_all = jnp.einsum(
        "mgaqbk,bmkgd->amqgd", probs_low, values_all, preferred_element_type=jnp.float32
    ).astype(jnp.bfloat16)
    heads_out = group_return(out_all).reshape(row_count, local_width)
    attn_partial = jnp.dot(heads_out, full_proj, preferred_element_type=jnp.float32)
    attn_branch = tp_sum(attn_partial).reshape(map_count, piece_rows, model_width) + proj_bias
    attn_part = gamma_one[:, None] * attn_branch
    mid_stream = stream_in + attn_part
    second_mod, second_back = jax.vjp(modulate, mid_stream, scale_two, shift_two)
    mlp_in = second_mod.astype(jnp.bfloat16).reshape(row_count, model_width)
    pre_act = jnp.dot(mlp_in, full_up, preferred_element_type=jnp.float32) + up_bias
    activation, gelu_back = jax.vjp(gelu_tanh, pre_act)
    act_low = activation.astype(jnp.bfloat16)
    mlp_partial = jnp.dot(act_low, full_down, preferred_element_type=jnp.float32)
    mlp_branch = tp_sum(mlp_partial).reshape(map_count, piece_rows, model_width) + down_bias
    mlp_part = gamma_two[:, None] * mlp_branch
    stream = mid_stream + mlp_part
    grad_top = out_grad.astype(jnp.float32)
    d_gamma_two = jnp.sum(grad_top * mlp_branch, axis=1)
    d_mlp = gamma_two[:, None] * grad_top
    d_down_bias = jnp.sum(d_mlp, axis=(0, 1))
    d_mlp_low = d_mlp.astype(jnp.bfloat16).reshape(row_count, model_width)
    g_down = jnp.einsum("rf,rd->fd", act_low, d_mlp_low, preferred_element_type=jnp.float32)
    d_act = jnp.einsum("rd,fd->rf", d_mlp_low, full_down, preferred_element_type=jnp.float32)
    (d_pre,) = gelu_back(d_act)
    d_up_bias = jnp.sum(d_pre, axis=0)
    d_pre_low = d_pre.astype(jnp.bfloat16)
    g_up = jnp.einsum("rd,rf->df", mlp_in, d_pre_low, preferred_element_type=jnp.float32)
    d_mlp_in_part = jnp.einsum("rf,df->rd", d_pre_low, full_up, preferred_element_type=jnp.float32)
    d_mlp_in = tp_sum(d_mlp_in_part).reshape(map_count, piece_rows, model_width)
    d_mid, d_scale_two, d_shift_two = second_back(d_mlp_in)
    d_mid = d_mid + grad_top
    d_gamma_one = jnp.sum(d_mid * attn_branch, axis=1)
    d_attn = gamma_one[:, None] * d_mid
    d_proj_bias = jnp.sum(d_attn, axis=(0, 1))
    d_attn_low = d_attn.astype(jnp.bfloat16).reshape(row_count, model_width)
    g_proj = jnp.einsum("ri,rd->id", heads_out, d_attn_low, preferred_element_type=jnp.float32)
    d_heads = jnp.einsum("rd,id->ri", d_attn_low, full_proj, preferred_element_type=jnp.float32)
    d_heads = d_heads.astype(jnp.bfloat16).reshape(head_shape)
    d_heads_all = group_send(d_heads.reshape(group_shape))
    probs = probs_low.astype(jnp.float32)
    d_probs = jnp.einsum(
        "amqgd,bmkgd->mgaqbk", d_heads_all, values_all, preferred_element_type=jnp.float32
    )
    row_delta = jnp.sum(probs * d_probs, axis=(-2, -1), keepdims=True)
    d_scores = (probs * (d_probs - row_delta)).astype(jnp.bfloat16)
    probs_again = probs_low
    d_query_all = jnp.einsum(
        "mgaqbk,bmkgd->amqgd", d_scores, keys_all, preferred_element_type=jnp.float32
    ).astype(jnp.bfloat16)
    d_key_all = jnp.einsum(
        "mgaqbk,amqgd->bmkgd", d_scores, query_all, preferred_element_type=jnp.float32
    ).astype(jnp.bfloat16)
    d_value_all = jnp.einsum(
        "mgaqbk,amqgd->bmkgd", probs_again, d_heads_all, preferred_element_type=jnp.float32
    ).astype(jnp.bfloat16)
    d_query_unit = group_return(d_query_all).reshape(head_shape).astype(jnp.float32)
    d_key_unit = group_return(d_key_all).reshape(head_shape).astype(jnp.float32)
    d_value = group_return(d_value_all).reshape(head_shape).astype(jnp.float32)
    early_shards = (
        lax.psum_scatter(
            g_up.astype(jnp.bfloat16), "shard", scatter_dimension=0, tiled=True
        ),
        lax.psum_scatter(
            g_proj.astype(jnp.bfloat16), "shard", scatter_dimension=1, tiled=True
        ),
        lax.psum_scatter(
            g_down.astype(jnp.bfloat16), "shard", scatter_dimension=1, tiled=True
        ),
    )
    early_shards, d_query_unit = lax.optimization_barrier((early_shards, d_query_unit))
    d_query, d_head_scale = query_back(d_query_unit)
    (d_key,) = key_back(d_key_unit)
    d_query = d_query.reshape(map_count, piece_rows, local_width)
    d_key = d_key.reshape(map_count, piece_rows, local_width)
    d_value = d_value.reshape(map_count, piece_rows, local_width)
    d_query_bias = jnp.sum(d_query, axis=(0, 1))
    d_value_bias = jnp.sum(d_value, axis=(0, 1))
    d_qkv = (
        jnp.stack([d_query, d_key, d_value], axis=2)
        .astype(jnp.bfloat16)
        .reshape(row_count, 3 * local_width)
    )
    g_qkv = jnp.einsum("rd,rc->dc", attn_in, d_qkv, preferred_element_type=jnp.float32).reshape(
        model_width, 3, local_width
    )
    d_attn_in_part = jnp.einsum("rc,dc->rd", d_qkv, qkv_matrix, preferred_element_type=jnp.float32)
    d_attn_in = tp_sum(d_attn_in_part).reshape(map_count, piece_rows, model_width)
    d_input, d_scale_one, d_shift_one = first_back(d_attn_in)
    d_input = d_input + d_mid
    d_mod_part = jnp.stack(
        [d_gamma_one, d_gamma_two, d_scale_one, d_scale_two, d_shift_one, d_shift_two], axis=1
    )
    d_mod = lax.psum(d_mod_part, "ctx").astype(jnp.bfloat16).reshape(map_count, 6 * model_width)
    d_mod_all = lax.all_gather(d_mod, "shard", axis=0, tiled=True)
    g_ada = jnp.einsum(
        "md,mc->dc", cond_cols, d_mod_all, preferred_element_type=jnp.float32
    ).reshape(ada_rows, 6, model_width)
    d_ada_bias = jnp.sum(d_mod_all.astype(jnp.float32), axis=0).reshape(6, model_width)
    d_cond_cols = jnp.einsum("mc,dc->md", d_mod_all, ada_local, preferred_element_type=jnp.float32)
    d_cond_in = lax.all_to_all(d_cond_cols, "shard", 0, 1, tiled=True)
    silu_value, silu_back = jax.vjp(jax.nn.silu, cond_wide)
    (d_cond,) = silu_back(d_cond_in)
    early_summed = lax.psum(early_shards, "ctx")
    qkv_low, early_summed = lax.optimization_barrier((g_qkv.astype(jnp.bfloat16), early_summed))
    qkv_shard = lax.psum_scatter(qkv_low, "shard", scatter_dimension=0, tiled=True)
    qkv_summed = lax.psum(qkv_shard, "ctx")
    summed = tuple(
        g.astype(jnp.float32) for g in (qkv_summed, early_summed[0], early_summed[1], early_summed[2])
    )
    square_sums = jnp.stack(
        [jnp.sum(stream * stream), jnp.sum(attn_part * attn_part), jnp.sum(mlp_part * mlp_part)]
    )
    small_parts = (
        square_sums,
        d_query_bias,
        d_value_bias,
        d_head_scale,
        d_proj_bias,
        d_up_bias,
        d_down_bias,
    )
    small_flat = small_sum(jnp.concatenate(small_parts))
    small = []
    offset = 0
    for part in small_parts:
        small.append(small_flat[offset:offset + part.shape[0]])
        offset += part.shape[0]
    entry_total = map_count * map_length * model_width * lax.axis_size("shard")
    norm_stats = jnp.sqrt(small[0] / entry_total)
    return (
        stream.astype(jnp.bfloat16),
        d_input.astype(jnp.bfloat16),
        d_cond,
        g_ada,
        d_ada_bias,
        summed[0],
        small[1],
        small[2],
        small[3],
        summed[2],
        small[4],
        summed[1],
        small[5],
        summed[3],
        small[6],
        norm_stats,
    )


def solution(mesh):
    in_specs = (
        P("shard", "ctx", None),
        P("shard", None),
        P("shard", None),
        P("shard", None, None),
        P(),
        P("shard", None, "tp"),
        P("tp"),
        P("tp"),
        P("tp"),
        P("tp", "shard"),
        P(),
        P("shard", "tp"),
        P("tp"),
        P("tp", "shard"),
        P(),
        P("shard", "ctx", None),
    )
    out_specs = (
        P("shard", "ctx", None),
        P("shard", "ctx", None),
        P("shard", None),
        P("shard", None, None),
        P(),
        P("shard", None, "tp"),
        P("tp"),
        P("tp"),
        P("tp"),
        P("tp", "shard"),
        P(),
        P("shard", "tp"),
        P("tp"),
        P("tp", "shard"),
        P(),
        P(),
    )
    return jax.shard_map(body, mesh=mesh, in_specs=in_specs, out_specs=out_specs, check_vma=False)
```

```python
import jax
import jax.numpy as jnp
from jax import lax
from jax.sharding import PartitionSpec as P


def layer_norm(values):
    center = values - jnp.mean(values, axis=-1, keepdims=True)
    spread = jnp.mean(center * center, axis=-1, keepdims=True)
    return center * lax.rsqrt(spread + 1e-06)


def modulate(values, scale, shift):
    return layer_norm(values) * (1.0 + scale[:, None, :]) + shift[:, None, :]


def unit_scaled(values, gains):
    normed = values * lax.rsqrt(jnp.sum(values * values, axis=-1, keepdims=True) + 1e-06)
    return normed * jnp.exp(gains)[None, None, :, None]


def unit_plain(values):
    return values * lax.rsqrt(jnp.sum(values * values, axis=-1, keepdims=True) + 1e-06)


def gelu_tanh(values):
    return jax.nn.gelu(values, approximate=True)


def tp_sum(values):
    count = lax.axis_size("tp")
    if count != 2:
        return lax.psum(values, "tp")
    return values + lax.ppermute(values, "tp", [(0, 1), (1, 0)])


def ctx_shifts(values):
    count = lax.axis_size("ctx")
    parts = [values]
    for shift in range(1, count):
        pairs = [(i, (i + shift) % count) for i in range(count)]
        parts.append(lax.ppermute(values, "ctx", pairs))
    return jnp.stack(parts)


def ctx_return(parts):
    count = lax.axis_size("ctx")
    total = parts[0].astype(jnp.float32)
    for shift in range(1, count):
        pairs = [(i, (i - shift) % count) for i in range(count)]
        total = total + lax.ppermute(parts[shift], "ctx", pairs).astype(jnp.float32)
    return total


def group_send(values):
    count = lax.axis_size("ctx")
    me = lax.axis_index("ctx")
    parts = []
    for shift in range(count):
        block = lax.dynamic_index_in_dim(values, (me + shift) % count, axis=2, keepdims=False)
        if shift:
            pairs = [(i, (i + shift) % count) for i in range(count)]
            block = lax.ppermute(block, "ctx", pairs)
        parts.append(block)
    return jnp.stack(parts)


def group_return(parts):
    count = lax.axis_size("ctx")
    me = lax.axis_index("ctx")
    back = [parts[0]]
    for shift in range(1, count):
        pairs = [(i, (i - shift) % count) for i in range(count)]
        back.append(lax.ppermute(parts[shift], "ctx", pairs))
    stacked = jnp.stack(back)
    order = (jnp.arange(count, dtype=jnp.int32) - me) % count
    return jnp.moveaxis(jnp.take(stacked, order, axis=0), 0, 2)


def gather_axis(values, axis):
    count = lax.axis_size(axis)
    me = lax.axis_index(axis)
    parts = [values]
    for shift in range(1, count):
        pairs = [(i, (i + shift) % count) for i in range(count)]
        parts.append(lax.ppermute(values, axis, pairs))
    stacked = jnp.stack(parts)
    order = (me - jnp.arange(count, dtype=jnp.int32)) % count
    return jnp.take(stacked, order, axis=0)


def small_sum(values):
    every = gather_axis(gather_axis(values, "ctx"), "shard")
    return jnp.sum(every, axis=(0, 1))


def body(
    hidden_in,
    cond,
    scale_len,
    ada_weight,
    ada_bias,
    qkv_weight,
    query_bias,
    value_bias,
    head_scale,
    proj_weight,
    proj_bias,
    up_weight,
    up_bias,
    down_weight,
    down_bias,
    out_grad,
):
    map_count = hidden_in.shape[0]
    piece_rows = hidden_in.shape[1]
    model_width = hidden_in.shape[2]
    ctx_count = lax.axis_size("ctx")
    ctx_index = lax.axis_index("ctx")
    shard_index = lax.axis_index("shard")
    map_length = piece_rows * ctx_count
    heads_here = head_scale.shape[0]
    local_width = query_bias.shape[0]
    head_dim = local_width // heads_here
    row_count = map_count * piece_rows
    head_shape = (map_count, piece_rows, heads_here, head_dim)
    ada_rows = ada_weight.shape[0]
    shard_count = lax.axis_size("shard")
    full_qkv = lax.all_gather(qkv_weight, "shard", axis=0, tiled=True)
    full_proj = lax.all_gather(proj_weight, "shard", axis=1, tiled=True)
    full_up = lax.all_gather(up_weight, "shard", axis=0, tiled=True)
    full_down = lax.all_gather(down_weight, "shard", axis=1, tiled=True)
    qkv_matrix = full_qkv.reshape(model_width, 3 * local_width)

    cond_wide = cond.astype(jnp.float32)
    cond_all = lax.all_gather(cond, "shard", axis=0, tiled=True).astype(jnp.float32)
    cond_in_all = jax.nn.silu(cond_all).astype(jnp.bfloat16)
    cond_cols = lax.dynamic_slice_in_dim(cond_in_all, shard_index * ada_rows, ada_rows, axis=1)
    ada_local = ada_weight.reshape(ada_rows, 6 * model_width)
    mod_partial = jnp.dot(cond_cols, ada_local, preferred_element_type=jnp.float32)
    modulation = lax.psum_scatter(mod_partial, "shard", scatter_dimension=0, tiled=True)
    modulation = modulation.reshape(map_count, 6, model_width) + ada_bias[None]
    gamma_one = modulation[:, 0]
    gamma_two = modulation[:, 1]
    scale_one = modulation[:, 2]
    scale_two = modulation[:, 3]
    shift_one = modulation[:, 4]
    shift_two = modulation[:, 5]
    stream_in = hidden_in.astype(jnp.float32)
    first_mod, first_back = jax.vjp(modulate, stream_in, scale_one, shift_one)
    attn_in = first_mod.astype(jnp.bfloat16).reshape(row_count, model_width)
    qkv = jnp.dot(attn_in, qkv_matrix, preferred_element_type=jnp.float32).reshape(
        map_count, piece_rows, 3, local_width
    )
    query = (qkv[:, :, 0] + query_bias).reshape(head_shape)
    key_raw = qkv[:, :, 1].reshape(head_shape)
    value_low = (qkv[:, :, 2] + value_bias).astype(jnp.bfloat16).reshape(head_shape)
    query_unit, query_back = jax.vjp(unit_scaled, query, head_scale)
    key_unit, key_back = jax.vjp(unit_plain, key_raw)
    query_low = query_unit.astype(jnp.bfloat16)
    key_low = key_unit.astype(jnp.bfloat16)
    group_heads = heads_here // ctx_count
    group_shape = (map_count, piece_rows, ctx_count, group_heads, head_dim)
    query_all = group_send(query_low.reshape(group_shape))
    keys_all = group_send(key_low.reshape(group_shape))
    values_all = group_send(value_low.reshape(group_shape))
    scale_ends = jnp.cumsum(scale_len, axis=1)
    owners = (ctx_index - jnp.arange(ctx_count, dtype=jnp.int32)) % ctx_count
    token_pos = owners[:, None] * piece_rows + jnp.arange(piece_rows, dtype=jnp.int32)[None, :]
    ends = scale_ends[:, None, None, :]
    visible_end = jnp.min(jnp.where(ends > token_pos[None, :, :, None], ends, map_length), axis=3)
    key_mask = token_pos[None, None, None, :, :] < visible_end[:, :, :, None, None]

    def masked_scores():
        raw_scores = jnp.einsum(
            "amqgd,bmkgd->mgaqbk", query_all, keys_all, preferred_element_type=jnp.float32
        )
        return jnp.where(key_mask[:, None], raw_scores, -1e30)

    scores = masked_scores()
    row_max = jnp.max(scores, axis=(-2, -1), keepdims=True)
    exp_scores = jnp.exp(scores - row_max)
    exp_total = jnp.sum(exp_scores, axis=(-2, -1), keepdims=True)
    log_total = row_max + jnp.log(exp_total)
    probs_low = (exp_scores / exp_total).astype(jnp.bfloat16)
    out_all = jnp.einsum(
        "mgaqbk,bmkgd->amqgd", probs_low, values_all, preferred_element_type=jnp.float32
    ).astype(jnp.bfloat16)
    heads_out = group_return(out_all).reshape(row_count, local_width)
    attn_partial = jnp.dot(heads_out, full_proj, preferred_element_type=jnp.float32)
    attn_branch = tp_sum(attn_partial).reshape(map_count, piece_rows, model_width) + proj_bias
    attn_part = gamma_one[:, None] * attn_branch
    mid_stream = stream_in + attn_part
    second_mod, second_back = jax.vjp(modulate, mid_stream, scale_two, shift_two)
    mlp_in = second_mod.astype(jnp.bfloat16).reshape(row_count, model_width)
    pre_act = jnp.dot(mlp_in, full_up, preferred_element_type=jnp.float32) + up_bias
    activation, gelu_back = jax.vjp(gelu_tanh, pre_act)
    act_low = activation.astype(jnp.bfloat16)
    mlp_partial = jnp.dot(act_low, full_down, preferred_element_type=jnp.float32)
    mlp_branch = tp_sum(mlp_partial).reshape(map_count, piece_rows, model_width) + down_bias
    mlp_part = gamma_two[:, None] * mlp_branch
    stream = mid_stream + mlp_part
    grad_top = out_grad.astype(jnp.float32)
    d_gamma_two = jnp.sum(grad_top * mlp_branch, axis=1)
    d_mlp = gamma_two[:, None] * grad_top
    d_down_bias = jnp.sum(d_mlp, axis=(0, 1))
    d_mlp_low = d_mlp.astype(jnp.bfloat16).reshape(row_count, model_width)
    g_down = jnp.einsum("rf,rd->fd", act_low, d_mlp_low, preferred_element_type=jnp.float32)
    d_act = jnp.einsum("rd,fd->rf", d_mlp_low, full_down, preferred_element_type=jnp.float32)
    (d_pre,) = gelu_back(d_act)
    d_up_bias = jnp.sum(d_pre, axis=0)
    d_pre_low = d_pre.astype(jnp.bfloat16)
    g_up = jnp.einsum("rd,rf->df", mlp_in, d_pre_low, preferred_element_type=jnp.float32)
    d_mlp_in_part = jnp.einsum("rf,df->rd", d_pre_low, full_up, preferred_element_type=jnp.float32)
    d_mlp_in = tp_sum(d_mlp_in_part).reshape(map_count, piece_rows, model_width)
    d_mid, d_scale_two, d_shift_two = second_back(d_mlp_in)
    d_mid = d_mid + grad_top
    d_gamma_one = jnp.sum(d_mid * attn_branch, axis=1)
    d_attn = gamma_one[:, None] * d_mid
    d_proj_bias = jnp.sum(d_attn, axis=(0, 1))
    d_attn_low = d_attn.astype(jnp.bfloat16).reshape(row_count, model_width)
    g_proj = jnp.einsum("ri,rd->id", heads_out, d_attn_low, preferred_element_type=jnp.float32)
    d_heads = jnp.einsum("rd,id->ri", d_attn_low, full_proj, preferred_element_type=jnp.float32)
    d_heads = d_heads.astype(jnp.bfloat16).reshape(head_shape)
    d_heads_all = group_send(d_heads.reshape(group_shape))
    probs = probs_low.astype(jnp.float32)
    d_probs = jnp.einsum(
        "amqgd,bmkgd->mgaqbk", d_heads_all, values_all, preferred_element_type=jnp.float32
    )
    row_delta = jnp.sum(probs * d_probs, axis=(-2, -1), keepdims=True)
    d_scores = (probs * (d_probs - row_delta)).astype(jnp.bfloat16)
    probs_again = probs_low
    d_query_all = jnp.einsum(
        "mgaqbk,bmkgd->amqgd", d_scores, keys_all, preferred_element_type=jnp.float32
    ).astype(jnp.bfloat16)
    d_key_all = jnp.einsum(
        "mgaqbk,amqgd->bmkgd", d_scores, query_all, preferred_element_type=jnp.float32
    ).astype(jnp.bfloat16)
    d_value_all = jnp.einsum(
        "mgaqbk,amqgd->bmkgd", probs_again, d_heads_all, preferred_element_type=jnp.float32
    ).astype(jnp.bfloat16)
    d_query_unit = group_return(d_query_all).reshape(head_shape).astype(jnp.float32)
    d_key_unit = group_return(d_key_all).reshape(head_shape).astype(jnp.float32)
    d_value = group_return(d_value_all).reshape(head_shape).astype(jnp.float32)
    shard_count = lax.axis_size("shard")
    up_rows = g_up.astype(jnp.bfloat16).reshape(shard_count, -1)
    proj_rows = jnp.moveaxis(
        g_proj.astype(jnp.bfloat16).reshape(g_proj.shape[0], shard_count, -1), 1, 0
    ).reshape(shard_count, -1)
    down_rows = jnp.moveaxis(
        g_down.astype(jnp.bfloat16).reshape(g_down.shape[0], shard_count, -1), 1, 0
    ).reshape(shard_count, -1)
    early_rows = jnp.concatenate([up_rows, proj_rows, down_rows], axis=1)
    lanes = g_up.shape[1]
    early_flat = lax.psum_scatter(
        early_rows.reshape(-1, lanes), "shard", scatter_dimension=0, tiled=True
    )
    early_flat, d_query_unit = lax.optimization_barrier((early_flat, d_query_unit))
    d_query, d_head_scale = query_back(d_query_unit)
    (d_key,) = key_back(d_key_unit)
    d_query = d_query.reshape(map_count, piece_rows, local_width)
    d_key = d_key.reshape(map_count, piece_rows, local_width)
    d_value = d_value.reshape(map_count, piece_rows, local_width)
    d_query_bias = jnp.sum(d_query, axis=(0, 1))
    d_value_bias = jnp.sum(d_value, axis=(0, 1))
    d_qkv = (
        jnp.stack([d_query, d_key, d_value], axis=2)
        .astype(jnp.bfloat16)
        .reshape(row_count, 3 * local_width)
    )
    g_qkv = jnp.einsum("rd,rc->dc", attn_in, d_qkv, preferred_element_type=jnp.float32).reshape(
        model_width, 3, local_width
    )
    d_attn_in_part = jnp.einsum("rc,dc->rd", d_qkv, qkv_matrix, preferred_element_type=jnp.float32)
    d_attn_in = tp_sum(d_attn_in_part).reshape(map_count, piece_rows, model_width)
    d_input, d_scale_one, d_shift_one = first_back(d_attn_in)
    d_input = d_input + d_mid
    d_mod_part = jnp.stack(
        [d_gamma_one, d_gamma_two, d_scale_one, d_scale_two, d_shift_one, d_shift_two], axis=1
    )
    d_mod = lax.psum(d_mod_part, "ctx").astype(jnp.bfloat16).reshape(map_count, 6 * model_width)
    d_mod_all = lax.all_gather(d_mod, "shard", axis=0, tiled=True)
    g_ada = jnp.einsum(
        "md,mc->dc", cond_cols, d_mod_all, preferred_element_type=jnp.float32
    ).reshape(ada_rows, 6, model_width)
    d_ada_bias = jnp.sum(d_mod_all.astype(jnp.float32), axis=0).reshape(6, model_width)
    d_cond_cols = jnp.einsum("mc,dc->md", d_mod_all, ada_local, preferred_element_type=jnp.float32)
    d_cond_in = lax.all_to_all(d_cond_cols, "shard", 0, 1, tiled=True)
    silu_value, silu_back = jax.vjp(jax.nn.silu, cond_wide)
    (d_cond,) = silu_back(d_cond_in)
    early_flat = lax.psum(early_flat, "ctx").reshape(-1)
    up_size, proj_size = up_rows.shape[1], proj_rows.shape[1]
    early_summed = (
        early_flat[:up_size].reshape(g_up.shape[0] // shard_count, g_up.shape[1]),
        early_flat[up_size:up_size + proj_size].reshape(g_proj.shape[0], -1),
        early_flat[up_size + proj_size:].reshape(g_down.shape[0], -1),
    )
    qkv_low, early_summed = lax.optimization_barrier((g_qkv.astype(jnp.bfloat16), early_summed))
    qkv_shard = lax.psum_scatter(qkv_low, "shard", scatter_dimension=0, tiled=True)
    qkv_summed = lax.psum(qkv_shard, "ctx")
    summed = tuple(
        g.astype(jnp.float32) for g in (qkv_summed, early_summed[0], early_summed[1], early_summed[2])
    )
    square_sums = jnp.stack(
        [jnp.sum(stream * stream), jnp.sum(attn_part * attn_part), jnp.sum(mlp_part * mlp_part)]
    )
    small_parts = (
        square_sums,
        d_query_bias,
        d_value_bias,
        d_head_scale,
        d_proj_bias,
        d_up_bias,
        d_down_bias,
    )
    small_flat = small_sum(jnp.concatenate(small_parts))
    small = []
    offset = 0
    for part in small_parts:
        small.append(small_flat[offset:offset + part.shape[0]])
        offset += part.shape[0]
    entry_total = map_count * map_length * model_width * lax.axis_size("shard")
    norm_stats = jnp.sqrt(small[0] / entry_total)
    return (
        stream.astype(jnp.bfloat16),
        d_input.astype(jnp.bfloat16),
        d_cond,
        g_ada,
        d_ada_bias,
        summed[0],
        small[1],
        small[2],
        small[3],
        summed[2],
        small[4],
        summed[1],
        small[5],
        summed[3],
        small[6],
        norm_stats,
    )


def solution(mesh):
    in_specs = (
        P("shard", "ctx", None),
        P("shard", None),
        P("shard", None),
        P("shard", None, None),
        P(),
        P("shard", None, "tp"),
        P("tp"),
        P("tp"),
        P("tp"),
        P("tp", "shard"),
        P(),
        P("shard", "tp"),
        P("tp"),
        P("tp", "shard"),
        P(),
        P("shard", "ctx", None),
    )
    out_specs = (
        P("shard", "ctx", None),
        P("shard", "ctx", None),
        P("shard", None),
        P("shard", None, None),
        P(),
        P("shard", None, "tp"),
        P("tp"),
        P("tp"),
        P("tp"),
        P("tp", "shard"),
        P(),
        P("shard", "tp"),
        P("tp"),
        P("tp", "shard"),
        P(),
        P(),
    )
    return jax.shard_map(body, mesh=mesh, in_specs=in_specs, out_specs=out_specs, check_vma=False)
```

```python
import jax
import jax.numpy as jnp
from jax import lax
from jax.sharding import PartitionSpec as P


def layer_norm(values):
    center = values - jnp.mean(values, axis=-1, keepdims=True)
    spread = jnp.mean(center * center, axis=-1, keepdims=True)
    return center * lax.rsqrt(spread + 1e-06)


def modulate(values, scale, shift):
    return layer_norm(values) * (1.0 + scale[:, None, :]) + shift[:, None, :]


def unit_scaled(values, gains):
    normed = values * lax.rsqrt(jnp.sum(values * values, axis=-1, keepdims=True) + 1e-06)
    return normed * jnp.exp(gains)[None, None, :, None]


def unit_plain(values):
    return values * lax.rsqrt(jnp.sum(values * values, axis=-1, keepdims=True) + 1e-06)


def gelu_tanh(values):
    return jax.nn.gelu(values, approximate=True)


def tp_sum(values):
    count = lax.axis_size("tp")
    if count != 2:
        return lax.psum(values, "tp")
    return values + lax.ppermute(values, "tp", [(0, 1), (1, 0)])


def ctx_shifts(values):
    count = lax.axis_size("ctx")
    parts = [values]
    for shift in range(1, count):
        pairs = [(i, (i + shift) % count) for i in range(count)]
        parts.append(lax.ppermute(values, "ctx", pairs))
    return jnp.stack(parts)


def ctx_return(parts):
    count = lax.axis_size("ctx")
    total = parts[0].astype(jnp.float32)
    for shift in range(1, count):
        pairs = [(i, (i - shift) % count) for i in range(count)]
        total = total + lax.ppermute(parts[shift], "ctx", pairs).astype(jnp.float32)
    return total


def group_send(values):
    count = lax.axis_size("ctx")
    me = lax.axis_index("ctx")
    parts = []
    for shift in range(count):
        block = lax.dynamic_index_in_dim(values, (me + shift) % count, axis=2, keepdims=False)
        if shift:
            pairs = [(i, (i + shift) % count) for i in range(count)]
            block = lax.ppermute(block, "ctx", pairs)
        parts.append(block)
    return jnp.stack(parts)


def group_return(parts):
    count = lax.axis_size("ctx")
    me = lax.axis_index("ctx")
    back = [parts[0]]
    for shift in range(1, count):
        pairs = [(i, (i - shift) % count) for i in range(count)]
        back.append(lax.ppermute(parts[shift], "ctx", pairs))
    stacked = jnp.stack(back)
    order = (jnp.arange(count, dtype=jnp.int32) - me) % count
    return jnp.moveaxis(jnp.take(stacked, order, axis=0), 0, 2)


def gather_axis(values, axis):
    count = lax.axis_size(axis)
    me = lax.axis_index(axis)
    parts = [values]
    for shift in range(1, count):
        pairs = [(i, (i + shift) % count) for i in range(count)]
        parts.append(lax.ppermute(values, axis, pairs))
    stacked = jnp.stack(parts)
    order = (me - jnp.arange(count, dtype=jnp.int32)) % count
    return jnp.take(stacked, order, axis=0)


def small_sum(values):
    every = gather_axis(gather_axis(values, "ctx"), "shard")
    return jnp.sum(every, axis=(0, 1))


def body(
    hidden_in,
    cond,
    scale_len,
    ada_weight,
    ada_bias,
    qkv_weight,
    query_bias,
    value_bias,
    head_scale,
    proj_weight,
    proj_bias,
    up_weight,
    up_bias,
    down_weight,
    down_bias,
    out_grad,
):
    map_count = hidden_in.shape[0]
    piece_rows = hidden_in.shape[1]
    model_width = hidden_in.shape[2]
    ctx_count = lax.axis_size("ctx")
    ctx_index = lax.axis_index("ctx")
    shard_index = lax.axis_index("shard")
    map_length = piece_rows * ctx_count
    heads_here = head_scale.shape[0]
    local_width = query_bias.shape[0]
    head_dim = local_width // heads_here
    row_count = map_count * piece_rows
    head_shape = (map_count, piece_rows, heads_here, head_dim)
    ada_rows = ada_weight.shape[0]
    shard_count = lax.axis_size("shard")
    full_qkv = lax.all_gather(qkv_weight, "shard", axis=0, tiled=True)
    full_proj = lax.all_gather(proj_weight, "shard", axis=1, tiled=True)
    full_up = lax.all_gather(up_weight, "shard", axis=0, tiled=True)
    full_down = lax.all_gather(down_weight, "shard", axis=1, tiled=True)
    qkv_matrix = full_qkv.reshape(model_width, 3 * local_width)

    cond_wide = cond.astype(jnp.float32)
    cond_all = lax.all_gather(cond, "shard", axis=0, tiled=True).astype(jnp.float32)
    cond_in_all = jax.nn.silu(cond_all).astype(jnp.bfloat16)
    cond_cols = lax.dynamic_slice_in_dim(cond_in_all, shard_index * ada_rows, ada_rows, axis=1)
    ada_local = ada_weight.reshape(ada_rows, 6 * model_width)
    mod_partial = jnp.dot(cond_cols, ada_local, preferred_element_type=jnp.float32)
    modulation = lax.psum_scatter(mod_partial, "shard", scatter_dimension=0, tiled=True)
    modulation = modulation.reshape(map_count, 6, model_width) + ada_bias[None]
    gamma_one = modulation[:, 0]
    gamma_two = modulation[:, 1]
    scale_one = modulation[:, 2]
    scale_two = modulation[:, 3]
    shift_one = modulation[:, 4]
    shift_two = modulation[:, 5]
    stream_in = hidden_in.astype(jnp.float32)
    first_mod, first_back = jax.vjp(modulate, stream_in, scale_one, shift_one)
    attn_in = first_mod.astype(jnp.bfloat16).reshape(row_count, model_width)
    qkv = jnp.dot(attn_in, qkv_matrix, preferred_element_type=jnp.float32).reshape(
        map_count, piece_rows, 3, local_width
    )
    query = (qkv[:, :, 0] + query_bias).reshape(head_shape)
    key_raw = qkv[:, :, 1].reshape(head_shape)
    value_low = (qkv[:, :, 2] + value_bias).astype(jnp.bfloat16).reshape(head_shape)
    query_unit, query_back = jax.vjp(unit_scaled, query, head_scale)
    key_unit, key_back = jax.vjp(unit_plain, key_raw)
    query_low = query_unit.astype(jnp.bfloat16)
    key_low = key_unit.astype(jnp.bfloat16)
    group_heads = heads_here // ctx_count
    group_shape = (map_count, piece_rows, ctx_count, group_heads, head_dim)
    query_all = group_send(query_low.reshape(group_shape))
    keys_all = group_send(key_low.reshape(group_shape))
    values_all = group_send(value_low.reshape(group_shape))
    scale_ends = jnp.cumsum(scale_len, axis=1)
    owners = (ctx_index - jnp.arange(ctx_count, dtype=jnp.int32)) % ctx_count
    token_pos = owners[:, None] * piece_rows + jnp.arange(piece_rows, dtype=jnp.int32)[None, :]
    ends = scale_ends[:, None, None, :]
    visible_end = jnp.min(jnp.where(ends > token_pos[None, :, :, None], ends, map_length), axis=3)
    key_mask = token_pos[None, None, None, :, :] < visible_end[:, :, :, None, None]

    def masked_scores():
        raw_scores = jnp.einsum(
            "amqgd,bmkgd->mgaqbk", query_all, keys_all, preferred_element_type=jnp.float32
        )
        return jnp.where(key_mask[:, None], raw_scores, -1e30)

    scores = masked_scores()
    row_max = jnp.max(scores, axis=(-2, -1), keepdims=True)
    exp_scores = jnp.exp(scores - row_max)
    exp_total = jnp.sum(exp_scores, axis=(-2, -1), keepdims=True)
    log_total = row_max + jnp.log(exp_total)
    probs_low = (exp_scores / exp_total).astype(jnp.bfloat16)
    out_all = jnp.einsum(
        "mgaqbk,bmkgd->amqgd", probs_low, values_all, preferred_element_type=jnp.float32
    ).astype(jnp.bfloat16)
    heads_out = group_return(out_all).reshape(row_count, local_width)
    attn_partial = jnp.dot(heads_out, full_proj, preferred_element_type=jnp.float32)
    attn_branch = tp_sum(attn_partial).reshape(map_count, piece_rows, model_width) + proj_bias
    attn_part = gamma_one[:, None] * attn_branch
    mid_stream = stream_in + attn_part
    second_mod, second_back = jax.vjp(modulate, mid_stream, scale_two, shift_two)
    mlp_in = second_mod.astype(jnp.bfloat16).reshape(row_count, model_width)
    pre_act = jnp.dot(mlp_in, full_up, preferred_element_type=jnp.float32) + up_bias
    activation, gelu_back = jax.vjp(gelu_tanh, pre_act)
    act_low = activation.astype(jnp.bfloat16)
    mlp_partial = jnp.dot(act_low, full_down, preferred_element_type=jnp.float32)
    mlp_branch = tp_sum(mlp_partial).reshape(map_count, piece_rows, model_width) + down_bias
    mlp_part = gamma_two[:, None] * mlp_branch
    stream = mid_stream + mlp_part
    grad_top = out_grad.astype(jnp.float32)
    d_gamma_two = jnp.sum(grad_top * mlp_branch, axis=1)
    d_mlp = gamma_two[:, None] * grad_top
    d_down_bias = jnp.sum(d_mlp, axis=(0, 1))
    d_mlp_low = d_mlp.astype(jnp.bfloat16).reshape(row_count, model_width)
    g_down = jnp.einsum("rf,rd->fd", act_low, d_mlp_low, preferred_element_type=jnp.float32)
    d_act = jnp.einsum("rd,fd->rf", d_mlp_low, full_down, preferred_element_type=jnp.float32)
    (d_pre,) = gelu_back(d_act)
    d_up_bias = jnp.sum(d_pre, axis=0)
    d_pre_low = d_pre.astype(jnp.bfloat16)
    g_up = jnp.einsum("rd,rf->df", mlp_in, d_pre_low, preferred_element_type=jnp.float32)
    d_mlp_in_part = jnp.einsum("rf,df->rd", d_pre_low, full_up, preferred_element_type=jnp.float32)
    d_mlp_in = tp_sum(d_mlp_in_part).reshape(map_count, piece_rows, model_width)
    d_mid, d_scale_two, d_shift_two = second_back(d_mlp_in)
    d_mid = d_mid + grad_top
    d_gamma_one = jnp.sum(d_mid * attn_branch, axis=1)
    d_attn = gamma_one[:, None] * d_mid
    d_proj_bias = jnp.sum(d_attn, axis=(0, 1))
    d_attn_low = d_attn.astype(jnp.bfloat16).reshape(row_count, model_width)
    g_proj = jnp.einsum("ri,rd->id", heads_out, d_attn_low, preferred_element_type=jnp.float32)
    d_heads = jnp.einsum("rd,id->ri", d_attn_low, full_proj, preferred_element_type=jnp.float32)
    d_heads = d_heads.astype(jnp.bfloat16).reshape(head_shape)
    d_heads_all = group_send(d_heads.reshape(group_shape))
    probs = probs_low.astype(jnp.float32)
    d_probs = jnp.einsum(
        "amqgd,bmkgd->mgaqbk", d_heads_all, values_all, preferred_element_type=jnp.float32
    )
    row_delta = jnp.sum(probs * d_probs, axis=(-2, -1), keepdims=True)
    d_scores = (probs * (d_probs - row_delta)).astype(jnp.bfloat16)
    probs_again = probs_low
    d_query_all = jnp.einsum(
        "mgaqbk,bmkgd->amqgd", d_scores, keys_all, preferred_element_type=jnp.float32
    ).astype(jnp.bfloat16)
    d_key_all = jnp.einsum(
        "mgaqbk,amqgd->bmkgd", d_scores, query_all, preferred_element_type=jnp.float32
    ).astype(jnp.bfloat16)
    d_value_all = jnp.einsum(
        "mgaqbk,amqgd->bmkgd", probs_again, d_heads_all, preferred_element_type=jnp.float32
    ).astype(jnp.bfloat16)
    d_query_unit = group_return(d_query_all).reshape(head_shape).astype(jnp.float32)
    d_key_unit = group_return(d_key_all).reshape(head_shape).astype(jnp.float32)
    d_value = group_return(d_value_all).reshape(head_shape).astype(jnp.float32)
    early_shards = (
        lax.psum_scatter(
            g_up.astype(jnp.bfloat16), "shard", scatter_dimension=0, tiled=True
        ),
        lax.psum_scatter(
            g_proj.astype(jnp.bfloat16), "shard", scatter_dimension=1, tiled=True
        ),
        lax.psum_scatter(
            g_down.astype(jnp.bfloat16), "shard", scatter_dimension=1, tiled=True
        ),
    )
    early_shards, d_query_unit = lax.optimization_barrier((early_shards, d_query_unit))
    d_query, d_head_scale = query_back(d_query_unit)
    (d_key,) = key_back(d_key_unit)
    d_query = d_query.reshape(map_count, piece_rows, local_width)
    d_key = d_key.reshape(map_count, piece_rows, local_width)
    d_value = d_value.reshape(map_count, piece_rows, local_width)
    d_query_bias = jnp.sum(d_query, axis=(0, 1))
    d_value_bias = jnp.sum(d_value, axis=(0, 1))
    d_qkv = (
        jnp.stack([d_query, d_key, d_value], axis=2)
        .astype(jnp.bfloat16)
        .reshape(row_count, 3 * local_width)
    )
    g_qkv = jnp.einsum("rd,rc->dc", attn_in, d_qkv, preferred_element_type=jnp.float32).reshape(
        model_width, 3, local_width
    )
    early_summed = lax.psum(early_shards, "ctx")
    qkv_low, early_summed = lax.optimization_barrier((g_qkv.astype(jnp.bfloat16), early_summed))
    qkv_shard = lax.psum_scatter(qkv_low, "shard", scatter_dimension=0, tiled=True)
    d_attn_in_part = jnp.einsum("rc,dc->rd", d_qkv, qkv_matrix, preferred_element_type=jnp.float32)
    d_attn_in = tp_sum(d_attn_in_part).reshape(map_count, piece_rows, model_width)
    d_input, d_scale_one, d_shift_one = first_back(d_attn_in)
    d_input = d_input + d_mid
    d_mod_part = jnp.stack(
        [d_gamma_one, d_gamma_two, d_scale_one, d_scale_two, d_shift_one, d_shift_two], axis=1
    )
    d_mod = lax.psum(d_mod_part, "ctx").astype(jnp.bfloat16).reshape(map_count, 6 * model_width)
    qkv_shard, d_mod = lax.optimization_barrier((qkv_shard, d_mod))
    d_mod_all = lax.all_gather(d_mod, "shard", axis=0, tiled=True)
    g_ada = jnp.einsum(
        "md,mc->dc", cond_cols, d_mod_all, preferred_element_type=jnp.float32
    ).reshape(ada_rows, 6, model_width)
    d_ada_bias = jnp.sum(d_mod_all.astype(jnp.float32), axis=0).reshape(6, model_width)
    d_cond_cols = jnp.einsum("mc,dc->md", d_mod_all, ada_local, preferred_element_type=jnp.float32)
    d_cond_in = lax.all_to_all(d_cond_cols, "shard", 0, 1, tiled=True)
    silu_value, silu_back = jax.vjp(jax.nn.silu, cond_wide)
    (d_cond,) = silu_back(d_cond_in)
    qkv_summed = lax.psum(qkv_shard, "ctx")
    summed = tuple(
        g.astype(jnp.float32) for g in (qkv_summed, early_summed[0], early_summed[1], early_summed[2])
    )
    square_sums = jnp.stack(
        [jnp.sum(stream * stream), jnp.sum(attn_part * attn_part), jnp.sum(mlp_part * mlp_part)]
    )
    small_parts = (
        square_sums,
        d_query_bias,
        d_value_bias,
        d_head_scale,
        d_proj_bias,
        d_up_bias,
        d_down_bias,
    )
    small_flat = small_sum(jnp.concatenate(small_parts))
    small = []
    offset = 0
    for part in small_parts:
        small.append(small_flat[offset:offset + part.shape[0]])
        offset += part.shape[0]
    entry_total = map_count * map_length * model_width * lax.axis_size("shard")
    norm_stats = jnp.sqrt(small[0] / entry_total)
    return (
        stream.astype(jnp.bfloat16),
        d_input.astype(jnp.bfloat16),
        d_cond,
        g_ada,
        d_ada_bias,
        summed[0],
        small[1],
        small[2],
        small[3],
        summed[2],
        small[4],
        summed[1],
        small[5],
        summed[3],
        small[6],
        norm_stats,
    )


def solution(mesh):
    in_specs = (
        P("shard", "ctx", None),
        P("shard", None),
        P("shard", None),
        P("shard", None, None),
        P(),
        P("shard", None, "tp"),
        P("tp"),
        P("tp"),
        P("tp"),
        P("tp", "shard"),
        P(),
        P("shard", "tp"),
        P("tp"),
        P("tp", "shard"),
        P(),
        P("shard", "ctx", None),
    )
    out_specs = (
        P("shard", "ctx", None),
        P("shard", "ctx", None),
        P("shard", None),
        P("shard", None, None),
        P(),
        P("shard", None, "tp"),
        P("tp"),
        P("tp"),
        P("tp"),
        P("tp", "shard"),
        P(),
        P("shard", "tp"),
        P("tp"),
        P("tp", "shard"),
        P(),
        P(),
    )
    return jax.shard_map(body, mesh=mesh, in_specs=in_specs, out_specs=out_specs, check_vma=False)
```

```python
import jax
import jax.numpy as jnp
from jax import lax
from jax.sharding import PartitionSpec as P


def layer_norm(values):
    center = values - jnp.mean(values, axis=-1, keepdims=True)
    spread = jnp.mean(center * center, axis=-1, keepdims=True)
    return center * lax.rsqrt(spread + 1e-06)


def modulate(values, scale, shift):
    return layer_norm(values) * (1.0 + scale[:, None, :]) + shift[:, None, :]


def unit_scaled(values, gains):
    normed = values * lax.rsqrt(jnp.sum(values * values, axis=-1, keepdims=True) + 1e-06)
    return normed * jnp.exp(gains)[None, None, :, None]


def unit_plain(values):
    return values * lax.rsqrt(jnp.sum(values * values, axis=-1, keepdims=True) + 1e-06)


def gelu_tanh(values):
    return jax.nn.gelu(values, approximate=True)


def tp_sum(values):
    count = lax.axis_size("tp")
    if count != 2:
        return lax.psum(values, "tp")
    return values + lax.ppermute(values, "tp", [(0, 1), (1, 0)])


def ctx_shifts(values):
    count = lax.axis_size("ctx")
    parts = [values]
    for shift in range(1, count):
        pairs = [(i, (i + shift) % count) for i in range(count)]
        parts.append(lax.ppermute(values, "ctx", pairs))
    return jnp.stack(parts)


def ctx_return(parts):
    count = lax.axis_size("ctx")
    total = parts[0].astype(jnp.float32)
    for shift in range(1, count):
        pairs = [(i, (i - shift) % count) for i in range(count)]
        total = total + lax.ppermute(parts[shift], "ctx", pairs).astype(jnp.float32)
    return total


def group_send(values):
    count = lax.axis_size("ctx")
    me = lax.axis_index("ctx")
    parts = []
    for shift in range(count):
        block = lax.dynamic_index_in_dim(values, (me + shift) % count, axis=2, keepdims=False)
        if shift:
            pairs = [(i, (i + shift) % count) for i in range(count)]
            block = lax.ppermute(block, "ctx", pairs)
        parts.append(block)
    return jnp.stack(parts)


def group_return(parts):
    count = lax.axis_size("ctx")
    me = lax.axis_index("ctx")
    back = [parts[0]]
    for shift in range(1, count):
        pairs = [(i, (i - shift) % count) for i in range(count)]
        back.append(lax.ppermute(parts[shift], "ctx", pairs))
    stacked = jnp.stack(back)
    order = (jnp.arange(count, dtype=jnp.int32) - me) % count
    return jnp.moveaxis(jnp.take(stacked, order, axis=0), 0, 2)


def gather_axis(values, axis):
    count = lax.axis_size(axis)
    me = lax.axis_index(axis)
    parts = [values]
    for shift in range(1, count):
        pairs = [(i, (i + shift) % count) for i in range(count)]
        parts.append(lax.ppermute(values, axis, pairs))
    stacked = jnp.stack(parts)
    order = (me - jnp.arange(count, dtype=jnp.int32)) % count
    return jnp.take(stacked, order, axis=0)


def small_sum(values):
    every = gather_axis(gather_axis(values, "ctx"), "shard")
    return jnp.sum(every, axis=(0, 1))


def body(
    hidden_in,
    cond,
    scale_len,
    ada_weight,
    ada_bias,
    qkv_weight,
    query_bias,
    value_bias,
    head_scale,
    proj_weight,
    proj_bias,
    up_weight,
    up_bias,
    down_weight,
    down_bias,
    out_grad,
):
    map_count = hidden_in.shape[0]
    piece_rows = hidden_in.shape[1]
    model_width = hidden_in.shape[2]
    ctx_count = lax.axis_size("ctx")
    ctx_index = lax.axis_index("ctx")
    shard_index = lax.axis_index("shard")
    map_length = piece_rows * ctx_count
    heads_here = head_scale.shape[0]
    local_width = query_bias.shape[0]
    head_dim = local_width // heads_here
    row_count = map_count * piece_rows
    head_shape = (map_count, piece_rows, heads_here, head_dim)
    ada_rows = ada_weight.shape[0]
    shard_count = lax.axis_size("shard")
    full_qkv = lax.all_gather(qkv_weight, "shard", axis=0, tiled=True)
    full_proj = lax.all_gather(proj_weight, "shard", axis=1, tiled=True)
    full_up = lax.all_gather(up_weight, "shard", axis=0, tiled=True)
    full_down = lax.all_gather(down_weight, "shard", axis=1, tiled=True)
    qkv_matrix = full_qkv.reshape(model_width, 3 * local_width)

    cond_wide = cond.astype(jnp.float32)
    cond_all = lax.all_gather(cond, "shard", axis=0, tiled=True).astype(jnp.float32)
    cond_in_all = jax.nn.silu(cond_all).astype(jnp.bfloat16)
    cond_cols = lax.dynamic_slice_in_dim(cond_in_all, shard_index * ada_rows, ada_rows, axis=1)
    ada_local = ada_weight.reshape(ada_rows, 6 * model_width)
    mod_partial = jnp.dot(cond_cols, ada_local, preferred_element_type=jnp.float32)
    modulation = lax.psum_scatter(mod_partial, "shard", scatter_dimension=0, tiled=True)
    modulation = modulation.reshape(map_count, 6, model_width) + ada_bias[None]
    gamma_one = modulation[:, 0]
    gamma_two = modulation[:, 1]
    scale_one = modulation[:, 2]
    scale_two = modulation[:, 3]
    shift_one = modulation[:, 4]
    shift_two = modulation[:, 5]
    stream_in = hidden_in.astype(jnp.float32)
    first_mod, first_back = jax.vjp(modulate, stream_in, scale_one, shift_one)
    attn_in = first_mod.astype(jnp.bfloat16).reshape(row_count, model_width)
    qkv = jnp.dot(attn_in, qkv_matrix, preferred_element_type=jnp.float32).reshape(
        map_count, piece_rows, 3, local_width
    )
    query = (qkv[:, :, 0] + query_bias).reshape(head_shape)
    key_raw = qkv[:, :, 1].reshape(head_shape)
    value_low = (qkv[:, :, 2] + value_bias).astype(jnp.bfloat16).reshape(head_shape)
    query_unit, query_back = jax.vjp(unit_scaled, query, head_scale)
    key_unit, key_back = jax.vjp(unit_plain, key_raw)
    query_low = query_unit.astype(jnp.bfloat16)
    key_low = key_unit.astype(jnp.bfloat16)
    group_heads = heads_here // ctx_count
    group_shape = (map_count, piece_rows, ctx_count, group_heads, head_dim)
    query_all = group_send(query_low.reshape(group_shape))
    keys_all = group_send(key_low.reshape(group_shape))
    values_all = group_send(value_low.reshape(group_shape))
    scale_ends = jnp.cumsum(scale_len, axis=1)
    owners = (ctx_index - jnp.arange(ctx_count, dtype=jnp.int32)) % ctx_count
    token_pos = owners[:, None] * piece_rows + jnp.arange(piece_rows, dtype=jnp.int32)[None, :]
    ends = scale_ends[:, None, None, :]
    visible_end = jnp.min(jnp.where(ends > token_pos[None, :, :, None], ends, map_length), axis=3)
    key_mask = token_pos[None, None, None, :, :] < visible_end[:, :, :, None, None]

    def masked_scores():
        raw_scores = jnp.einsum(
            "amqgd,bmkgd->mgaqbk", query_all, keys_all, preferred_element_type=jnp.float32
        )
        return jnp.where(key_mask[:, None], raw_scores, -1e30)

    scores = masked_scores()
    row_max = jnp.max(scores, axis=(-2, -1), keepdims=True)
    exp_scores = jnp.exp(scores - row_max)
    exp_total = jnp.sum(exp_scores, axis=(-2, -1), keepdims=True)
    log_total = row_max + jnp.log(exp_total)
    probs_low = (exp_scores / exp_total).astype(jnp.bfloat16)
    out_all = jnp.einsum(
        "mgaqbk,bmkgd->amqgd", probs_low, values_all, preferred_element_type=jnp.float32
    ).astype(jnp.bfloat16)
    heads_out = group_return(out_all).reshape(row_count, local_width)
    attn_partial = jnp.dot(heads_out, full_proj, preferred_element_type=jnp.float32)
    attn_branch = tp_sum(attn_partial).reshape(map_count, piece_rows, model_width) + proj_bias
    attn_part = gamma_one[:, None] * attn_branch
    mid_stream = stream_in + attn_part
    second_mod, second_back = jax.vjp(modulate, mid_stream, scale_two, shift_two)
    mlp_in = second_mod.astype(jnp.bfloat16).reshape(row_count, model_width)
    pre_act = jnp.dot(mlp_in, full_up, preferred_element_type=jnp.float32) + up_bias
    activation, gelu_back = jax.vjp(gelu_tanh, pre_act)
    act_low = activation.astype(jnp.bfloat16)
    mlp_partial = jnp.dot(act_low, full_down, preferred_element_type=jnp.float32)
    mlp_branch = tp_sum(mlp_partial).reshape(map_count, piece_rows, model_width) + down_bias
    mlp_part = gamma_two[:, None] * mlp_branch
    stream = mid_stream + mlp_part
    grad_top = out_grad.astype(jnp.float32)
    d_gamma_two = jnp.sum(grad_top * mlp_branch, axis=1)
    d_mlp = gamma_two[:, None] * grad_top
    d_down_bias = jnp.sum(d_mlp, axis=(0, 1))
    d_mlp_low = d_mlp.astype(jnp.bfloat16).reshape(row_count, model_width)
    g_down = jnp.einsum("rf,rd->fd", act_low, d_mlp_low, preferred_element_type=jnp.float32)
    d_act = jnp.einsum("rd,fd->rf", d_mlp_low, full_down, preferred_element_type=jnp.float32)
    (d_pre,) = gelu_back(d_act)
    d_up_bias = jnp.sum(d_pre, axis=0)
    d_pre_low = d_pre.astype(jnp.bfloat16)
    g_up = jnp.einsum("rd,rf->df", mlp_in, d_pre_low, preferred_element_type=jnp.float32)
    d_mlp_in_part = jnp.einsum("rf,df->rd", d_pre_low, full_up, preferred_element_type=jnp.float32)
    d_mlp_in = tp_sum(d_mlp_in_part).reshape(map_count, piece_rows, model_width)
    d_mid, d_scale_two, d_shift_two = second_back(d_mlp_in)
    d_mid = d_mid + grad_top
    d_gamma_one = jnp.sum(d_mid * attn_branch, axis=1)
    d_attn = gamma_one[:, None] * d_mid
    d_proj_bias = jnp.sum(d_attn, axis=(0, 1))
    d_attn_low = d_attn.astype(jnp.bfloat16).reshape(row_count, model_width)
    g_proj = jnp.einsum("ri,rd->id", heads_out, d_attn_low, preferred_element_type=jnp.float32)
    d_heads = jnp.einsum("rd,id->ri", d_attn_low, full_proj, preferred_element_type=jnp.float32)
    d_heads = d_heads.astype(jnp.bfloat16).reshape(head_shape)
    d_heads_all = group_send(d_heads.reshape(group_shape))
    probs = probs_low.astype(jnp.float32)
    d_probs = jnp.einsum(
        "amqgd,bmkgd->mgaqbk", d_heads_all, values_all, preferred_element_type=jnp.float32
    )
    row_delta = jnp.sum(probs * d_probs, axis=(-2, -1), keepdims=True)
    d_scores = (probs * (d_probs - row_delta)).astype(jnp.bfloat16)
    probs_again = probs_low
    d_query_all = jnp.einsum(
        "mgaqbk,bmkgd->amqgd", d_scores, keys_all, preferred_element_type=jnp.float32
    ).astype(jnp.bfloat16)
    d_key_all = jnp.einsum(
        "mgaqbk,amqgd->bmkgd", d_scores, query_all, preferred_element_type=jnp.float32
    ).astype(jnp.bfloat16)
    d_value_all = jnp.einsum(
        "mgaqbk,amqgd->bmkgd", probs_again, d_heads_all, preferred_element_type=jnp.float32
    ).astype(jnp.bfloat16)
    d_query_unit = group_return(d_query_all).reshape(head_shape).astype(jnp.float32)
    d_key_unit = group_return(d_key_all).reshape(head_shape).astype(jnp.float32)
    d_value = group_return(d_value_all).reshape(head_shape).astype(jnp.float32)
    early_shards = (
        lax.psum_scatter(
            g_up.astype(jnp.bfloat16), "shard", scatter_dimension=0, tiled=True
        ),
        lax.psum_scatter(
            g_proj.astype(jnp.bfloat16), "shard", scatter_dimension=1, tiled=True
        ),
        lax.psum_scatter(
            g_down.astype(jnp.bfloat16), "shard", scatter_dimension=1, tiled=True
        ),
    )
    early_shards, d_query_unit, d_key_unit, d_value = lax.optimization_barrier(
        (early_shards, d_query_unit, d_key_unit, d_value)
    )
    d_query, d_head_scale = query_back(d_query_unit)
    (d_key,) = key_back(d_key_unit)
    d_query = d_query.reshape(map_count, piece_rows, local_width)
    d_key = d_key.reshape(map_count, piece_rows, local_width)
    d_value = d_value.reshape(map_count, piece_rows, local_width)
    d_query_bias = jnp.sum(d_query, axis=(0, 1))
    d_value_bias = jnp.sum(d_value, axis=(0, 1))
    d_qkv = (
        jnp.stack([d_query, d_key, d_value], axis=2)
        .astype(jnp.bfloat16)
        .reshape(row_count, 3 * local_width)
    )
    g_qkv = jnp.einsum("rd,rc->dc", attn_in, d_qkv, preferred_element_type=jnp.float32).reshape(
        model_width, 3, local_width
    )
    early_summed = lax.psum(early_shards, "ctx")
    qkv_low, early_summed = lax.optimization_barrier((g_qkv.astype(jnp.bfloat16), early_summed))
    qkv_shard = lax.psum_scatter(qkv_low, "shard", scatter_dimension=0, tiled=True)
    d_attn_in_part = jnp.einsum("rc,dc->rd", d_qkv, qkv_matrix, preferred_element_type=jnp.float32)
    d_attn_in = tp_sum(d_attn_in_part).reshape(map_count, piece_rows, model_width)
    d_input, d_scale_one, d_shift_one = first_back(d_attn_in)
    d_input = d_input + d_mid
    d_mod_part = jnp.stack(
        [d_gamma_one, d_gamma_two, d_scale_one, d_scale_two, d_shift_one, d_shift_two], axis=1
    )
    d_mod = lax.psum(d_mod_part, "ctx").astype(jnp.bfloat16).reshape(map_count, 6 * model_width)
    qkv_shard, d_mod = lax.optimization_barrier((qkv_shard, d_mod))
    d_mod_all = lax.all_gather(d_mod, "shard", axis=0, tiled=True)
    g_ada = jnp.einsum(
        "md,mc->dc", cond_cols, d_mod_all, preferred_element_type=jnp.float32
    ).reshape(ada_rows, 6, model_width)
    d_ada_bias = jnp.sum(d_mod_all.astype(jnp.float32), axis=0).reshape(6, model_width)
    d_cond_cols = jnp.einsum("mc,dc->md", d_mod_all, ada_local, preferred_element_type=jnp.float32)
    d_cond_in = lax.all_to_all(d_cond_cols, "shard", 0, 1, tiled=True)
    silu_value, silu_back = jax.vjp(jax.nn.silu, cond_wide)
    (d_cond,) = silu_back(d_cond_in)
    qkv_summed = lax.psum(qkv_shard, "ctx")
    summed = tuple(
        g.astype(jnp.float32) for g in (qkv_summed, early_summed[0], early_summed[1], early_summed[2])
    )
    square_sums = jnp.stack(
        [jnp.sum(stream * stream), jnp.sum(attn_part * attn_part), jnp.sum(mlp_part * mlp_part)]
    )
    small_parts = (
        square_sums,
        d_query_bias,
        d_value_bias,
        d_head_scale,
        d_proj_bias,
        d_up_bias,
        d_down_bias,
    )
    small_flat = small_sum(jnp.concatenate(small_parts))
    small = []
    offset = 0
    for part in small_parts:
        small.append(small_flat[offset:offset + part.shape[0]])
        offset += part.shape[0]
    entry_total = map_count * map_length * model_width * lax.axis_size("shard")
    norm_stats = jnp.sqrt(small[0] / entry_total)
    return (
        stream.astype(jnp.bfloat16),
        d_input.astype(jnp.bfloat16),
        d_cond,
        g_ada,
        d_ada_bias,
        summed[0],
        small[1],
        small[2],
        small[3],
        summed[2],
        small[4],
        summed[1],
        small[5],
        summed[3],
        small[6],
        norm_stats,
    )


def solution(mesh):
    in_specs = (
        P("shard", "ctx", None),
        P("shard", None),
        P("shard", None),
        P("shard", None, None),
        P(),
        P("shard", None, "tp"),
        P("tp"),
        P("tp"),
        P("tp"),
        P("tp", "shard"),
        P(),
        P("shard", "tp"),
        P("tp"),
        P("tp", "shard"),
        P(),
        P("shard", "ctx", None),
    )
    out_specs = (
        P("shard", "ctx", None),
        P("shard", "ctx", None),
        P("shard", None),
        P("shard", None, None),
        P(),
        P("shard", None, "tp"),
        P("tp"),
        P("tp"),
        P("tp"),
        P("tp", "shard"),
        P(),
        P("shard", "tp"),
        P("tp"),
        P("tp", "shard"),
        P(),
        P(),
    )
    return jax.shard_map(body, mesh=mesh, in_specs=in_specs, out_specs=out_specs, check_vma=False)
```

```python
import jax
import jax.numpy as jnp
from jax import lax
from jax.sharding import PartitionSpec as P


def layer_norm(values):
    center = values - jnp.mean(values, axis=-1, keepdims=True)
    spread = jnp.mean(center * center, axis=-1, keepdims=True)
    return center * lax.rsqrt(spread + 1e-06)


def modulate(values, scale, shift):
    return layer_norm(values) * (1.0 + scale[:, None, :]) + shift[:, None, :]


def unit_scaled(values, gains):
    normed = values * lax.rsqrt(jnp.sum(values * values, axis=-1, keepdims=True) + 1e-06)
    return normed * jnp.exp(gains)[None, None, :, None]


def unit_plain(values):
    return values * lax.rsqrt(jnp.sum(values * values, axis=-1, keepdims=True) + 1e-06)


def gelu_tanh(values):
    return jax.nn.gelu(values, approximate=True)


def tp_sum(values):
    count = lax.axis_size("tp")
    if count != 2:
        return lax.psum(values, "tp")
    return values + lax.ppermute(values, "tp", [(0, 1), (1, 0)])


def ctx_shifts(values):
    count = lax.axis_size("ctx")
    parts = [values]
    for shift in range(1, count):
        pairs = [(i, (i + shift) % count) for i in range(count)]
        parts.append(lax.ppermute(values, "ctx", pairs))
    return jnp.stack(parts)


def ctx_return(parts):
    count = lax.axis_size("ctx")
    total = parts[0].astype(jnp.float32)
    for shift in range(1, count):
        pairs = [(i, (i - shift) % count) for i in range(count)]
        total = total + lax.ppermute(parts[shift], "ctx", pairs).astype(jnp.float32)
    return total


def group_send(values):
    count = lax.axis_size("ctx")
    me = lax.axis_index("ctx")
    parts = []
    for shift in range(count):
        block = lax.dynamic_index_in_dim(values, (me + shift) % count, axis=2, keepdims=False)
        if shift:
            pairs = [(i, (i + shift) % count) for i in range(count)]
            block = lax.ppermute(block, "ctx", pairs)
        parts.append(block)
    return jnp.stack(parts)


def group_return(parts):
    count = lax.axis_size("ctx")
    me = lax.axis_index("ctx")
    back = [parts[0]]
    for shift in range(1, count):
        pairs = [(i, (i - shift) % count) for i in range(count)]
        back.append(lax.ppermute(parts[shift], "ctx", pairs))
    stacked = jnp.stack(back)
    order = (jnp.arange(count, dtype=jnp.int32) - me) % count
    return jnp.moveaxis(jnp.take(stacked, order, axis=0), 0, 2)


def gather_axis(values, axis):
    count = lax.axis_size(axis)
    me = lax.axis_index(axis)
    parts = [values]
    for shift in range(1, count):
        pairs = [(i, (i + shift) % count) for i in range(count)]
        parts.append(lax.ppermute(values, axis, pairs))
    stacked = jnp.stack(parts)
    order = (me - jnp.arange(count, dtype=jnp.int32)) % count
    return jnp.take(stacked, order, axis=0)


def small_sum(values):
    every = gather_axis(gather_axis(values, "ctx"), "shard")
    return jnp.sum(every, axis=(0, 1))


def body(
    hidden_in,
    cond,
    scale_len,
    ada_weight,
    ada_bias,
    qkv_weight,
    query_bias,
    value_bias,
    head_scale,
    proj_weight,
    proj_bias,
    up_weight,
    up_bias,
    down_weight,
    down_bias,
    out_grad,
):
    map_count = hidden_in.shape[0]
    piece_rows = hidden_in.shape[1]
    model_width = hidden_in.shape[2]
    ctx_count = lax.axis_size("ctx")
    ctx_index = lax.axis_index("ctx")
    shard_index = lax.axis_index("shard")
    map_length = piece_rows * ctx_count
    heads_here = head_scale.shape[0]
    local_width = query_bias.shape[0]
    head_dim = local_width // heads_here
    row_count = map_count * piece_rows
    head_shape = (map_count, piece_rows, heads_here, head_dim)
    ada_rows = ada_weight.shape[0]
    shard_count = lax.axis_size("shard")
    full_qkv = lax.all_gather(qkv_weight, "shard", axis=0, tiled=True)
    full_proj = lax.all_gather(proj_weight, "shard", axis=1, tiled=True)
    full_up = lax.all_gather(up_weight, "shard", axis=0, tiled=True)
    full_down = lax.all_gather(down_weight, "shard", axis=1, tiled=True)
    qkv_matrix = full_qkv.reshape(model_width, 3 * local_width)

    cond_wide = cond.astype(jnp.float32)
    cond_all = lax.all_gather(cond, "shard", axis=0, tiled=True).astype(jnp.float32)
    cond_in_all = jax.nn.silu(cond_all).astype(jnp.bfloat16)
    cond_cols = lax.dynamic_slice_in_dim(cond_in_all, shard_index * ada_rows, ada_rows, axis=1)
    ada_local = ada_weight.reshape(ada_rows, 6 * model_width)
    mod_partial = jnp.dot(cond_cols, ada_local, preferred_element_type=jnp.float32)
    modulation = lax.psum_scatter(mod_partial, "shard", scatter_dimension=0, tiled=True)
    modulation = modulation.reshape(map_count, 6, model_width) + ada_bias[None]
    gamma_one = modulation[:, 0]
    gamma_two = modulation[:, 1]
    scale_one = modulation[:, 2]
    scale_two = modulation[:, 3]
    shift_one = modulation[:, 4]
    shift_two = modulation[:, 5]
    stream_in = hidden_in.astype(jnp.float32)
    first_mod, first_back = jax.vjp(modulate, stream_in, scale_one, shift_one)
    attn_in = first_mod.astype(jnp.bfloat16).reshape(row_count, model_width)
    qkv = jnp.dot(attn_in, qkv_matrix, preferred_element_type=jnp.float32).reshape(
        map_count, piece_rows, 3, local_width
    )
    query = (qkv[:, :, 0] + query_bias).reshape(head_shape)
    key_raw = qkv[:, :, 1].reshape(head_shape)
    value_low = (qkv[:, :, 2] + value_bias).astype(jnp.bfloat16).reshape(head_shape)
    query_unit, query_back = jax.vjp(unit_scaled, query, head_scale)
    key_unit, key_back = jax.vjp(unit_plain, key_raw)
    query_low = query_unit.astype(jnp.bfloat16)
    key_low = key_unit.astype(jnp.bfloat16)
    group_heads = heads_here // ctx_count
    group_shape = (map_count, piece_rows, ctx_count, group_heads, head_dim)
    query_all = group_send(query_low.reshape(group_shape))
    keys_all = group_send(key_low.reshape(group_shape))
    values_all = group_send(value_low.reshape(group_shape))
    scale_ends = jnp.cumsum(scale_len, axis=1)
    owners = (ctx_index - jnp.arange(ctx_count, dtype=jnp.int32)) % ctx_count
    token_pos = owners[:, None] * piece_rows + jnp.arange(piece_rows, dtype=jnp.int32)[None, :]
    ends = scale_ends[:, None, None, :]
    visible_end = jnp.min(jnp.where(ends > token_pos[None, :, :, None], ends, map_length), axis=3)
    key_mask = token_pos[None, None, None, :, :] < visible_end[:, :, :, None, None]

    def masked_scores():
        raw_scores = jnp.einsum(
            "amqgd,bmkgd->mgaqbk", query_all, keys_all, preferred_element_type=jnp.float32
        )
        return jnp.where(key_mask[:, None], raw_scores, -1e30)

    scores = masked_scores()
    row_max = jnp.max(scores, axis=(-2, -1), keepdims=True)
    exp_scores = jnp.exp(scores - row_max)
    exp_total = jnp.sum(exp_scores, axis=(-2, -1), keepdims=True)
    log_total = row_max + jnp.log(exp_total)
    probs_low = (exp_scores / exp_total).astype(jnp.bfloat16)
    out_all = jnp.einsum(
        "mgaqbk,bmkgd->amqgd", probs_low, values_all, preferred_element_type=jnp.float32
    ).astype(jnp.bfloat16)
    heads_out = group_return(out_all).reshape(row_count, local_width)
    attn_partial = jnp.dot(heads_out, full_proj, preferred_element_type=jnp.float32)
    attn_branch = tp_sum(attn_partial).reshape(map_count, piece_rows, model_width) + proj_bias
    attn_part = gamma_one[:, None] * attn_branch
    mid_stream = stream_in + attn_part
    second_mod, second_back = jax.vjp(modulate, mid_stream, scale_two, shift_two)
    mlp_in = second_mod.astype(jnp.bfloat16).reshape(row_count, model_width)
    pre_act = jnp.dot(mlp_in, full_up, preferred_element_type=jnp.float32) + up_bias
    activation, gelu_back = jax.vjp(gelu_tanh, pre_act)
    act_low = activation.astype(jnp.bfloat16)
    mlp_partial = jnp.dot(act_low, full_down, preferred_element_type=jnp.float32)
    mlp_branch = tp_sum(mlp_partial).reshape(map_count, piece_rows, model_width) + down_bias
    mlp_part = gamma_two[:, None] * mlp_branch
    stream = mid_stream + mlp_part
    grad_top = out_grad.astype(jnp.float32)
    d_gamma_two = jnp.sum(grad_top * mlp_branch, axis=1)
    d_mlp = gamma_two[:, None] * grad_top
    d_down_bias = jnp.sum(d_mlp, axis=(0, 1))
    d_mlp_low = d_mlp.astype(jnp.bfloat16).reshape(row_count, model_width)
    g_down = jnp.einsum("rf,rd->fd", act_low, d_mlp_low, preferred_element_type=jnp.float32)
    d_act = jnp.einsum("rd,fd->rf", d_mlp_low, full_down, preferred_element_type=jnp.float32)
    (d_pre,) = gelu_back(d_act)
    d_up_bias = jnp.sum(d_pre, axis=0)
    d_pre_low = d_pre.astype(jnp.bfloat16)
    g_up = jnp.einsum("rd,rf->df", mlp_in, d_pre_low, preferred_element_type=jnp.float32)
    d_mlp_in_part = jnp.einsum("rf,df->rd", d_pre_low, full_up, preferred_element_type=jnp.float32)
    d_mlp_in = tp_sum(d_mlp_in_part).reshape(map_count, piece_rows, model_width)
    d_mid, d_scale_two, d_shift_two = second_back(d_mlp_in)
    d_mid = d_mid + grad_top
    d_gamma_one = jnp.sum(d_mid * attn_branch, axis=1)
    d_attn = gamma_one[:, None] * d_mid
    d_proj_bias = jnp.sum(d_attn, axis=(0, 1))
    d_attn_low = d_attn.astype(jnp.bfloat16).reshape(row_count, model_width)
    g_proj = jnp.einsum("ri,rd->id", heads_out, d_attn_low, preferred_element_type=jnp.float32)
    d_heads = jnp.einsum("rd,id->ri", d_attn_low, full_proj, preferred_element_type=jnp.float32)
    d_heads = d_heads.astype(jnp.bfloat16).reshape(head_shape)
    d_heads_all = group_send(d_heads.reshape(group_shape))
    probs = probs_low.astype(jnp.float32)
    d_probs = jnp.einsum(
        "amqgd,bmkgd->mgaqbk", d_heads_all, values_all, preferred_element_type=jnp.float32
    )
    row_delta = jnp.sum(probs * d_probs, axis=(-2, -1), keepdims=True)
    d_scores = (probs * (d_probs - row_delta)).astype(jnp.bfloat16)
    probs_again = probs_low
    d_query_all = jnp.einsum(
        "mgaqbk,bmkgd->amqgd", d_scores, keys_all, preferred_element_type=jnp.float32
    ).astype(jnp.bfloat16)
    d_key_all = jnp.einsum(
        "mgaqbk,amqgd->bmkgd", d_scores, query_all, preferred_element_type=jnp.float32
    ).astype(jnp.bfloat16)
    d_value_all = jnp.einsum(
        "mgaqbk,amqgd->bmkgd", probs_again, d_heads_all, preferred_element_type=jnp.float32
    ).astype(jnp.bfloat16)
    d_query_unit = group_return(d_query_all).reshape(head_shape).astype(jnp.float32)
    d_key_unit = group_return(d_key_all).reshape(head_shape).astype(jnp.float32)
    d_value = group_return(d_value_all).reshape(head_shape).astype(jnp.float32)
    early_shards = (
        lax.psum_scatter(
            g_up.astype(jnp.bfloat16), "shard", scatter_dimension=0, tiled=True
        ),
        lax.psum_scatter(
            g_proj.astype(jnp.bfloat16), "shard", scatter_dimension=1, tiled=True
        ),
        lax.psum_scatter(
            g_down.astype(jnp.bfloat16), "shard", scatter_dimension=1, tiled=True
        ),
    )
    early_shards, d_query_unit, d_key_unit, d_value = lax.optimization_barrier(
        (early_shards, d_query_unit, d_key_unit, d_value)
    )
    d_query, d_head_scale = query_back(d_query_unit)
    (d_key,) = key_back(d_key_unit)
    d_query = d_query.reshape(map_count, piece_rows, local_width)
    d_key = d_key.reshape(map_count, piece_rows, local_width)
    d_value = d_value.reshape(map_count, piece_rows, local_width)
    d_query_bias = jnp.sum(d_query, axis=(0, 1))
    d_value_bias = jnp.sum(d_value, axis=(0, 1))
    d_qkv = (
        jnp.stack([d_query, d_key, d_value], axis=2)
        .astype(jnp.bfloat16)
        .reshape(row_count, 3 * local_width)
    )
    g_qkv = jnp.einsum("rd,rc->dc", attn_in, d_qkv, preferred_element_type=jnp.float32).reshape(
        model_width, 3, local_width
    )
    early_summed = lax.psum(early_shards, "ctx")
    qkv_low, early_summed = lax.optimization_barrier((g_qkv.astype(jnp.bfloat16), early_summed))
    qkv_shard = lax.psum_scatter(qkv_low, "shard", scatter_dimension=0, tiled=True)
    d_attn_in_part = jnp.einsum("rc,dc->rd", d_qkv, qkv_matrix, preferred_element_type=jnp.float32)
    d_attn_in = tp_sum(d_attn_in_part).reshape(map_count, piece_rows, model_width)
    d_input, d_scale_one, d_shift_one = first_back(d_attn_in)
    d_input = d_input + d_mid
    d_mod_part = jnp.stack(
        [d_gamma_one, d_gamma_two, d_scale_one, d_scale_two, d_shift_one, d_shift_two], axis=1
    )
    d_mod = lax.psum(d_mod_part, "ctx").astype(jnp.bfloat16).reshape(map_count, 6 * model_width)
    d_mod_all = lax.all_gather(d_mod, "shard", axis=0, tiled=True)
    g_ada = jnp.einsum(
        "md,mc->dc", cond_cols, d_mod_all, preferred_element_type=jnp.float32
    ).reshape(ada_rows, 6, model_width)
    d_ada_bias = jnp.sum(d_mod_all.astype(jnp.float32), axis=0).reshape(6, model_width)
    d_cond_cols = jnp.einsum("mc,dc->md", d_mod_all, ada_local, preferred_element_type=jnp.float32)
    d_cond_in = lax.all_to_all(d_cond_cols, "shard", 0, 1, tiled=True)
    silu_value, silu_back = jax.vjp(jax.nn.silu, cond_wide)
    (d_cond,) = silu_back(d_cond_in)
    qkv_summed = lax.psum(qkv_shard, "ctx")
    summed = tuple(
        g.astype(jnp.float32) for g in (qkv_summed, early_summed[0], early_summed[1], early_summed[2])
    )
    square_sums = jnp.stack(
        [jnp.sum(stream * stream), jnp.sum(attn_part * attn_part), jnp.sum(mlp_part * mlp_part)]
    )
    small_parts = (
        square_sums,
        d_query_bias,
        d_value_bias,
        d_head_scale,
        d_proj_bias,
        d_up_bias,
        d_down_bias,
    )
    small_flat = small_sum(jnp.concatenate(small_parts))
    small = []
    offset = 0
    for part in small_parts:
        small.append(small_flat[offset:offset + part.shape[0]])
        offset += part.shape[0]
    entry_total = map_count * map_length * model_width * lax.axis_size("shard")
    norm_stats = jnp.sqrt(small[0] / entry_total)
    return (
        stream.astype(jnp.bfloat16),
        d_input.astype(jnp.bfloat16),
        d_cond,
        g_ada,
        d_ada_bias,
        summed[0],
        small[1],
        small[2],
        small[3],
        summed[2],
        small[4],
        summed[1],
        small[5],
        summed[3],
        small[6],
        norm_stats,
    )


def solution(mesh):
    in_specs = (
        P("shard", "ctx", None),
        P("shard", None),
        P("shard", None),
        P("shard", None, None),
        P(),
        P("shard", None, "tp"),
        P("tp"),
        P("tp"),
        P("tp"),
        P("tp", "shard"),
        P(),
        P("shard", "tp"),
        P("tp"),
        P("tp", "shard"),
        P(),
        P("shard", "ctx", None),
    )
    out_specs = (
        P("shard", "ctx", None),
        P("shard", "ctx", None),
        P("shard", None),
        P("shard", None, None),
        P(),
        P("shard", None, "tp"),
        P("tp"),
        P("tp"),
        P("tp"),
        P("tp", "shard"),
        P(),
        P("shard", "tp"),
        P("tp"),
        P("tp", "shard"),
        P(),
        P(),
    )
    return jax.shard_map(body, mesh=mesh, in_specs=in_specs, out_specs=out_specs, check_vma=False)
```

```python
import jax
import jax.numpy as jnp
from jax import lax
from jax.sharding import PartitionSpec as P


def layer_norm(values):
    center = values - jnp.mean(values, axis=-1, keepdims=True)
    spread = jnp.mean(center * center, axis=-1, keepdims=True)
    return center * lax.rsqrt(spread + 1e-06)


def modulate(values, scale, shift):
    return layer_norm(values) * (1.0 + scale[:, None, :]) + shift[:, None, :]


def unit_scaled(values, gains):
    normed = values * lax.rsqrt(jnp.sum(values * values, axis=-1, keepdims=True) + 1e-06)
    return normed * jnp.exp(gains)[None, None, :, None]


def unit_plain(values):
    return values * lax.rsqrt(jnp.sum(values * values, axis=-1, keepdims=True) + 1e-06)


def gelu_tanh(values):
    return jax.nn.gelu(values, approximate=True)


def tp_sum(values):
    count = lax.axis_size("tp")
    if count != 2:
        return lax.psum(values, "tp")
    return values + lax.ppermute(values, "tp", [(0, 1), (1, 0)])


def ctx_shifts(values):
    count = lax.axis_size("ctx")
    parts = [values]
    for shift in range(1, count):
        pairs = [(i, (i + shift) % count) for i in range(count)]
        parts.append(lax.ppermute(values, "ctx", pairs))
    return jnp.stack(parts)


def ctx_return(parts):
    count = lax.axis_size("ctx")
    total = parts[0].astype(jnp.float32)
    for shift in range(1, count):
        pairs = [(i, (i - shift) % count) for i in range(count)]
        total = total + lax.ppermute(parts[shift], "ctx", pairs).astype(jnp.float32)
    return total


def group_send(values):
    count = lax.axis_size("ctx")
    me = lax.axis_index("ctx")
    parts = []
    for shift in range(count):
        block = lax.dynamic_index_in_dim(values, (me + shift) % count, axis=2, keepdims=False)
        if shift:
            pairs = [(i, (i + shift) % count) for i in range(count)]
            block = lax.ppermute(block, "ctx", pairs)
        parts.append(block)
    return jnp.stack(parts)


def group_return(parts):
    count = lax.axis_size("ctx")
    me = lax.axis_index("ctx")
    back = [parts[0]]
    for shift in range(1, count):
        pairs = [(i, (i - shift) % count) for i in range(count)]
        back.append(lax.ppermute(parts[shift], "ctx", pairs))
    stacked = jnp.stack(back)
    order = (jnp.arange(count, dtype=jnp.int32) - me) % count
    return jnp.moveaxis(jnp.take(stacked, order, axis=0), 0, 2)


def gather_axis(values, axis):
    count = lax.axis_size(axis)
    me = lax.axis_index(axis)
    parts = [values]
    for shift in range(1, count):
        pairs = [(i, (i + shift) % count) for i in range(count)]
        parts.append(lax.ppermute(values, axis, pairs))
    stacked = jnp.stack(parts)
    order = (me - jnp.arange(count, dtype=jnp.int32)) % count
    return jnp.take(stacked, order, axis=0)


def small_sum(values):
    every = gather_axis(gather_axis(values, "ctx"), "shard")
    return jnp.sum(every, axis=(0, 1))


def body(
    hidden_in,
    cond,
    scale_len,
    ada_weight,
    ada_bias,
    qkv_weight,
    query_bias,
    value_bias,
    head_scale,
    proj_weight,
    proj_bias,
    up_weight,
    up_bias,
    down_weight,
    down_bias,
    out_grad,
):
    map_count = hidden_in.shape[0]
    piece_rows = hidden_in.shape[1]
    model_width = hidden_in.shape[2]
    ctx_count = lax.axis_size("ctx")
    ctx_index = lax.axis_index("ctx")
    shard_index = lax.axis_index("shard")
    map_length = piece_rows * ctx_count
    heads_here = head_scale.shape[0]
    local_width = query_bias.shape[0]
    head_dim = local_width // heads_here
    row_count = map_count * piece_rows
    head_shape = (map_count, piece_rows, heads_here, head_dim)
    ada_rows = ada_weight.shape[0]
    shard_count = lax.axis_size("shard")
    full_qkv = lax.all_gather(qkv_weight, "shard", axis=0, tiled=True)
    full_proj = lax.all_gather(proj_weight, "shard", axis=1, tiled=True)
    full_up = lax.all_gather(up_weight, "shard", axis=0, tiled=True)
    full_down = lax.all_gather(down_weight, "shard", axis=1, tiled=True)
    qkv_matrix = full_qkv.reshape(model_width, 3 * local_width)

    cond_wide = cond.astype(jnp.float32)
    cond_all = lax.all_gather(cond, "shard", axis=0, tiled=True).astype(jnp.float32)
    cond_in_all = jax.nn.silu(cond_all).astype(jnp.bfloat16)
    cond_cols = lax.dynamic_slice_in_dim(cond_in_all, shard_index * ada_rows, ada_rows, axis=1)
    ada_local = ada_weight.reshape(ada_rows, 6 * model_width)
    mod_partial = jnp.dot(cond_cols, ada_local, preferred_element_type=jnp.float32)
    modulation = lax.psum_scatter(mod_partial, "shard", scatter_dimension=0, tiled=True)
    modulation = modulation.reshape(map_count, 6, model_width) + ada_bias[None]
    gamma_one = modulation[:, 0]
    gamma_two = modulation[:, 1]
    scale_one = modulation[:, 2]
    scale_two = modulation[:, 3]
    shift_one = modulation[:, 4]
    shift_two = modulation[:, 5]
    stream_in = hidden_in.astype(jnp.float32)
    first_mod, first_back = jax.vjp(modulate, stream_in, scale_one, shift_one)
    attn_in = first_mod.astype(jnp.bfloat16).reshape(row_count, model_width)
    qkv = jnp.dot(attn_in, qkv_matrix, preferred_element_type=jnp.float32).reshape(
        map_count, piece_rows, 3, local_width
    )
    query = (qkv[:, :, 0] + query_bias).reshape(head_shape)
    key_raw = qkv[:, :, 1].reshape(head_shape)
    value_low = (qkv[:, :, 2] + value_bias).astype(jnp.bfloat16).reshape(head_shape)
    query_unit, query_back = jax.vjp(unit_scaled, query, head_scale)
    key_unit, key_back = jax.vjp(unit_plain, key_raw)
    query_low = query_unit.astype(jnp.bfloat16)
    key_low = key_unit.astype(jnp.bfloat16)
    group_heads = heads_here // ctx_count
    group_shape = (map_count, piece_rows, ctx_count, group_heads, head_dim)
    query_all = group_send(query_low.reshape(group_shape))
    keys_all = group_send(key_low.reshape(group_shape))
    values_all = group_send(value_low.reshape(group_shape))
    scale_ends = jnp.cumsum(scale_len, axis=1)
    owners = (ctx_index - jnp.arange(ctx_count, dtype=jnp.int32)) % ctx_count
    token_pos = owners[:, None] * piece_rows + jnp.arange(piece_rows, dtype=jnp.int32)[None, :]
    ends = scale_ends[:, None, None, :]
    visible_end = jnp.min(jnp.where(ends > token_pos[None, :, :, None], ends, map_length), axis=3)
    key_mask = token_pos[None, None, None, :, :] < visible_end[:, :, :, None, None]

    def masked_scores():
        raw_scores = jnp.einsum(
            "amqgd,bmkgd->mgaqbk", query_all, keys_all, preferred_element_type=jnp.float32
        )
        return jnp.where(key_mask[:, None], raw_scores, -1e30)

    scores = masked_scores()
    row_max = jnp.max(scores, axis=(-2, -1), keepdims=True)
    exp_scores = jnp.exp(scores - row_max)
    exp_total = jnp.sum(exp_scores, axis=(-2, -1), keepdims=True)
    log_total = row_max + jnp.log(exp_total)
    probs_low = (exp_scores / exp_total).astype(jnp.bfloat16)
    out_all = jnp.einsum(
        "mgaqbk,bmkgd->amqgd", probs_low, values_all, preferred_element_type=jnp.float32
    ).astype(jnp.bfloat16)
    heads_out = group_return(out_all).reshape(row_count, local_width)
    attn_partial = jnp.dot(heads_out, full_proj, preferred_element_type=jnp.float32)
    attn_branch = tp_sum(attn_partial).reshape(map_count, piece_rows, model_width) + proj_bias
    attn_part = gamma_one[:, None] * attn_branch
    mid_stream = stream_in + attn_part
    second_mod, second_back = jax.vjp(modulate, mid_stream, scale_two, shift_two)
    mlp_in = second_mod.astype(jnp.bfloat16).reshape(row_count, model_width)
    pre_act = jnp.dot(mlp_in, full_up, preferred_element_type=jnp.float32) + up_bias
    activation, gelu_back = jax.vjp(gelu_tanh, pre_act)
    act_low = activation.astype(jnp.bfloat16)
    mlp_partial = jnp.dot(act_low, full_down, preferred_element_type=jnp.float32)
    mlp_branch = tp_sum(mlp_partial).reshape(map_count, piece_rows, model_width) + down_bias
    mlp_part = gamma_two[:, None] * mlp_branch
    stream = mid_stream + mlp_part
    grad_top = out_grad.astype(jnp.float32)
    d_gamma_two = jnp.sum(grad_top * mlp_branch, axis=1)
    d_mlp = gamma_two[:, None] * grad_top
    d_down_bias = jnp.sum(d_mlp, axis=(0, 1))
    d_mlp_low = d_mlp.astype(jnp.bfloat16).reshape(row_count, model_width)
    g_down = jnp.einsum("rf,rd->fd", act_low, d_mlp_low, preferred_element_type=jnp.float32)
    d_act = jnp.einsum("rd,fd->rf", d_mlp_low, full_down, preferred_element_type=jnp.float32)
    (d_pre,) = gelu_back(d_act)
    d_up_bias = jnp.sum(d_pre, axis=0)
    d_pre_low = d_pre.astype(jnp.bfloat16)
    g_up = jnp.einsum("rd,rf->df", mlp_in, d_pre_low, preferred_element_type=jnp.float32)
    d_mlp_in_part = jnp.einsum("rf,df->rd", d_pre_low, full_up, preferred_element_type=jnp.float32)
    d_mlp_in = tp_sum(d_mlp_in_part).reshape(map_count, piece_rows, model_width)
    d_mid, d_scale_two, d_shift_two = second_back(d_mlp_in)
    d_mid = d_mid + grad_top
    d_gamma_one = jnp.sum(d_mid * attn_branch, axis=1)
    d_attn = gamma_one[:, None] * d_mid
    d_proj_bias = jnp.sum(d_attn, axis=(0, 1))
    d_attn_low = d_attn.astype(jnp.bfloat16).reshape(row_count, model_width)
    g_proj = jnp.einsum("ri,rd->id", heads_out, d_attn_low, preferred_element_type=jnp.float32)
    d_heads = jnp.einsum("rd,id->ri", d_attn_low, full_proj, preferred_element_type=jnp.float32)
    d_heads = d_heads.astype(jnp.bfloat16).reshape(head_shape)
    d_heads_all = group_send(d_heads.reshape(group_shape))
    probs = probs_low.astype(jnp.float32)
    d_probs = jnp.einsum(
        "amqgd,bmkgd->mgaqbk", d_heads_all, values_all, preferred_element_type=jnp.float32
    )
    row_delta = jnp.sum(probs * d_probs, axis=(-2, -1), keepdims=True)
    d_scores = (probs * (d_probs - row_delta)).astype(jnp.bfloat16)
    probs_again = probs_low
    d_query_all = jnp.einsum(
        "mgaqbk,bmkgd->amqgd", d_scores, keys_all, preferred_element_type=jnp.float32
    ).astype(jnp.bfloat16)
    d_key_all = jnp.einsum(
        "mgaqbk,amqgd->bmkgd", d_scores, query_all, preferred_element_type=jnp.float32
    ).astype(jnp.bfloat16)
    d_value_all = jnp.einsum(
        "mgaqbk,amqgd->bmkgd", probs_again, d_heads_all, preferred_element_type=jnp.float32
    ).astype(jnp.bfloat16)
    d_query_unit = group_return(d_query_all).reshape(head_shape).astype(jnp.float32)
    d_key_unit = group_return(d_key_all).reshape(head_shape).astype(jnp.float32)
    d_value = group_return(d_value_all).reshape(head_shape).astype(jnp.float32)
    early_shards = (
        lax.psum_scatter(
            g_up.astype(jnp.bfloat16), "shard", scatter_dimension=0, tiled=True
        ),
        lax.psum_scatter(
            g_proj.astype(jnp.bfloat16), "shard", scatter_dimension=1, tiled=True
        ),
        lax.psum_scatter(
            g_down.astype(jnp.bfloat16), "shard", scatter_dimension=1, tiled=True
        ),
    )
    early_shards, d_query_unit, d_key_unit, d_value = lax.optimization_barrier(
        (early_shards, d_query_unit, d_key_unit, d_value)
    )
    d_query, d_head_scale = query_back(d_query_unit)
    (d_key,) = key_back(d_key_unit)
    d_query = d_query.reshape(map_count, piece_rows, local_width)
    d_key = d_key.reshape(map_count, piece_rows, local_width)
    d_value = d_value.reshape(map_count, piece_rows, local_width)
    d_query_bias = jnp.sum(d_query, axis=(0, 1))
    d_value_bias = jnp.sum(d_value, axis=(0, 1))
    d_qkv = (
        jnp.stack([d_query, d_key, d_value], axis=2)
        .astype(jnp.bfloat16)
        .reshape(row_count, 3 * local_width)
    )
    g_qkv = jnp.einsum("rd,rc->dc", attn_in, d_qkv, preferred_element_type=jnp.float32).reshape(
        model_width, 3, local_width
    )
    early_summed = lax.psum(early_shards, "ctx")
    qkv_low, early_summed = lax.optimization_barrier((g_qkv.astype(jnp.bfloat16), early_summed))
    qkv_shard = lax.psum_scatter(qkv_low, "shard", scatter_dimension=0, tiled=True)
    d_attn_in_part = jnp.einsum("rc,dc->rd", d_qkv, qkv_matrix, preferred_element_type=jnp.float32)
    d_attn_in = tp_sum(d_attn_in_part).reshape(map_count, piece_rows, model_width)
    d_input, d_scale_one, d_shift_one = first_back(d_attn_in)
    d_input = d_input + d_mid
    d_mod_part = jnp.stack(
        [d_gamma_one, d_gamma_two, d_scale_one, d_scale_two, d_shift_one, d_shift_two], axis=1
    )
    d_mod = lax.psum(d_mod_part, "ctx").astype(jnp.bfloat16).reshape(map_count, 6 * model_width)
    d_mod_all = lax.all_gather(d_mod, "shard", axis=0, tiled=True)
    qkv_shard, d_mod_all = lax.optimization_barrier((qkv_shard, d_mod_all))
    g_ada = jnp.einsum(
        "md,mc->dc", cond_cols, d_mod_all, preferred_element_type=jnp.float32
    ).reshape(ada_rows, 6, model_width)
    d_ada_bias = jnp.sum(d_mod_all.astype(jnp.float32), axis=0).reshape(6, model_width)
    d_cond_cols = jnp.einsum("mc,dc->md", d_mod_all, ada_local, preferred_element_type=jnp.float32)
    d_cond_in = lax.all_to_all(d_cond_cols, "shard", 0, 1, tiled=True)
    silu_value, silu_back = jax.vjp(jax.nn.silu, cond_wide)
    (d_cond,) = silu_back(d_cond_in)
    qkv_summed = lax.psum(qkv_shard, "ctx")
    summed = tuple(
        g.astype(jnp.float32) for g in (qkv_summed, early_summed[0], early_summed[1], early_summed[2])
    )
    square_sums = jnp.stack(
        [jnp.sum(stream * stream), jnp.sum(attn_part * attn_part), jnp.sum(mlp_part * mlp_part)]
    )
    small_parts = (
        square_sums,
        d_query_bias,
        d_value_bias,
        d_head_scale,
        d_proj_bias,
        d_up_bias,
        d_down_bias,
    )
    small_flat = small_sum(jnp.concatenate(small_parts))
    small = []
    offset = 0
    for part in small_parts:
        small.append(small_flat[offset:offset + part.shape[0]])
        offset += part.shape[0]
    entry_total = map_count * map_length * model_width * lax.axis_size("shard")
    norm_stats = jnp.sqrt(small[0] / entry_total)
    return (
        stream.astype(jnp.bfloat16),
        d_input.astype(jnp.bfloat16),
        d_cond,
        g_ada,
        d_ada_bias,
        summed[0],
        small[1],
        small[2],
        small[3],
        summed[2],
        small[4],
        summed[1],
        small[5],
        summed[3],
        small[6],
        norm_stats,
    )


def solution(mesh):
    in_specs = (
        P("shard", "ctx", None),
        P("shard", None),
        P("shard", None),
        P("shard", None, None),
        P(),
        P("shard", None, "tp"),
        P("tp"),
        P("tp"),
        P("tp"),
        P("tp", "shard"),
        P(),
        P("shard", "tp"),
        P("tp"),
        P("tp", "shard"),
        P(),
        P("shard", "ctx", None),
    )
    out_specs = (
        P("shard", "ctx", None),
        P("shard", "ctx", None),
        P("shard", None),
        P("shard", None, None),
        P(),
        P("shard", None, "tp"),
        P("tp"),
        P("tp"),
        P("tp"),
        P("tp", "shard"),
        P(),
        P("shard", "tp"),
        P("tp"),
        P("tp", "shard"),
        P(),
        P(),
    )
    return jax.shard_map(body, mesh=mesh, in_specs=in_specs, out_specs=out_specs, check_vma=False)
```
